32 devices in a mesh: groups: 2 (over y), inner: 16 (over z, x, core).
Axes of the slice: x: 2, y: 2, z: 4, core: 2. Of those that a mesh axis runs over, the one named last changes fastest.
Arguments:
- ticks: bfloat16 [262144, 128], P(('groups', 'inner')), parts along dimension 0, may hold values from -6 to 6
- conv_weight: bfloat16 [2048, 768], replicated, may hold values from -0.125 to 0.125
- norm_gain: float32 [768], replicated, may hold values from 0.25 to 1.75
- qkv_weight: bfloat16 [768, 2304], replicated, may hold values from -0.21875 to 0.21875
- head_gain: float32 [768], replicated, may hold values from 0.25 to 1.75
- out_weight: bfloat16 [768, 768], replicated, may hold values from -0.21875 to 0.21875
- state_in: float32 [24, 64, 64], P('groups'), parts along dimension 0, may hold values from -768 to 768
Outputs:
- layer_out: bfloat16 [32768, 768], P(('groups', 'inner')), parts along dimension 0
The draws below stay inside these ranges and needn't reach their ends.
There are 2 independent parts, one for each index of `groups`. The reference program is written for one: setup_inputs(seed, part) draws one part's arguments, and reference() takes and returns one part's arrays. A program takes and returns all parts, laid end to end along the dimension named above; an argument that names none is the same for every part. Nothing has to cross between parts.
All inputs are finite; a program needn't handle non-finite values.
Results may differ from the reference program's by a relative error of at most 0.008.
Values may be sent and summed in bfloat16 or wider, within the bound.
No kernel may reach another device: no remote copies, remote signals or barrier semaphores. Data moves between devices by JAX's collectives and lax.ppermute only.
A program may use at most 192 MiB of HBM per device.

```python
import jax
import jax.numpy as jnp
from jax import lax

D = 768
HEADS = 12
DH = 64
FEAT = 128
STRIDE = 8
KERNEL = 16
TOK_DEV = 1024
BLK = 512
TOKENS = 16384
TICKS = 131072
N_INNER = 16


def shard_levels(rng, extent, cuts, least, top_value):
    def one(axis_at, shards_of):
        steps = jax.random.uniform(jax.random.fold_in(jax.random.fold_in(rng, 6), axis_at), (shards_of,), jnp.float32, least / len(cuts), top_value / len(cuts))
        return jnp.repeat(jnp.exp(steps), extent[axis_at] // shards_of).reshape((-1,) + (1,) * (len(extent) - axis_at - 1))

    level = one(*cuts[0])
    for cut in cuts[1:]:
        level = level * one(*cut)
    return level


def centred(rng, shape, spread, reach, split=(), kind=jnp.bfloat16):
    loudness = shard_levels(rng, shape, split, -0.22, 0.18) if split else 1.0
    drawn = jax.random.normal(rng, shape, jnp.float32) * spread * loudness
    return jnp.minimum(jnp.maximum(drawn, -reach), reach).astype(kind)


def setup_inputs(seed: int = 0, part: int = 0) -> dict:
    streams_of = jax.random.split(jax.random.key(seed), 8)
    part_keys = jax.random.split(jax.random.fold_in(streams_of[7], part), 8)
    return {
        "ticks": centred(part_keys[0], (TICKS, FEAT), 1.0, 6.0, ((0, 16),)),
        "conv_weight": centred(streams_of[1], (KERNEL * FEAT, D), (KERNEL * FEAT) ** -0.5, 0.125),
        "norm_gain": jnp.clip(1.0 + 0.15 * jax.random.normal(streams_of[2], (D,), jnp.float32), 0.25, 1.75),
        "qkv_weight": centred(streams_of[3], (D, 3 * D), D ** -0.5, 0.21875),
        "head_gain": jnp.clip(1.0 + 0.15 * jax.random.normal(streams_of[4], (D,), jnp.float32), 0.25, 1.75),
        "out_weight": centred(streams_of[5], (D, D), D ** -0.5, 0.21875),
        "state_in": centred(part_keys[6], (HEADS, DH, DH), ((TOK_DEV * N_INNER) ** 0.5), 768.0, (), jnp.float32),
    }


def reference(ticks, conv_weight, norm_gain, qkv_weight, head_gain, out_weight, state_in):
    row_width = STRIDE * FEAT
    tick_rows = ticks.reshape(TOKENS, row_width)
    earlier_rows = jnp.concatenate([jnp.zeros((1, row_width), tick_rows.dtype), tick_rows[:-1]], 0)
    embedded = (jnp.dot(earlier_rows, conv_weight[:row_width], preferred_element_type=jnp.float32) + jnp.dot(tick_rows, conv_weight[row_width:], preferred_element_type=jnp.float32)).astype(jnp.bfloat16)
    embed_f = embedded.astype(jnp.float32)
    normed = (embed_f * lax.rsqrt(lax.optimization_barrier(jnp.mean(embed_f * embed_f, -1, keepdims=True)) + 1e-05) * norm_gain).astype(jnp.bfloat16)
    qkv = jnp.dot(normed, qkv_weight, preferred_element_type=jnp.float32).astype(jnp.bfloat16)
    block_count = TOKENS // BLK
    queries = qkv[:, :D].reshape(block_count, BLK, HEADS, DH)
    keys_all = qkv[:, D:2 * D].reshape(block_count, BLK, HEADS, DH)
    values_all = qkv[:, 2 * D:].reshape(block_count, BLK, HEADS, DH)
    lower = jnp.arange(BLK)[:, None] >= jnp.arange(BLK)[None, :]

    def one_block(carried, pieces):
        query_b, key_b, value_b = pieces
        query_f = query_b.astype(jnp.float32)
        key_f = key_b.astype(jnp.float32)
        value_f = value_b.astype(jnp.float32)
        scores = jnp.einsum('thd,shd->hts', query_f, key_f)
        scores = jnp.where(lower[None], scores, 0.0).astype(jnp.bfloat16).astype(jnp.float32)
        inside_term = jnp.einsum('hts,shd->thd', scores, value_f)
        carried_term = jnp.einsum('thi,hij->thj', query_f, carried, precision=lax.Precision.HIGHEST)
        updated = carried + jnp.einsum('thi,thj->hij', key_f, value_f)
        return (updated, inside_term + carried_term)
    final_state, combined = lax.scan(one_block, state_in.astype(jnp.float32), (queries, keys_all, values_all))
    combined = combined.reshape(TOKENS, HEADS, DH)
    attended = combined * lax.rsqrt(lax.optimization_barrier(jnp.mean(combined * combined, -1, keepdims=True)) + 1e-06) * head_gain.reshape(HEADS, DH)
    attended = attended.reshape(TOKENS, D).astype(jnp.bfloat16)
    return (embed_f + jnp.dot(attended, out_weight, preferred_element_type=jnp.float32)).astype(jnp.bfloat16)
```

```python
import jax
import jax.numpy as jnp
from jax import lax
from jax.sharding import PartitionSpec as P

STRIDE = 8
BLK = 512


def from_behind(value, axis, steps):
    count = lax.axis_size(axis)
    initial, last = (max(0, -steps), min(count, count - steps))
    return lax.ppermute(value, axis, [(source, source + steps) for source in range(initial, last)])


def exclusive_scan(value, axis):
    count = lax.axis_size(axis)
    total = value
    steps = 1
    while steps < count:
        total = total + from_behind(total, axis, steps)
        steps *= 2
    return total - value


def shards(ticks, conv_weight, norm_gain, qkv_weight, head_gain, out_weight, state_in):
    row_width = STRIDE * ticks.shape[1]
    token_count = ticks.shape[0] // STRIDE
    tick_rows = ticks.reshape(token_count, row_width)
    weight_prev = conv_weight[:row_width]
    current = jnp.dot(tick_rows, conv_weight[row_width:], preferred_element_type=jnp.float32)
    last_row = from_behind(tick_rows[token_count - 1 :], "inner", 1)
    earlier_rows = jnp.concatenate([last_row, tick_rows[:-1]], 0)
    embedded_f = current + jnp.dot(earlier_rows, weight_prev, preferred_element_type=jnp.float32)
    embedded = embedded_f.astype(jnp.bfloat16)
    embed_f = embedded.astype(jnp.float32)
    normed = (
        embed_f * lax.rsqrt(jnp.mean(embed_f * embed_f, -1, keepdims=True) + 1e-05) * norm_gain
    ).astype(jnp.bfloat16)
    qkv = jnp.dot(normed, qkv_weight, preferred_element_type=jnp.float32).astype(jnp.bfloat16)
    model_width = embedded.shape[1]
    head_count = state_in.shape[0]
    head_size = state_in.shape[1]
    block_count = token_count // BLK
    queries = qkv[:, :model_width].reshape(block_count, BLK, head_count, head_size)
    keys_all = qkv[:, model_width : 2 * model_width].reshape(
        block_count, BLK, head_count, head_size
    )
    values_all = qkv[:, 2 * model_width :].reshape(block_count, BLK, head_count, head_size)
    block_states = jnp.einsum(
        "bthi,bthj->bhij", keys_all, values_all, preferred_element_type=jnp.float32
    )
    local_state = jnp.sum(block_states, 0)
    prefix = exclusive_scan(local_state, "inner")
    carried = state_in + prefix
    within = jnp.cumsum(block_states, 0) - block_states
    state_before = carried[None] + within
    lower = jnp.arange(BLK)[:, None] >= jnp.arange(BLK)[None, :]
    scores = jnp.einsum("bthd,bshd->bhts", queries, keys_all, preferred_element_type=jnp.float32)
    scores = jnp.where(lower[None, None], scores, 0.0).astype(jnp.bfloat16)
    inside_term = jnp.einsum(
        "bhts,bshd->bthd", scores, values_all, preferred_element_type=jnp.float32
    )
    carried_term = jnp.einsum(
        "bthi,bhij->bthj",
        queries.astype(jnp.float32),
        state_before,
        precision=lax.Precision.HIGHEST,
    )
    combined = (inside_term + carried_term).reshape(token_count, head_count, head_size)
    attended = (
        combined
        * lax.rsqrt(jnp.mean(combined * combined, -1, keepdims=True) + 1e-06)
        * head_gain.reshape(head_count, head_size)
    )
    attended = attended.reshape(token_count, model_width).astype(jnp.bfloat16)
    return (embed_f + jnp.dot(attended, out_weight, preferred_element_type=jnp.float32)).astype(
        jnp.bfloat16
    )


def solution(mesh):
    in_specs = (P(("groups", "inner"), None), P(), P(), P(), P(), P(), P("groups", None, None))
    out_specs = P(("groups", "inner"), None)
    return jax.shard_map(shards, mesh=mesh, in_specs=in_specs, out_specs=out_specs, check_vma=False)
```

```python
import functools

import jax
import jax.numpy as jnp
from jax import lax
from jax.experimental import pallas as pl
from jax.experimental.pallas import tpu as pltpu
from jax.sharding import PartitionSpec as P

STRIDE = 8
BLK = 512
PAIR = 128


def from_behind(value, axis, steps):
    count = lax.axis_size(axis)
    initial, last = (max(0, -steps), min(count, count - steps))
    return lax.ppermute(value, axis, [(source, source + steps) for source in range(initial, last)])


def exclusive_scan(value, axis):
    count = lax.axis_size(axis)
    total = value
    steps = 1
    while steps < count:
        total = total + from_behind(total, axis, steps)
        steps *= 2
    return total - value


def embed_kernel(ticks_ref, prev_ref, conv_ref, gain_ref, qkv_w_ref,
                 emb_ref, q_ref, inside_ref, state_ref, wide_ref):
    b = pl.program_id(0)
    block_ticks = ticks_ref.shape[0]
    tokens = block_ticks // STRIDE
    model_width = emb_ref.shape[1]

    @pl.when(b == 0)
    def _():
        wide_ref[0:STRIDE, :] = prev_ref[STRIDE : 2 * STRIDE, :].astype(jnp.float32)

    @pl.when(b > 0)
    def _():
        wide_ref[0:STRIDE, :] = wide_ref[block_ticks : block_ticks + STRIDE, :]

    wide_ref[STRIDE:, :] = ticks_ref[...].astype(jnp.float32)
    pieces = [wide_ref[pl.ds(j, tokens, stride=STRIDE), :] for j in range(2 * STRIDE)]
    lhs = jnp.concatenate(pieces, axis=1).astype(jnp.bfloat16)
    emb = jnp.dot(lhs, conv_ref[...], preferred_element_type=jnp.float32).astype(jnp.bfloat16)
    emb_ref[...] = emb
    embed_f = emb.astype(jnp.float32)
    mean_sq = jnp.mean(embed_f * embed_f, axis=-1, keepdims=True)
    normed = (embed_f * lax.rsqrt(mean_sq + 1e-05) * gain_ref[...]).astype(jnp.bfloat16)

    def project(part):
        weight = qkv_w_ref[:, part * model_width : (part + 1) * model_width]
        return jnp.dot(normed, weight, preferred_element_type=jnp.float32).astype(jnp.bfloat16)

    queries, keys, values = project(0), project(1), project(2)
    q_ref[...] = queries
    lane = lax.broadcasted_iota(jnp.int32, (1, PAIR), 1)
    first = lane < PAIR // 2
    causal = (lax.broadcasted_iota(jnp.int32, (tokens, tokens), 0)
              >= lax.broadcasted_iota(jnp.int32, (tokens, tokens), 1))
    zero = jnp.zeros((), jnp.bfloat16)
    for pair in range(model_width // PAIR):
        cols = slice(pair * PAIR, (pair + 1) * PAIR)
        q_pair, k_pair, v_pair = queries[:, cols], keys[:, cols], values[:, cols]
        inside = None
        for use in (first, ~first):
            q_one = jnp.where(use, q_pair, zero)
            scores = lax.dot_general(q_one, k_pair, (((1,), (1,)), ((), ())),
                                     preferred_element_type=jnp.float32)
            scores = jnp.where(causal, scores, 0.0).astype(jnp.bfloat16)
            term = jnp.dot(scores, jnp.where(use, v_pair, zero), preferred_element_type=jnp.float32)
            inside = term if inside is None else inside + term
        inside_ref[:, cols] = inside
        kv = lax.dot_general(k_pair, v_pair, (((0,), (0,)), ((), ())),
                             preferred_element_type=jnp.float32)
        half = PAIR // 2
        state_ref[0, pair] = jnp.where(first, kv[:half], kv[half:])


def out_kernel(q_ref, state_ref, inside_ref, emb_ref, hgain_ref, out_w_ref, out_ref, att_ref):
    model_width = out_ref.shape[1]
    lane = lax.broadcasted_iota(jnp.int32, (1, PAIR), 1)
    first = lane < PAIR // 2
    head_size = PAIR // 2
    for pair in range(model_width // PAIR):
        cols = slice(pair * PAIR, (pair + 1) * PAIR)
        packed = state_ref[0, pair]
        diag = jnp.concatenate([jnp.where(first, packed, 0.0), jnp.where(first, 0.0, packed)], axis=0)
        high = diag.astype(jnp.bfloat16)
        low = (diag - high.astype(jnp.float32)).astype(jnp.bfloat16)
        q_pair = q_ref[:, cols]
        carried = (jnp.dot(q_pair, high, preferred_element_type=jnp.float32)
                   + jnp.dot(q_pair, low, preferred_element_type=jnp.float32))
        combined = inside_ref[:, cols] + carried
        square = combined * combined
        sum_first = jnp.sum(jnp.where(first, square, 0.0), axis=-1, keepdims=True)
        sum_second = jnp.sum(jnp.where(first, 0.0, square), axis=-1, keepdims=True)
        scale = jnp.where(first, lax.rsqrt(sum_first / head_size + 1e-06),
                          lax.rsqrt(sum_second / head_size + 1e-06))
        att_ref[:, cols] = (combined * scale * hgain_ref[:, cols]).astype(jnp.bfloat16)
    out = emb_ref[...].astype(jnp.float32) + jnp.dot(att_ref[...], out_w_ref[...],
                                                     preferred_element_type=jnp.float32)
    out_ref[...] = out.astype(jnp.bfloat16)


def full(shape):
    return pl.BlockSpec(shape, lambda b: (0,) * len(shape))


def shards(ticks, conv_weight, norm_gain, qkv_weight, head_gain, out_weight, state_in):
    tick_count, feat = ticks.shape
    token_count = tick_count // STRIDE
    model_width = conv_weight.shape[1]
    head_count, head_size = state_in.shape[0], state_in.shape[1]
    pairs = model_width // PAIR
    blocks = token_count // BLK
    block_ticks = BLK * STRIDE

    prev = from_behind(ticks[tick_count - 2 * STRIDE :], "inner", 1)
    rows_spec = pl.BlockSpec((BLK, model_width), lambda b: (b, 0))
    state_spec = pl.BlockSpec((1, pairs, head_size, PAIR), lambda b: (b, 0, 0, 0))
    emb, queries, inside, states = pl.pallas_call(
        embed_kernel,
        grid=(blocks,),
        in_specs=[
            pl.BlockSpec((block_ticks, feat), lambda b: (b, 0)),
            full((2 * STRIDE, feat)),
            full(conv_weight.shape),
            full((1, model_width)),
            full(qkv_weight.shape),
        ],
        out_specs=[rows_spec, rows_spec, rows_spec, state_spec],
        out_shape=[
            jax.ShapeDtypeStruct((token_count, model_width), jnp.bfloat16),
            jax.ShapeDtypeStruct((token_count, model_width), jnp.bfloat16),
            jax.ShapeDtypeStruct((token_count, model_width), jnp.float32),
            jax.ShapeDtypeStruct((blocks, pairs, head_size, PAIR), jnp.float32),
        ],
        scratch_shapes=[pltpu.VMEM((block_ticks + STRIDE, feat), jnp.float32)],
        compiler_params=pltpu.CompilerParams(dimension_semantics=("arbitrary",)),
    )(ticks, prev, conv_weight, norm_gain.reshape(1, model_width), qkv_weight)

    local = states[0]
    for block in range(1, blocks):
        local = local + states[block]
    prefix = exclusive_scan(local, "inner")
    packed_in = state_in.reshape(pairs, 2, head_size, head_size).transpose(0, 2, 1, 3)
    carried = packed_in.reshape(pairs, head_size, PAIR) + prefix
    before = [carried]
    for block in range(1, blocks):
        before.append(before[-1] + states[block - 1])
    before = jnp.stack(before)

    return pl.pallas_call(
        out_kernel,
        grid=(blocks,),
        in_specs=[
            rows_spec,
            state_spec,
            rows_spec,
            rows_spec,
            full((1, model_width)),
            full(out_weight.shape),
        ],
        out_specs=rows_spec,
        out_shape=jax.ShapeDtypeStruct((token_count, model_width), jnp.bfloat16),
        scratch_shapes=[pltpu.VMEM((BLK, model_width), jnp.bfloat16)],
        compiler_params=pltpu.CompilerParams(dimension_semantics=("arbitrary",)),
    )(queries, before, inside, emb, head_gain.reshape(1, model_width), out_weight)


def solution(mesh):
    in_specs = (P(("groups", "inner"), None), P(), P(), P(), P(), P(), P("groups", None, None))
    out_specs = P(("groups", "inner"), None)
    return jax.shard_map(shards, mesh=mesh, in_specs=in_specs, out_specs=out_specs, check_vma=False)
```

```python
import jax
import jax.numpy as jnp
from jax import lax
from jax.experimental import pallas as pl
from jax.experimental.pallas import tpu as pltpu
from jax.sharding import PartitionSpec as P

STRIDE = 8
BLK = 512
PAIR = 128


def from_behind(value, axis, steps):
    count = lax.axis_size(axis)
    initial, last = (max(0, -steps), min(count, count - steps))
    return lax.ppermute(value, axis, [(source, source + steps) for source in range(initial, last)])


def exclusive_scan(value, axis):
    count = lax.axis_size(axis)
    total = value
    steps = 1
    while steps < count:
        total = total + from_behind(total, axis, steps)
        steps *= 2
    return total - value


def conv_kernel(ticks_ref, prev_ref, conv_ref, gain_ref, emb_ref, normed_ref, wide_ref):
    b = pl.program_id(0)
    block_ticks = ticks_ref.shape[0]
    tokens = block_ticks // STRIDE

    @pl.when(b == 0)
    def _():
        wide_ref[0:STRIDE, :] = prev_ref[STRIDE : 2 * STRIDE, :].astype(jnp.float32)

    @pl.when(b > 0)
    def _():
        wide_ref[0:STRIDE, :] = wide_ref[block_ticks : block_ticks + STRIDE, :]

    wide_ref[STRIDE:, :] = ticks_ref[...].astype(jnp.float32)
    pieces = [wide_ref[pl.ds(j, tokens, stride=STRIDE), :] for j in range(2 * STRIDE)]
    lhs = jnp.concatenate(pieces, axis=1).astype(jnp.bfloat16)
    emb = jnp.dot(lhs, conv_ref[...], preferred_element_type=jnp.float32).astype(jnp.bfloat16)
    emb_ref[...] = emb
    embed_f = emb.astype(jnp.float32)
    mean_sq = jnp.mean(embed_f * embed_f, axis=-1, keepdims=True)
    normed_ref[...] = (embed_f * lax.rsqrt(mean_sq + 1e-05) * gain_ref[...]).astype(jnp.bfloat16)


def attend_kernel(normed_ref, wq_ref, wk_ref, wv_ref, q_ref, inside_ref, state_ref):
    normed = normed_ref[...]
    tokens = normed.shape[0]

    def project(weight_ref):
        return jnp.dot(normed, weight_ref[...], preferred_element_type=jnp.float32).astype(jnp.bfloat16)

    queries, keys, values = project(wq_ref), project(wk_ref), project(wv_ref)
    q_ref[...] = queries
    lane = lax.broadcasted_iota(jnp.int32, (1, PAIR), 1)
    first = lane < PAIR // 2
    causal = (lax.broadcasted_iota(jnp.int32, (tokens, tokens), 0)
              >= lax.broadcasted_iota(jnp.int32, (tokens, tokens), 1))
    zero = jnp.zeros((), jnp.bfloat16)
    for pair in range(queries.shape[1] // PAIR):
        cols = slice(pair * PAIR, (pair + 1) * PAIR)
        q_pair, k_pair, v_pair = queries[:, cols], keys[:, cols], values[:, cols]
        kv = lax.dot_general(k_pair, v_pair, (((0,), (0,)), ((), ())),
                             preferred_element_type=jnp.float32)
        half = PAIR // 2
        state_ref[0, pair] = jnp.where(first, kv[:half], kv[half:])
        inside = None
        for use in (first, ~first):
            q_one = jnp.where(use, q_pair, zero)
            scores = lax.dot_general(q_one, k_pair, (((1,), (1,)), ((), ())),
                                     preferred_element_type=jnp.float32)
            scores = jnp.where(causal, scores, 0.0).astype(jnp.bfloat16)
            term = jnp.dot(scores, jnp.where(use, v_pair, zero), preferred_element_type=jnp.float32)
            inside = term if inside is None else inside + term
        inside_ref[:, cols] = inside


def head_norm_kernel(q_ref, state_ref, inside_ref, hgain_ref, att_ref):
    lane = lax.broadcasted_iota(jnp.int32, (1, PAIR), 1)
    first = lane < PAIR // 2
    head_size = PAIR // 2
    for pair in range(att_ref.shape[1] // PAIR):
        cols = slice(pair * PAIR, (pair + 1) * PAIR)
        packed = state_ref[0, pair]
        diag = jnp.concatenate([jnp.where(first, packed, 0.0), jnp.where(first, 0.0, packed)], axis=0)
        high = diag.astype(jnp.bfloat16)
        low = (diag - high.astype(jnp.float32)).astype(jnp.bfloat16)
        q_pair = q_ref[:, cols]
        carried = (jnp.dot(q_pair, high, preferred_element_type=jnp.float32)
                   + jnp.dot(q_pair, low, preferred_element_type=jnp.float32))
        combined = inside_ref[:, cols] + carried
        square = combined * combined
        sum_first = jnp.sum(jnp.where(first, square, 0.0), axis=-1, keepdims=True)
        sum_second = jnp.sum(jnp.where(first, 0.0, square), axis=-1, keepdims=True)
        scale = jnp.where(first, lax.rsqrt(sum_first / head_size + 1e-06),
                          lax.rsqrt(sum_second / head_size + 1e-06))
        att_ref[:, cols] = (combined * scale * hgain_ref[...][:, cols]).astype(jnp.bfloat16)


def project_kernel(*refs):
    emb_ref, w_ref = refs[0], refs[1]
    att_refs, out_ref = refs[2:-1], refs[-1]
    width = att_refs[0].shape[1]
    total = emb_ref[...].astype(jnp.float32)
    for chunk, att_ref in enumerate(att_refs):
        total = total + jnp.dot(att_ref[...], w_ref[chunk * width : (chunk + 1) * width, :],
                                preferred_element_type=jnp.float32)
    out_ref[...] = total.astype(jnp.bfloat16)


def full(shape):
    return pl.BlockSpec(shape, lambda b: (0,) * len(shape))


def rows(width):
    return pl.BlockSpec((BLK, width), lambda b: (b, 0))


def cost(flops, nbytes):
    return pl.CostEstimate(flops=int(flops), transcendentals=0, bytes_accessed=int(nbytes))


CHUNKS = 3


def shards(ticks, conv_weight, norm_gain, qkv_weight, head_gain, out_weight, state_in):
    tick_count, feat = ticks.shape
    token_count = tick_count // STRIDE
    model_width = conv_weight.shape[1]
    head_size = state_in.shape[1]
    pairs = model_width // PAIR
    blocks = token_count // BLK
    block_ticks = BLK * STRIDE
    width = model_width // CHUNKS
    chunk_pairs = width // PAIR
    params = pltpu.CompilerParams(dimension_semantics=("arbitrary",))
    bf16, f32 = jnp.bfloat16, jnp.float32

    prev = from_behind(ticks[tick_count - 2 * STRIDE :], "inner", 1)
    emb, normed = pl.pallas_call(
        conv_kernel,
        grid=(blocks,),
        in_specs=[
            pl.BlockSpec((block_ticks, feat), lambda b: (b, 0)),
            full((2 * STRIDE, feat)),
            full(conv_weight.shape),
            full((1, model_width)),
        ],
        out_specs=[rows(model_width), rows(model_width)],
        out_shape=[jax.ShapeDtypeStruct((token_count, model_width), bf16)] * 2,
        scratch_shapes=[pltpu.VMEM((block_ticks + STRIDE, feat), f32)],
        compiler_params=params,
        cost_estimate=cost(2 * token_count * conv_weight.size, 2 * (ticks.size + conv_weight.size) + 4 * emb_bytes(token_count, model_width)),
    )(ticks, prev, conv_weight, norm_gain.reshape(1, model_width))

    packed_in = state_in.reshape(pairs, 2, head_size, head_size).transpose(0, 2, 1, 3)
    packed_in = packed_in.reshape(pairs, head_size, PAIR)
    state_spec = pl.BlockSpec((1, chunk_pairs, head_size, PAIR), lambda b: (b, 0, 0, 0))
    atts = []
    for chunk in range(CHUNKS):
        def weight_spec(part, chunk=chunk):
            return pl.BlockSpec((model_width, width), lambda b: (0, part * CHUNKS + chunk))

        queries, inside, states = pl.pallas_call(
            attend_kernel,
            grid=(blocks,),
            in_specs=[rows(model_width), weight_spec(0), weight_spec(1), weight_spec(2)],
            out_specs=[rows(width), rows(width), state_spec],
            out_shape=[
                jax.ShapeDtypeStruct((token_count, width), bf16),
                jax.ShapeDtypeStruct((token_count, width), f32),
                jax.ShapeDtypeStruct((blocks, chunk_pairs, head_size, PAIR), f32),
            ],
            compiler_params=params,
            cost_estimate=cost(2 * token_count * model_width * 3 * width + 4 * token_count * BLK * width * 2,
                               2 * token_count * model_width + 6 * model_width * width + 6 * token_count * width),
        )(normed, qkv_weight, qkv_weight, qkv_weight)
        local = states[0]
        for block in range(1, blocks):
            local = local + states[block]
        prefix = exclusive_scan(local, "inner")
        carried = packed_in[chunk * chunk_pairs : (chunk + 1) * chunk_pairs] + prefix
        before = [carried]
        for block in range(1, blocks):
            before.append(before[-1] + states[block - 1])
        before = jnp.stack(before)
        atts.append(pl.pallas_call(
            head_norm_kernel,
            grid=(blocks,),
            in_specs=[rows(width), state_spec, rows(width), pl.BlockSpec((1, width), lambda b, chunk=chunk: (0, chunk))],
            out_specs=rows(width),
            out_shape=jax.ShapeDtypeStruct((token_count, width), bf16),
            compiler_params=params,
            cost_estimate=cost(4 * token_count * width * PAIR, 8 * token_count * width),
        )(queries, before, inside, head_gain.reshape(1, model_width)))

    return pl.pallas_call(
        project_kernel,
        grid=(blocks,),
        in_specs=[rows(model_width), full(out_weight.shape)] + [rows(width)] * CHUNKS,
        out_specs=rows(model_width),
        out_shape=jax.ShapeDtypeStruct((token_count, model_width), bf16),
        compiler_params=params,
        cost_estimate=cost(2 * token_count * out_weight.size, 2 * out_weight.size + 6 * token_count * model_width),
    )(emb, out_weight, *atts)


def emb_bytes(tokens, width):
    return tokens * width


def solution(mesh):
    in_specs = (P(("groups", "inner"), None), P(), P(), P(), P(), P(), P("groups", None, None))
    out_specs = P(("groups", "inner"), None)
    return jax.shard_map(shards, mesh=mesh, in_specs=in_specs, out_specs=out_specs, check_vma=False)
```

```python
import functools

import jax
import jax.numpy as jnp
from jax import lax
from jax.experimental import pallas as pl
from jax.experimental.pallas import tpu as pltpu
from jax.sharding import PartitionSpec as P

STRIDE = 8
BLK = 512
PAIR = 128
SUB = 128


def from_behind(value, axis, steps):
    count = lax.axis_size(axis)
    initial, last = (max(0, -steps), min(count, count - steps))
    return lax.ppermute(value, axis, [(source, source + steps) for source in range(initial, last)])


def exclusive_scan(value, axis):
    count = lax.axis_size(axis)
    total = value
    steps = 1
    while steps < count:
        total = total + from_behind(total, axis, steps)
        steps *= 2
    return total - value


def embed_kernel(ticks_ref, prev_ref, conv_ref, gain_ref, qkv_w_ref,
                 emb_ref, q_ref, inside_ref, state_ref, wide_ref, run_ref):
    b = pl.program_id(0)
    block_ticks = ticks_ref.shape[0]
    tokens = block_ticks // STRIDE
    model_width = emb_ref.shape[1]

    @pl.when(b == 0)
    def _():
        wide_ref[0:STRIDE, :] = prev_ref[STRIDE : 2 * STRIDE, :].astype(jnp.float32)

    @pl.when(b > 0)
    def _():
        wide_ref[0:STRIDE, :] = wide_ref[block_ticks : block_ticks + STRIDE, :]

    wide_ref[STRIDE:, :] = ticks_ref[...].astype(jnp.float32)
    pieces = [wide_ref[pl.ds(j, tokens, stride=STRIDE), :] for j in range(2 * STRIDE)]
    lhs = jnp.concatenate(pieces, axis=1).astype(jnp.bfloat16)
    emb = jnp.dot(lhs, conv_ref[...], preferred_element_type=jnp.float32).astype(jnp.bfloat16)
    emb_ref[...] = emb
    embed_f = emb.astype(jnp.float32)
    mean_sq = jnp.mean(embed_f * embed_f, axis=-1, keepdims=True)
    normed = (embed_f * lax.rsqrt(mean_sq + 1e-05) * gain_ref[...]).astype(jnp.bfloat16)

    def project(part):
        weight = qkv_w_ref[:, part * model_width : (part + 1) * model_width]
        return jnp.dot(normed, weight, preferred_element_type=jnp.float32).astype(jnp.bfloat16)

    queries, keys, values = project(0), project(1), project(2)
    q_ref[...] = queries

    @pl.when(b == 0)
    def _():
        run_ref[...] = jnp.zeros_like(run_ref)

    lane = lax.broadcasted_iota(jnp.int32, (1, PAIR), 1)
    first = lane < PAIR // 2
    half = PAIR // 2
    causal = (lax.broadcasted_iota(jnp.int32, (2 * SUB, SUB), 0) % SUB
              >= lax.broadcasted_iota(jnp.int32, (2 * SUB, SUB), 1))
    same_head = ((lax.broadcasted_iota(jnp.int32, (PAIR, PAIR), 0) < half)
                 == (lax.broadcasted_iota(jnp.int32, (PAIR, PAIR), 1) < half))
    zero = jnp.zeros((), jnp.bfloat16)
    for pair in range(model_width // PAIR):
        cols = slice(pair * PAIR, (pair + 1) * PAIR)
        running = run_ref[pair]
        for sub in range(tokens // SUB):
            span = slice(sub * SUB, (sub + 1) * SUB)
            q_sub, k_sub, v_sub = queries[span, cols], keys[span, cols], values[span, cols]
            stacked_q = jnp.concatenate([jnp.where(first, q_sub, zero), jnp.where(first, zero, q_sub)], axis=0)
            scores = lax.dot_general(stacked_q, k_sub, (((1,), (1,)), ((), ())),
                                     preferred_element_type=jnp.float32)
            scores = jnp.where(causal, scores, 0.0).astype(jnp.bfloat16)
            side = jnp.concatenate([scores[:SUB], scores[SUB:]], axis=1)
            stacked_v = jnp.concatenate([jnp.where(first, v_sub, zero), jnp.where(first, zero, v_sub)], axis=0)
            intra = jnp.dot(side, stacked_v, preferred_element_type=jnp.float32)
            high = running.astype(jnp.bfloat16)
            low = (running - high.astype(jnp.float32)).astype(jnp.bfloat16)
            inter = (jnp.dot(q_sub, high, preferred_element_type=jnp.float32)
                     + jnp.dot(q_sub, low, preferred_element_type=jnp.float32))
            inside_ref[span, cols] = intra + inter
            kv = lax.dot_general(k_sub, v_sub, (((0,), (0,)), ((), ())),
                                 preferred_element_type=jnp.float32)
            running = running + jnp.where(same_head, kv, 0.0)
        run_ref[pair] = running

    @pl.when(b == pl.num_programs(0) - 1)
    def _():
        for pair in range(model_width // PAIR):
            total = run_ref[pair]
            state_ref[pair] = jnp.where(first, total[:half], total[half:])


def out_kernel(q_ref, state_ref, inside_ref, emb_ref, hgain_ref, out_w_ref, out_ref, att_ref):
    model_width = out_ref.shape[1]
    lane = lax.broadcasted_iota(jnp.int32, (1, PAIR), 1)
    first = lane < PAIR // 2
    head_size = PAIR // 2
    for pair in range(model_width // PAIR):
        cols = slice(pair * PAIR, (pair + 1) * PAIR)
        packed = state_ref[pair]
        diag = jnp.concatenate([jnp.where(first, packed, 0.0), jnp.where(first, 0.0, packed)], axis=0)
        high = diag.astype(jnp.bfloat16)
        low = (diag - high.astype(jnp.float32)).astype(jnp.bfloat16)
        q_pair = q_ref[:, cols]
        carried = (jnp.dot(q_pair, high, preferred_element_type=jnp.float32)
                   + jnp.dot(q_pair, low, preferred_element_type=jnp.float32))
        combined = inside_ref[:, cols] + carried
        square = combined * combined
        sum_first = jnp.sum(jnp.where(first, square, 0.0), axis=-1, keepdims=True)
        sum_second = jnp.sum(jnp.where(first, 0.0, square), axis=-1, keepdims=True)
        scale = jnp.where(first, lax.rsqrt(sum_first / head_size + 1e-06),
                          lax.rsqrt(sum_second / head_size + 1e-06))
        att_ref[:, cols] = (combined * scale * hgain_ref[:, cols]).astype(jnp.bfloat16)
    out = emb_ref[...].astype(jnp.float32) + jnp.dot(att_ref[...], out_w_ref[...],
                                                     preferred_element_type=jnp.float32)
    out_ref[...] = out.astype(jnp.bfloat16)


def full(shape):
    return pl.BlockSpec(shape, lambda b: (0,) * len(shape))


def shards(ticks, conv_weight, norm_gain, qkv_weight, head_gain, out_weight, state_in):
    tick_count, feat = ticks.shape
    token_count = tick_count // STRIDE
    model_width = conv_weight.shape[1]
    head_count, head_size = state_in.shape[0], state_in.shape[1]
    pairs = model_width // PAIR
    blocks = token_count // BLK
    block_ticks = BLK * STRIDE

    prev = from_behind(ticks[tick_count - 2 * STRIDE :], "inner", 1)
    rows_spec = pl.BlockSpec((BLK, model_width), lambda b: (b, 0))
    state_spec = full((pairs, head_size, PAIR))
    emb, queries, inside, states = pl.pallas_call(
        embed_kernel,
        grid=(blocks,),
        in_specs=[
            pl.BlockSpec((block_ticks, feat), lambda b: (b, 0)),
            full((2 * STRIDE, feat)),
            full(conv_weight.shape),
            full((1, model_width)),
            full(qkv_weight.shape),
        ],
        out_specs=[rows_spec, rows_spec, rows_spec, state_spec],
        out_shape=[
            jax.ShapeDtypeStruct((token_count, model_width), jnp.bfloat16),
            jax.ShapeDtypeStruct((token_count, model_width), jnp.bfloat16),
            jax.ShapeDtypeStruct((token_count, model_width), jnp.float32),
            jax.ShapeDtypeStruct((pairs, head_size, PAIR), jnp.float32),
        ],
        scratch_shapes=[pltpu.VMEM((block_ticks + STRIDE, feat), jnp.float32),
                        pltpu.VMEM((pairs, PAIR, PAIR), jnp.float32)],
        compiler_params=pltpu.CompilerParams(dimension_semantics=("arbitrary",)),
    )(ticks, prev, conv_weight, norm_gain.reshape(1, model_width), qkv_weight)

    prefix = exclusive_scan(states, "inner")
    packed_in = state_in.reshape(pairs, 2, head_size, head_size).transpose(0, 2, 1, 3)
    carried = packed_in.reshape(pairs, head_size, PAIR) + prefix

    return pl.pallas_call(
        out_kernel,
        grid=(blocks,),
        in_specs=[
            rows_spec,
            state_spec,
            rows_spec,
            rows_spec,
            full((1, model_width)),
            full(out_weight.shape),
        ],
        out_specs=rows_spec,
        out_shape=jax.ShapeDtypeStruct((token_count, model_width), jnp.bfloat16),
        scratch_shapes=[pltpu.VMEM((BLK, model_width), jnp.bfloat16)],
        compiler_params=pltpu.CompilerParams(dimension_semantics=("arbitrary",)),
    )(queries, carried, inside, emb, head_gain.reshape(1, model_width), out_weight)


def solution(mesh):
    in_specs = (P(("groups", "inner"), None), P(), P(), P(), P(), P(), P("groups", None, None))
    out_specs = P(("groups", "inner"), None)
    return jax.shard_map(shards, mesh=mesh, in_specs=in_specs, out_specs=out_specs, check_vma=False)
```

```python
import functools

import jax
import jax.numpy as jnp
from jax import lax
from jax.experimental import pallas as pl
from jax.experimental.pallas import tpu as pltpu
from jax.sharding import PartitionSpec as P

STRIDE = 8
BLK = 512
PAIR = 128


def from_behind(value, axis, steps):
    count = lax.axis_size(axis)
    initial, last = (max(0, -steps), min(count, count - steps))
    return lax.ppermute(value, axis, [(source, source + steps) for source in range(initial, last)])


def exclusive_scan(value, axis):
    count = lax.axis_size(axis)
    total = value
    steps = 1
    while steps < count:
        total = total + from_behind(total, axis, steps)
        steps *= 2
    return total - value


def embed_kernel(ticks_ref, prev_ref, conv_ref, gain_ref, qkv_w_ref,
                 emb_ref, q_ref, inside_ref, total_ref, first_ref, wide_ref):
    b = pl.program_id(0)
    block_ticks = ticks_ref.shape[0]
    tokens = block_ticks // STRIDE
    model_width = emb_ref.shape[1]

    @pl.when(b == 0)
    def _():
        wide_ref[0:STRIDE, :] = prev_ref[STRIDE : 2 * STRIDE, :].astype(jnp.float32)

    @pl.when(b > 0)
    def _():
        wide_ref[0:STRIDE, :] = wide_ref[block_ticks : block_ticks + STRIDE, :]

    wide_ref[STRIDE:, :] = ticks_ref[...].astype(jnp.float32)
    pieces = [wide_ref[pl.ds(j, tokens, stride=STRIDE), :] for j in range(2 * STRIDE)]
    lhs = jnp.concatenate(pieces, axis=1).astype(jnp.bfloat16)
    emb = jnp.dot(lhs, conv_ref[...], preferred_element_type=jnp.float32).astype(jnp.bfloat16)
    emb_ref[...] = emb
    embed_f = emb.astype(jnp.float32)
    mean_sq = jnp.mean(embed_f * embed_f, axis=-1, keepdims=True)
    normed = (embed_f * lax.rsqrt(mean_sq + 1e-05) * gain_ref[...]).astype(jnp.bfloat16)

    def project(part):
        weight = qkv_w_ref[:, part * model_width : (part + 1) * model_width]
        return jnp.dot(normed, weight, preferred_element_type=jnp.float32).astype(jnp.bfloat16)

    queries, keys, values = project(0), project(1), project(2)
    q_ref[...] = queries
    lane = lax.broadcasted_iota(jnp.int32, (1, PAIR), 1)
    first = lane < PAIR // 2
    causal = (lax.broadcasted_iota(jnp.int32, (tokens, tokens), 0)
              >= lax.broadcasted_iota(jnp.int32, (tokens, tokens), 1))
    zero = jnp.zeros((), jnp.bfloat16)
    for pair in range(model_width // PAIR):
        cols = slice(pair * PAIR, (pair + 1) * PAIR)
        q_pair, k_pair, v_pair = queries[:, cols], keys[:, cols], values[:, cols]
        inside = None
        for use in (first, ~first):
            q_one = jnp.where(use, q_pair, zero)
            scores = lax.dot_general(q_one, k_pair, (((1,), (1,)), ((), ())),
                                     preferred_element_type=jnp.float32)
            scores = jnp.where(causal, scores, 0.0).astype(jnp.bfloat16)
            term = jnp.dot(scores, jnp.where(use, v_pair, zero), preferred_element_type=jnp.float32)
            inside = term if inside is None else inside + term
        inside_ref[:, cols] = inside
        kv = lax.dot_general(k_pair, v_pair, (((0,), (0,)), ((), ())),
                             preferred_element_type=jnp.float32)
        half = PAIR // 2
        packed = jnp.where(first, kv[:half], kv[half:])

        @pl.when(b == 0)
        def _():
            first_ref[pair] = packed
            total_ref[pair] = packed

        @pl.when(b > 0)
        def _():
            total_ref[pair] = total_ref[pair] + packed


def out_kernel(q_ref, carried_ref, first_ref, inside_ref, emb_ref, hgain_ref, out_w_ref, out_ref, att_ref):
    b = pl.program_id(0)
    model_width = out_ref.shape[1]
    lane = lax.broadcasted_iota(jnp.int32, (1, PAIR), 1)
    first = lane < PAIR // 2
    head_size = PAIR // 2
    same_head = ((lax.broadcasted_iota(jnp.int32, (PAIR, PAIR), 0) < head_size)
                 == (lax.broadcasted_iota(jnp.int32, (PAIR, PAIR), 1) < head_size)).astype(jnp.bfloat16)
    for pair in range(model_width // PAIR):
        cols = slice(pair * PAIR, (pair + 1) * PAIR)
        packed = carried_ref[pair] + jnp.where(b > 0, first_ref[pair], 0.0)
        diag = jnp.concatenate([jnp.where(first, packed, 0.0), jnp.where(first, 0.0, packed)], axis=0)
        high = diag.astype(jnp.bfloat16)
        low = (diag - high.astype(jnp.float32)).astype(jnp.bfloat16)
        q_pair = q_ref[:, cols]
        carried = (jnp.dot(q_pair, high, preferred_element_type=jnp.float32)
                   + jnp.dot(q_pair, low, preferred_element_type=jnp.float32))
        combined = inside_ref[:, cols] + carried
        square = combined * combined
        square_high = square.astype(jnp.bfloat16)
        square_low = (square - square_high.astype(jnp.float32)).astype(jnp.bfloat16)
        head_sum = (jnp.dot(square_high, same_head, preferred_element_type=jnp.float32)
                    + jnp.dot(square_low, same_head, preferred_element_type=jnp.float32))
        scale = lax.rsqrt(head_sum / head_size + 1e-06)
        att_ref[:, cols] = (combined * scale * hgain_ref[:, cols]).astype(jnp.bfloat16)
    out = emb_ref[...].astype(jnp.float32) + jnp.dot(att_ref[...], out_w_ref[...],
                                                     preferred_element_type=jnp.float32)
    out_ref[...] = out.astype(jnp.bfloat16)


def full(shape):
    return pl.BlockSpec(shape, lambda b: (0,) * len(shape))


def shards(ticks, conv_weight, norm_gain, qkv_weight, head_gain, out_weight, state_in):
    tick_count, feat = ticks.shape
    token_count = tick_count // STRIDE
    model_width = conv_weight.shape[1]
    head_count, head_size = state_in.shape[0], state_in.shape[1]
    pairs = model_width // PAIR
    blocks = token_count // BLK
    block_ticks = BLK * STRIDE

    prev = from_behind(ticks[tick_count - 2 * STRIDE :], "inner", 1)
    rows_spec = pl.BlockSpec((BLK, model_width), lambda b: (b, 0))
    state_spec = full((pairs, head_size, PAIR))
    emb, queries, inside, total, first_state = pl.pallas_call(
        embed_kernel,
        grid=(blocks,),
        in_specs=[
            pl.BlockSpec((block_ticks, feat), lambda b: (b, 0)),
            full((2 * STRIDE, feat)),
            full(conv_weight.shape),
            full((1, model_width)),
            full(qkv_weight.shape),
        ],
        out_specs=[rows_spec, rows_spec, rows_spec, state_spec, state_spec],
        out_shape=[
            jax.ShapeDtypeStruct((token_count, model_width), jnp.bfloat16),
            jax.ShapeDtypeStruct((token_count, model_width), jnp.bfloat16),
            jax.ShapeDtypeStruct((token_count, model_width), jnp.float32),
            jax.ShapeDtypeStruct((pairs, head_size, PAIR), jnp.float32),
            jax.ShapeDtypeStruct((pairs, head_size, PAIR), jnp.float32),
        ],
        scratch_shapes=[pltpu.VMEM((block_ticks + STRIDE, feat), jnp.float32)],
        compiler_params=pltpu.CompilerParams(dimension_semantics=("arbitrary",)),
    )(ticks, prev, conv_weight, norm_gain.reshape(1, model_width), qkv_weight)

    prefix = exclusive_scan(total, "inner")
    packed_in = state_in.reshape(pairs, 2, head_size, head_size).transpose(0, 2, 1, 3)
    carried = packed_in.reshape(pairs, head_size, PAIR) + prefix

    return pl.pallas_call(
        out_kernel,
        grid=(blocks,),
        in_specs=[
            rows_spec,
            state_spec,
            state_spec,
            rows_spec,
            rows_spec,
            full((1, model_width)),
            full(out_weight.shape),
        ],
        out_specs=rows_spec,
        out_shape=jax.ShapeDtypeStruct((token_count, model_width), jnp.bfloat16),
        scratch_shapes=[pltpu.VMEM((BLK, model_width), jnp.bfloat16)],
        compiler_params=pltpu.CompilerParams(dimension_semantics=("arbitrary",)),
    )(queries, carried, first_state, inside, emb, head_gain.reshape(1, model_width), out_weight)


def solution(mesh):
    in_specs = (P(("groups", "inner"), None), P(), P(), P(), P(), P(), P("groups", None, None))
    out_specs = P(("groups", "inner"), None)
    return jax.shard_map(shards, mesh=mesh, in_specs=in_specs, out_specs=out_specs, check_vma=False)
```

```python
import functools

import jax
import jax.numpy as jnp
from jax import lax
from jax.experimental import pallas as pl
from jax.experimental.pallas import tpu as pltpu
from jax.sharding import PartitionSpec as P

STRIDE = 8
BLK = 512
PAIR = 128


def from_behind(value, axis, steps):
    count = lax.axis_size(axis)
    initial, last = (max(0, -steps), min(count, count - steps))
    return lax.ppermute(value, axis, [(source, source + steps) for source in range(initial, last)])


def exclusive_scan(value, axis):
    count = lax.axis_size(axis)
    total = value
    steps = 1
    while steps < count:
        total = total + from_behind(total, axis, steps)
        steps *= 2
    return total - value


def embed_kernel(ticks_ref, prev_ref, conv_ref, gain_ref, qkv_w_ref,
                 emb_ref, q_ref, k_ref, v_ref, state_ref, wide_ref):
    b = pl.program_id(0)
    block_ticks = ticks_ref.shape[0]
    tokens = block_ticks // STRIDE
    model_width = emb_ref.shape[1]

    @pl.when(b == 0)
    def _():
        wide_ref[0:STRIDE, :] = prev_ref[STRIDE : 2 * STRIDE, :].astype(jnp.float32)

    @pl.when(b > 0)
    def _():
        wide_ref[0:STRIDE, :] = wide_ref[block_ticks : block_ticks + STRIDE, :]

    wide_ref[STRIDE:, :] = ticks_ref[...].astype(jnp.float32)
    pieces = [wide_ref[pl.ds(j, tokens, stride=STRIDE), :] for j in range(2 * STRIDE)]
    lhs = jnp.concatenate(pieces, axis=1).astype(jnp.bfloat16)
    emb = jnp.dot(lhs, conv_ref[...], preferred_element_type=jnp.float32).astype(jnp.bfloat16)
    emb_ref[...] = emb
    embed_f = emb.astype(jnp.float32)
    mean_sq = jnp.mean(embed_f * embed_f, axis=-1, keepdims=True)
    normed = (embed_f * lax.rsqrt(mean_sq + 1e-05) * gain_ref[...]).astype(jnp.bfloat16)

    def project(part):
        weight = qkv_w_ref[:, part * model_width : (part + 1) * model_width]
        return jnp.dot(normed, weight, preferred_element_type=jnp.float32).astype(jnp.bfloat16)

    queries, keys, values = project(0), project(1), project(2)
    q_ref[...] = queries
    k_ref[...] = keys
    v_ref[...] = values
    lane = lax.broadcasted_iota(jnp.int32, (1, PAIR), 1)
    first = lane < PAIR // 2
    for pair in range(model_width // PAIR):
        cols = slice(pair * PAIR, (pair + 1) * PAIR)
        kv = lax.dot_general(keys[:, cols], values[:, cols], (((0,), (0,)), ((), ())),
                             preferred_element_type=jnp.float32)
        half = PAIR // 2
        state_ref[0, pair] = jnp.where(first, kv[:half], kv[half:])


def inside_kernel(q_ref, k_ref, v_ref, earlier_ref, inside_ref):
    del earlier_ref
    queries, keys, values = q_ref[...], k_ref[...], v_ref[...]
    tokens = queries.shape[0]
    lane = lax.broadcasted_iota(jnp.int32, (1, PAIR), 1)
    first = lane < PAIR // 2
    causal = (lax.broadcasted_iota(jnp.int32, (tokens, tokens), 0)
              >= lax.broadcasted_iota(jnp.int32, (tokens, tokens), 1))
    zero = jnp.zeros((), jnp.bfloat16)
    for pair in range(queries.shape[1] // PAIR):
        cols = slice(pair * PAIR, (pair + 1) * PAIR)
        q_pair, k_pair, v_pair = queries[:, cols], keys[:, cols], values[:, cols]
        inside = None
        for use in (first, ~first):
            q_one = jnp.where(use, q_pair, zero)
            scores = lax.dot_general(q_one, k_pair, (((1,), (1,)), ((), ())),
                                     preferred_element_type=jnp.float32)
            scores = jnp.where(causal, scores, 0.0).astype(jnp.bfloat16)
            term = jnp.dot(scores, jnp.where(use, v_pair, zero), preferred_element_type=jnp.float32)
            inside = term if inside is None else inside + term
        inside_ref[:, cols] = inside


def out_kernel(q_ref, state_ref, inside_ref, emb_ref, hgain_ref, out_w_ref, out_ref, att_ref):
    model_width = out_ref.shape[1]
    lane = lax.broadcasted_iota(jnp.int32, (1, PAIR), 1)
    first = lane < PAIR // 2
    head_size = PAIR // 2
    for pair in range(model_width // PAIR):
        cols = slice(pair * PAIR, (pair + 1) * PAIR)
        packed = state_ref[0, pair]
        diag = jnp.concatenate([jnp.where(first, packed, 0.0), jnp.where(first, 0.0, packed)], axis=0)
        high = diag.astype(jnp.bfloat16)
        low = (diag - high.astype(jnp.float32)).astype(jnp.bfloat16)
        q_pair = q_ref[:, cols]
        carried = (jnp.dot(q_pair, high, preferred_element_type=jnp.float32)
                   + jnp.dot(q_pair, low, preferred_element_type=jnp.float32))
        combined = inside_ref[:, cols] + carried
        square = combined * combined
        sum_first = jnp.sum(jnp.where(first, square, 0.0), axis=-1, keepdims=True)
        sum_second = jnp.sum(jnp.where(first, 0.0, square), axis=-1, keepdims=True)
        scale = jnp.where(first, lax.rsqrt(sum_first / head_size + 1e-06),
                          lax.rsqrt(sum_second / head_size + 1e-06))
        att_ref[:, cols] = (combined * scale * hgain_ref[:, cols]).astype(jnp.bfloat16)
    out = emb_ref[...].astype(jnp.float32) + jnp.dot(att_ref[...], out_w_ref[...],
                                                     preferred_element_type=jnp.float32)
    out_ref[...] = out.astype(jnp.bfloat16)


def full(shape):
    return pl.BlockSpec(shape, lambda b: (0,) * len(shape))


def shards(ticks, conv_weight, norm_gain, qkv_weight, head_gain, out_weight, state_in):
    tick_count, feat = ticks.shape
    token_count = tick_count // STRIDE
    model_width = conv_weight.shape[1]
    head_count, head_size = state_in.shape[0], state_in.shape[1]
    pairs = model_width // PAIR
    blocks = token_count // BLK
    block_ticks = BLK * STRIDE

    prev = from_behind(ticks[tick_count - 2 * STRIDE :], "inner", 1)
    rows_spec = pl.BlockSpec((BLK, model_width), lambda b: (b, 0))
    state_spec = pl.BlockSpec((1, pairs, head_size, PAIR), lambda b: (b, 0, 0, 0))
    emb, queries, keys, values, states = pl.pallas_call(
        embed_kernel,
        grid=(blocks,),
        in_specs=[
            pl.BlockSpec((block_ticks, feat), lambda b: (b, 0)),
            full((2 * STRIDE, feat)),
            full(conv_weight.shape),
            full((1, model_width)),
            full(qkv_weight.shape),
        ],
        out_specs=[rows_spec, rows_spec, rows_spec, rows_spec, state_spec],
        out_shape=[jax.ShapeDtypeStruct((token_count, model_width), jnp.bfloat16)] * 4 + [
            jax.ShapeDtypeStruct((blocks, pairs, head_size, PAIR), jnp.float32),
        ],
        scratch_shapes=[pltpu.VMEM((block_ticks + STRIDE, feat), jnp.float32)],
        compiler_params=pltpu.CompilerParams(dimension_semantics=("arbitrary",)),
    )(ticks, prev, conv_weight, norm_gain.reshape(1, model_width), qkv_weight)

    def inside_block(block, earlier, q, k, v):
        spec = pl.BlockSpec((BLK, model_width), lambda i, block=block: (block, 0))
        return pl.pallas_call(
            inside_kernel,
            grid=(1,),
            in_specs=[spec, spec, spec, pl.BlockSpec(memory_space=pl.ANY)],
            out_specs=spec,
            out_shape=jax.ShapeDtypeStruct((token_count, model_width), jnp.float32),
            input_output_aliases={3: 0},
            cost_estimate=pl.CostEstimate(flops=8 * BLK * BLK * model_width, transcendentals=0,
                                          bytes_accessed=6 * BLK * model_width + 4 * BLK * model_width),
        )(q, k, v, earlier)

    local = states[0]
    for block in range(1, blocks):
        local = local + states[block]
    count = lax.axis_size("inner")
    inside = jnp.zeros((token_count, model_width), jnp.float32)
    total, steps, block = local, 1, 0
    while steps < count:
        if block < blocks:
            total, q_in, k_in, v_in = lax.optimization_barrier((total, queries, keys, values))
        received = from_behind(total, "inner", steps)
        if block < blocks:
            inside = inside_block(block, inside, q_in, k_in, v_in)
            received, inside = lax.optimization_barrier((received, inside))
            block += 1
        total = total + received
        steps *= 2
    while block < blocks:
        inside = inside_block(block, inside, queries, keys, values)
        block += 1
    prefix = total - local
    packed_in = state_in.reshape(pairs, 2, head_size, head_size).transpose(0, 2, 1, 3)
    carried = packed_in.reshape(pairs, head_size, PAIR) + prefix
    before = [carried]
    for block in range(1, blocks):
        before.append(before[-1] + states[block - 1])
    before = jnp.stack(before)

    return pl.pallas_call(
        out_kernel,
        grid=(blocks,),
        in_specs=[
            rows_spec,
            state_spec,
            rows_spec,
            rows_spec,
            full((1, model_width)),
            full(out_weight.shape),
        ],
        out_specs=rows_spec,
        out_shape=jax.ShapeDtypeStruct((token_count, model_width), jnp.bfloat16),
        scratch_shapes=[pltpu.VMEM((BLK, model_width), jnp.bfloat16)],
        compiler_params=pltpu.CompilerParams(dimension_semantics=("arbitrary",)),
    )(queries, before, inside, emb, head_gain.reshape(1, model_width), out_weight)


def solution(mesh):
    in_specs = (P(("groups", "inner"), None), P(), P(), P(), P(), P(), P("groups", None, None))
    out_specs = P(("groups", "inner"), None)
    return jax.shard_map(shards, mesh=mesh, in_specs=in_specs, out_specs=out_specs, check_vma=False)
```

```python
import functools

import jax
import jax.numpy as jnp
from jax import lax
from jax.experimental import pallas as pl
from jax.experimental.pallas import tpu as pltpu
from jax.sharding import PartitionSpec as P

STRIDE = 8
BLK = 512
PAIR = 128


def from_behind(value, axis, steps):
    count = lax.axis_size(axis)
    initial, last = (max(0, -steps), min(count, count - steps))
    return lax.ppermute(value, axis, [(source, source + steps) for source in range(initial, last)])


def exclusive_scan(value, axis):
    count = lax.axis_size(axis)
    total = value
    steps = 1
    while steps < count:
        total = total + from_behind(total, axis, steps)
        steps *= 2
    return total - value


def embed_kernel(ticks_ref, prev_ref, conv_ref, gain_ref, qkv_w_ref,
                 emb_ref, q_ref, k_ref, v_ref, state_ref, wide_ref):
    b = pl.program_id(0)
    block_ticks = ticks_ref.shape[0]
    tokens = block_ticks // STRIDE
    model_width = emb_ref.shape[1]

    @pl.when(b == 0)
    def _():
        wide_ref[0:STRIDE, :] = prev_ref[STRIDE : 2 * STRIDE, :].astype(jnp.float32)

    @pl.when(b > 0)
    def _():
        wide_ref[0:STRIDE, :] = wide_ref[block_ticks : block_ticks + STRIDE, :]

    wide_ref[STRIDE:, :] = ticks_ref[...].astype(jnp.float32)
    pieces = [wide_ref[pl.ds(j, tokens, stride=STRIDE), :] for j in range(2 * STRIDE)]
    lhs = jnp.concatenate(pieces, axis=1).astype(jnp.bfloat16)
    emb = jnp.dot(lhs, conv_ref[...], preferred_element_type=jnp.float32).astype(jnp.bfloat16)
    emb_ref[...] = emb
    embed_f = emb.astype(jnp.float32)
    mean_sq = jnp.mean(embed_f * embed_f, axis=-1, keepdims=True)
    normed = (embed_f * lax.rsqrt(mean_sq + 1e-05) * gain_ref[...]).astype(jnp.bfloat16)

    def project(part):
        weight = qkv_w_ref[:, part * model_width : (part + 1) * model_width]
        return jnp.dot(normed, weight, preferred_element_type=jnp.float32).astype(jnp.bfloat16)

    queries, keys, values = project(0), project(1), project(2)
    q_ref[...] = queries
    k_ref[...] = keys
    v_ref[...] = values
    lane = lax.broadcasted_iota(jnp.int32, (1, PAIR), 1)
    first = lane < PAIR // 2
    for pair in range(model_width // PAIR):
        cols = slice(pair * PAIR, (pair + 1) * PAIR)
        kv = lax.dot_general(keys[:, cols], values[:, cols], (((0,), (0,)), ((), ())),
                             preferred_element_type=jnp.float32)
        half = PAIR // 2
        state_ref[0, pair] = jnp.where(first, kv[:half], kv[half:])


def inside_kernel(q_ref, k_ref, v_ref, earlier_ref, inside_ref):
    del earlier_ref
    first_inside_kernel(q_ref, k_ref, v_ref, inside_ref)


def first_inside_kernel(q_ref, k_ref, v_ref, inside_ref):
    queries, keys, values = q_ref[...], k_ref[...], v_ref[...]
    tokens = queries.shape[0]
    lane = lax.broadcasted_iota(jnp.int32, (1, PAIR), 1)
    first = lane < PAIR // 2
    causal = (lax.broadcasted_iota(jnp.int32, (tokens, tokens), 0)
              >= lax.broadcasted_iota(jnp.int32, (tokens, tokens), 1))
    zero = jnp.zeros((), jnp.bfloat16)
    for pair in range(queries.shape[1] // PAIR):
        cols = slice(pair * PAIR, (pair + 1) * PAIR)
        q_pair, k_pair, v_pair = queries[:, cols], keys[:, cols], values[:, cols]
        inside = None
        for use in (first, ~first):
            q_one = jnp.where(use, q_pair, zero)
            scores = lax.dot_general(q_one, k_pair, (((1,), (1,)), ((), ())),
                                     preferred_element_type=jnp.float32)
            scores = jnp.where(causal, scores, 0.0).astype(jnp.bfloat16)
            term = jnp.dot(scores, jnp.where(use, v_pair, zero), preferred_element_type=jnp.float32)
            inside = term if inside is None else inside + term
        inside_ref[:, cols] = inside


def out_kernel(q_ref, state_ref, inside_ref, emb_ref, hgain_ref, out_w_ref, out_ref, att_ref):
    model_width = out_ref.shape[1]
    lane = lax.broadcasted_iota(jnp.int32, (1, PAIR), 1)
    first = lane < PAIR // 2
    head_size = PAIR // 2
    for pair in range(model_width // PAIR):
        cols = slice(pair * PAIR, (pair + 1) * PAIR)
        packed = state_ref[0, pair]
        diag = jnp.concatenate([jnp.where(first, packed, 0.0), jnp.where(first, 0.0, packed)], axis=0)
        high = diag.astype(jnp.bfloat16)
        low = (diag - high.astype(jnp.float32)).astype(jnp.bfloat16)
        q_pair = q_ref[:, cols]
        carried = (jnp.dot(q_pair, high, preferred_element_type=jnp.float32)
                   + jnp.dot(q_pair, low, preferred_element_type=jnp.float32))
        combined = inside_ref[:, cols] + carried
        square = combined * combined
        sum_first = jnp.sum(jnp.where(first, square, 0.0), axis=-1, keepdims=True)
        sum_second = jnp.sum(jnp.where(first, 0.0, square), axis=-1, keepdims=True)
        scale = jnp.where(first, lax.rsqrt(sum_first / head_size + 1e-06),
                          lax.rsqrt(sum_second / head_size + 1e-06))
        att_ref[:, cols] = (combined * scale * hgain_ref[:, cols]).astype(jnp.bfloat16)
    out = emb_ref[...].astype(jnp.float32) + jnp.dot(att_ref[...], out_w_ref[...],
                                                     preferred_element_type=jnp.float32)
    out_ref[...] = out.astype(jnp.bfloat16)


def full(shape):
    return pl.BlockSpec(shape, lambda b: (0,) * len(shape))


def shards(ticks, conv_weight, norm_gain, qkv_weight, head_gain, out_weight, state_in):
    tick_count, feat = ticks.shape
    token_count = tick_count // STRIDE
    model_width = conv_weight.shape[1]
    head_count, head_size = state_in.shape[0], state_in.shape[1]
    pairs = model_width // PAIR
    blocks = token_count // BLK
    block_ticks = BLK * STRIDE

    prev = from_behind(ticks[tick_count - 2 * STRIDE :], "inner", 1)
    rows_spec = pl.BlockSpec((BLK, model_width), lambda b: (b, 0))
    state_spec = pl.BlockSpec((1, pairs, head_size, PAIR), lambda b: (b, 0, 0, 0))
    emb, queries, keys, values, states = pl.pallas_call(
        embed_kernel,
        grid=(blocks,),
        in_specs=[
            pl.BlockSpec((block_ticks, feat), lambda b: (b, 0)),
            full((2 * STRIDE, feat)),
            full(conv_weight.shape),
            full((1, model_width)),
            full(qkv_weight.shape),
        ],
        out_specs=[rows_spec, rows_spec, rows_spec, rows_spec, state_spec],
        out_shape=[jax.ShapeDtypeStruct((token_count, model_width), jnp.bfloat16)] * 4 + [
            jax.ShapeDtypeStruct((blocks, pairs, head_size, PAIR), jnp.float32),
        ],
        scratch_shapes=[pltpu.VMEM((block_ticks + STRIDE, feat), jnp.float32)],
        compiler_params=pltpu.CompilerParams(dimension_semantics=("arbitrary",)),
    )(ticks, prev, conv_weight, norm_gain.reshape(1, model_width), qkv_weight)

    def inside_block(block, earlier, q, k, v):
        spec = pl.BlockSpec((BLK, PAIR), lambda p, block=block: (block, p))
        in_specs, operands, aliases = [spec, spec, spec], [q, k, v], {}
        kernel = inside_kernel
        if earlier is not None:
            in_specs.append(pl.BlockSpec(memory_space=pl.ANY))
            operands.append(earlier)
            aliases = {3: 0}
        else:
            kernel = first_inside_kernel
        return pl.pallas_call(
            kernel,
            grid=(pairs,),
            in_specs=in_specs,
            out_specs=spec,
            out_shape=jax.ShapeDtypeStruct((token_count, model_width), jnp.float32),
            input_output_aliases=aliases,
            cost_estimate=pl.CostEstimate(flops=8 * BLK * BLK * model_width, transcendentals=0,
                                          bytes_accessed=6 * BLK * model_width + 4 * BLK * model_width),
        )(*operands)

    local = states[0]
    for block in range(1, blocks):
        local = local + states[block]
    count = lax.axis_size("inner")
    inside = None
    total, steps, block = local, 1, 0
    while steps < count:
        if block < blocks:
            total, q_in, k_in, v_in = lax.optimization_barrier((total, queries, keys, values))
        received = from_behind(total, "inner", steps)
        if block < blocks:
            inside = inside_block(block, inside, q_in, k_in, v_in)
            received, inside = lax.optimization_barrier((received, inside))
            block += 1
        total = total + received
        steps *= 2
    while block < blocks:
        inside = inside_block(block, inside, queries, keys, values)
        block += 1
    prefix = total - local
    packed_in = state_in.reshape(pairs, 2, head_size, head_size).transpose(0, 2, 1, 3)
    carried = packed_in.reshape(pairs, head_size, PAIR) + prefix
    before = [carried]
    for block in range(1, blocks):
        before.append(before[-1] + states[block - 1])
    before = jnp.stack(before)

    return pl.pallas_call(
        out_kernel,
        grid=(blocks,),
        in_specs=[
            rows_spec,
            state_spec,
            rows_spec,
            rows_spec,
            full((1, model_width)),
            full(out_weight.shape),
        ],
        out_specs=rows_spec,
        out_shape=jax.ShapeDtypeStruct((token_count, model_width), jnp.bfloat16),
        scratch_shapes=[pltpu.VMEM((BLK, model_width), jnp.bfloat16)],
        compiler_params=pltpu.CompilerParams(dimension_semantics=("arbitrary",)),
    )(queries, before, inside, emb, head_gain.reshape(1, model_width), out_weight)


def solution(mesh):
    in_specs = (P(("groups", "inner"), None), P(), P(), P(), P(), P(), P("groups", None, None))
    out_specs = P(("groups", "inner"), None)
    return jax.shard_map(shards, mesh=mesh, in_specs=in_specs, out_specs=out_specs, check_vma=False)
```

```python
import functools

import jax
import jax.numpy as jnp
from jax import lax
from jax.experimental import pallas as pl
from jax.experimental.pallas import tpu as pltpu
from jax.sharding import PartitionSpec as P

STRIDE = 8
BLK = 512
PAIR = 128


def from_behind(value, axis, steps):
    count = lax.axis_size(axis)
    initial, last = (max(0, -steps), min(count, count - steps))
    return lax.ppermute(value, axis, [(source, source + steps) for source in range(initial, last)])


def exclusive_scan(value, axis):
    count = lax.axis_size(axis)
    total = value
    steps = 1
    while steps < count:
        total = total + from_behind(total, axis, steps)
        steps *= 2
    return total - value


def embed_kernel(ticks_ref, prev_ref, conv_ref, gain_ref, qkv_w_ref,
                 emb_ref, q_ref, k_ref, v_ref, state_ref, wide_ref):
    b = pl.program_id(0)
    block_ticks = ticks_ref.shape[0]
    tokens = block_ticks // STRIDE
    model_width = emb_ref.shape[1]

    @pl.when(b == 0)
    def _():
        wide_ref[0:STRIDE, :] = prev_ref[STRIDE : 2 * STRIDE, :].astype(jnp.float32)

    @pl.when(b > 0)
    def _():
        wide_ref[0:STRIDE, :] = wide_ref[block_ticks : block_ticks + STRIDE, :]

    wide_ref[STRIDE:, :] = ticks_ref[...].astype(jnp.float32)
    pieces = [wide_ref[pl.ds(j, tokens, stride=STRIDE), :] for j in range(2 * STRIDE)]
    lhs = jnp.concatenate(pieces, axis=1).astype(jnp.bfloat16)
    emb = jnp.dot(lhs, conv_ref[...], preferred_element_type=jnp.float32).astype(jnp.bfloat16)
    emb_ref[...] = emb
    embed_f = emb.astype(jnp.float32)
    mean_sq = jnp.mean(embed_f * embed_f, axis=-1, keepdims=True)
    normed = (embed_f * lax.rsqrt(mean_sq + 1e-05) * gain_ref[...]).astype(jnp.bfloat16)

    def project(part):
        weight = qkv_w_ref[:, part * model_width : (part + 1) * model_width]
        return jnp.dot(normed, weight, preferred_element_type=jnp.float32).astype(jnp.bfloat16)

    queries, keys, values = project(0), project(1), project(2)
    q_ref[...] = queries
    k_ref[...] = keys
    v_ref[...] = values
    lane = lax.broadcasted_iota(jnp.int32, (1, PAIR), 1)
    first = lane < PAIR // 2
    for pair in range(model_width // PAIR):
        cols = slice(pair * PAIR, (pair + 1) * PAIR)
        kv = lax.dot_general(keys[:, cols], values[:, cols], (((0,), (0,)), ((), ())),
                             preferred_element_type=jnp.float32)
        half = PAIR // 2
        state_ref[0, pair] = jnp.where(first, kv[:half], kv[half:])


def inside_kernel(q_ref, k_ref, v_ref, earlier_ref, inside_ref):
    del earlier_ref
    first_inside_kernel(q_ref, k_ref, v_ref, inside_ref)


def first_inside_kernel(q_ref, k_ref, v_ref, inside_ref):
    queries, keys, values = q_ref[...], k_ref[...], v_ref[...]
    tokens = queries.shape[0]
    lane = lax.broadcasted_iota(jnp.int32, (1, PAIR), 1)
    first = lane < PAIR // 2
    causal = (lax.broadcasted_iota(jnp.int32, (tokens, tokens), 0)
              >= lax.broadcasted_iota(jnp.int32, (tokens, tokens), 1))
    zero = jnp.zeros((), jnp.bfloat16)
    for pair in range(queries.shape[1] // PAIR):
        cols = slice(pair * PAIR, (pair + 1) * PAIR)
        q_pair, k_pair, v_pair = queries[:, cols], keys[:, cols], values[:, cols]
        inside = None
        for use in (first, ~first):
            q_one = jnp.where(use, q_pair, zero)
            scores = lax.dot_general(q_one, k_pair, (((1,), (1,)), ((), ())),
                                     preferred_element_type=jnp.float32)
            scores = jnp.where(causal, scores, 0.0).astype(jnp.bfloat16)
            term = jnp.dot(scores, jnp.where(use, v_pair, zero), preferred_element_type=jnp.float32)
            inside = term if inside is None else inside + term
        inside_ref[:, cols] = inside


def out_kernel(q_ref, state_ref, inside_ref, emb_ref, hgain_ref, out_w_ref, out_ref, att_ref):
    model_width = out_ref.shape[1]
    lane = lax.broadcasted_iota(jnp.int32, (1, PAIR), 1)
    first = lane < PAIR // 2
    head_size = PAIR // 2
    for pair in range(model_width // PAIR):
        cols = slice(pair * PAIR, (pair + 1) * PAIR)
        packed = state_ref[0, pair]
        diag = jnp.concatenate([jnp.where(first, packed, 0.0), jnp.where(first, 0.0, packed)], axis=0)
        high = diag.astype(jnp.bfloat16)
        low = (diag - high.astype(jnp.float32)).astype(jnp.bfloat16)
        q_pair = q_ref[:, cols]
        carried = (jnp.dot(q_pair, high, preferred_element_type=jnp.float32)
                   + jnp.dot(q_pair, low, preferred_element_type=jnp.float32))
        combined = inside_ref[:, cols] + carried
        square = combined * combined
        sum_first = jnp.sum(jnp.where(first, square, 0.0), axis=-1, keepdims=True)
        sum_second = jnp.sum(jnp.where(first, 0.0, square), axis=-1, keepdims=True)
        scale = jnp.where(first, lax.rsqrt(sum_first / head_size + 1e-06),
                          lax.rsqrt(sum_second / head_size + 1e-06))
        att_ref[:, cols] = (combined * scale * hgain_ref[:, cols]).astype(jnp.bfloat16)
    out = emb_ref[...].astype(jnp.float32) + jnp.dot(att_ref[...], out_w_ref[...],
                                                     preferred_element_type=jnp.float32)
    out_ref[...] = out.astype(jnp.bfloat16)


def full(shape):
    return pl.BlockSpec(shape, lambda b: (0,) * len(shape))


def shards(ticks, conv_weight, norm_gain, qkv_weight, head_gain, out_weight, state_in):
    tick_count, feat = ticks.shape
    token_count = tick_count // STRIDE
    model_width = conv_weight.shape[1]
    head_count, head_size = state_in.shape[0], state_in.shape[1]
    pairs = model_width // PAIR
    blocks = token_count // BLK
    block_ticks = BLK * STRIDE

    prev = from_behind(ticks[tick_count - 2 * STRIDE :], "inner", 1)
    rows_spec = pl.BlockSpec((BLK, model_width), lambda b: (b, 0))
    state_spec = pl.BlockSpec((1, pairs, head_size, PAIR), lambda b: (b, 0, 0, 0))
    emb, queries, keys, values, states = pl.pallas_call(
        embed_kernel,
        grid=(blocks,),
        in_specs=[
            pl.BlockSpec((block_ticks, feat), lambda b: (b, 0)),
            full((2 * STRIDE, feat)),
            full(conv_weight.shape),
            full((1, model_width)),
            full(qkv_weight.shape),
        ],
        out_specs=[rows_spec, rows_spec, rows_spec, rows_spec, state_spec],
        out_shape=[jax.ShapeDtypeStruct((token_count, model_width), jnp.bfloat16)] * 4 + [
            jax.ShapeDtypeStruct((blocks, pairs, head_size, PAIR), jnp.float32),
        ],
        scratch_shapes=[pltpu.VMEM((block_ticks + STRIDE, feat), jnp.float32)],
        compiler_params=pltpu.CompilerParams(dimension_semantics=("arbitrary",)),
    )(ticks, prev, conv_weight, norm_gain.reshape(1, model_width), qkv_weight)

    def inside_block(block, earlier, q, k, v):
        spec = pl.BlockSpec((BLK, 3 * PAIR), lambda p, block=block: (block, p))
        in_specs, operands, aliases = [spec, spec, spec], [q, k, v], {}
        kernel = inside_kernel
        if earlier is not None:
            in_specs.append(pl.BlockSpec(memory_space=pl.ANY))
            operands.append(earlier)
            aliases = {3: 0}
        else:
            kernel = first_inside_kernel
        return pl.pallas_call(
            kernel,
            grid=(pairs // 3,),
            in_specs=in_specs,
            out_specs=spec,
            out_shape=jax.ShapeDtypeStruct((token_count, model_width), jnp.float32),
            input_output_aliases=aliases,
            cost_estimate=pl.CostEstimate(flops=8 * BLK * BLK * model_width, transcendentals=0,
                                          bytes_accessed=6 * BLK * model_width + 4 * BLK * model_width),
        )(*operands)

    local = states[0]
    for block in range(1, blocks):
        local = local + states[block]
    count = lax.axis_size("inner")
    inside = None
    total, steps, block = local, 1, 0
    while steps < count:
        if block < blocks:
            total, q_in, k_in, v_in = lax.optimization_barrier((total, queries, keys, values))
        received = from_behind(total, "inner", steps)
        if block < blocks:
            inside = inside_block(block, inside, q_in, k_in, v_in)
            received, inside = lax.optimization_barrier((received, inside))
            block += 1
        total = total + received
        steps *= 2
    while block < blocks:
        inside = inside_block(block, inside, queries, keys, values)
        block += 1
    prefix = total - local
    packed_in = state_in.reshape(pairs, 2, head_size, head_size).transpose(0, 2, 1, 3)
    carried = packed_in.reshape(pairs, head_size, PAIR) + prefix
    before = [carried]
    for block in range(1, blocks):
        before.append(before[-1] + states[block - 1])
    before = jnp.stack(before)

    return pl.pallas_call(
        out_kernel,
        grid=(blocks,),
        in_specs=[
            rows_spec,
            state_spec,
            rows_spec,
            rows_spec,
            full((1, model_width)),
            full(out_weight.shape),
        ],
        out_specs=rows_spec,
        out_shape=jax.ShapeDtypeStruct((token_count, model_width), jnp.bfloat16),
        scratch_shapes=[pltpu.VMEM((BLK, model_width), jnp.bfloat16)],
        compiler_params=pltpu.CompilerParams(dimension_semantics=("arbitrary",)),
    )(queries, before, inside, emb, head_gain.reshape(1, model_width), out_weight)


def solution(mesh):
    in_specs = (P(("groups", "inner"), None), P(), P(), P(), P(), P(), P("groups", None, None))
    out_specs = P(("groups", "inner"), None)
    return jax.shard_map(shards, mesh=mesh, in_specs=in_specs, out_specs=out_specs, check_vma=False)
```

```python
import functools

import jax
import jax.numpy as jnp
from jax import lax
from jax.experimental import pallas as pl
from jax.experimental.pallas import tpu as pltpu
from jax.sharding import PartitionSpec as P

STRIDE = 8
BLK = 512
PAIR = 128


def from_behind(value, axis, steps):
    count = lax.axis_size(axis)
    initial, last = (max(0, -steps), min(count, count - steps))
    return lax.ppermute(value, axis, [(source, source + steps) for source in range(initial, last)])


def exclusive_scan(value, axis):
    count = lax.axis_size(axis)
    total = value
    steps = 1
    while steps < count:
        total = total + from_behind(total, axis, steps)
        steps *= 2
    return total - value


def embed_kernel(ticks_ref, prev_ref, conv_ref, gain_ref, qkv_w_ref,
                 emb_ref, q_ref, k_ref, v_ref, state_ref, wide_ref):
    b = pl.program_id(0)
    block_ticks = ticks_ref.shape[0]
    tokens = block_ticks // STRIDE
    model_width = emb_ref.shape[1]

    @pl.when(b == 0)
    def _():
        wide_ref[0:STRIDE, :] = prev_ref[STRIDE : 2 * STRIDE, :].astype(jnp.float32)

    @pl.when(b > 0)
    def _():
        wide_ref[0:STRIDE, :] = wide_ref[block_ticks : block_ticks + STRIDE, :]

    wide_ref[STRIDE:, :] = ticks_ref[...].astype(jnp.float32)
    pieces = [wide_ref[pl.ds(j, tokens, stride=STRIDE), :] for j in range(2 * STRIDE)]
    lhs = jnp.concatenate(pieces, axis=1).astype(jnp.bfloat16)
    emb = jnp.dot(lhs, conv_ref[...], preferred_element_type=jnp.float32).astype(jnp.bfloat16)
    emb_ref[...] = emb
    embed_f = emb.astype(jnp.float32)
    mean_sq = jnp.mean(embed_f * embed_f, axis=-1, keepdims=True)
    normed = (embed_f * lax.rsqrt(mean_sq + 1e-05) * gain_ref[...]).astype(jnp.bfloat16)

    def project(part):
        weight = qkv_w_ref[:, part * model_width : (part + 1) * model_width]
        return jnp.dot(normed, weight, preferred_element_type=jnp.float32).astype(jnp.bfloat16)

    queries, keys, values = project(0), project(1), project(2)
    q_ref[...] = queries
    k_ref[...] = keys
    v_ref[...] = values
    lane = lax.broadcasted_iota(jnp.int32, (1, PAIR), 1)
    first = lane < PAIR // 2
    for pair in range(model_width // PAIR):
        cols = slice(pair * PAIR, (pair + 1) * PAIR)
        kv = lax.dot_general(keys[:, cols], values[:, cols], (((0,), (0,)), ((), ())),
                             preferred_element_type=jnp.float32)
        half = PAIR // 2
        state_ref[0, pair] = jnp.where(first, kv[:half], kv[half:])


def inside_kernel(q_ref, k_ref, v_ref, earlier_ref, inside_ref):
    del earlier_ref
    first_inside_kernel(q_ref, k_ref, v_ref, inside_ref)


def first_inside_kernel(q_ref, k_ref, v_ref, inside_ref):
    queries, keys, values = q_ref[...], k_ref[...], v_ref[...]
    tokens = queries.shape[0]
    lane = lax.broadcasted_iota(jnp.int32, (1, PAIR), 1)
    first = lane < PAIR // 2
    causal = (lax.broadcasted_iota(jnp.int32, (tokens, tokens), 0)
              >= lax.broadcasted_iota(jnp.int32, (tokens, tokens), 1))
    zero = jnp.zeros((), jnp.bfloat16)
    for pair in range(queries.shape[1] // PAIR):
        cols = slice(pair * PAIR, (pair + 1) * PAIR)
        q_pair, k_pair, v_pair = queries[:, cols], keys[:, cols], values[:, cols]
        inside = None
        for use in (first, ~first):
            q_one = jnp.where(use, q_pair, zero)
            scores = lax.dot_general(q_one, k_pair, (((1,), (1,)), ((), ())),
                                     preferred_element_type=jnp.float32)
            scores = jnp.where(causal, scores, 0.0).astype(jnp.bfloat16)
            term = jnp.dot(scores, jnp.where(use, v_pair, zero), preferred_element_type=jnp.float32)
            inside = term if inside is None else inside + term
        inside_ref[:, cols] = inside


def out_kernel(q_ref, state_ref, inside_ref, emb_ref, hgain_ref, out_w_ref, out_ref, att_ref):
    model_width = out_ref.shape[1]
    lane = lax.broadcasted_iota(jnp.int32, (1, PAIR), 1)
    first = lane < PAIR // 2
    head_size = PAIR // 2
    for pair in range(model_width // PAIR):
        cols = slice(pair * PAIR, (pair + 1) * PAIR)
        packed = state_ref[0, pair]
        diag = jnp.concatenate([jnp.where(first, packed, 0.0), jnp.where(first, 0.0, packed)], axis=0)
        high = diag.astype(jnp.bfloat16)
        low = (diag - high.astype(jnp.float32)).astype(jnp.bfloat16)
        q_pair = q_ref[:, cols]
        carried = (jnp.dot(q_pair, high, preferred_element_type=jnp.float32)
                   + jnp.dot(q_pair, low, preferred_element_type=jnp.float32))
        combined = inside_ref[:, cols] + carried
        square = combined * combined
        sum_first = jnp.sum(jnp.where(first, square, 0.0), axis=-1, keepdims=True)
        sum_second = jnp.sum(jnp.where(first, 0.0, square), axis=-1, keepdims=True)
        scale = jnp.where(first, lax.rsqrt(sum_first / head_size + 1e-06),
                          lax.rsqrt(sum_second / head_size + 1e-06))
        att_ref[:, cols] = (combined * scale * hgain_ref[:, cols]).astype(jnp.bfloat16)
    out = emb_ref[...].astype(jnp.float32) + jnp.dot(att_ref[...], out_w_ref[...],
                                                     preferred_element_type=jnp.float32)
    out_ref[...] = out.astype(jnp.bfloat16)


def full(shape):
    return pl.BlockSpec(shape, lambda b: (0,) * len(shape))


def shards(ticks, conv_weight, norm_gain, qkv_weight, head_gain, out_weight, state_in):
    tick_count, feat = ticks.shape
    token_count = tick_count // STRIDE
    model_width = conv_weight.shape[1]
    head_count, head_size = state_in.shape[0], state_in.shape[1]
    pairs = model_width // PAIR
    blocks = token_count // BLK
    block_ticks = BLK * STRIDE

    prev = from_behind(ticks[tick_count - 2 * STRIDE :], "inner", 1)
    rows_spec = pl.BlockSpec((BLK, model_width), lambda b: (b, 0))
    state_spec = pl.BlockSpec((1, pairs, head_size, PAIR), lambda b: (b, 0, 0, 0))
    emb, queries, keys, values, states = pl.pallas_call(
        embed_kernel,
        grid=(blocks,),
        in_specs=[
            pl.BlockSpec((block_ticks, feat), lambda b: (b, 0)),
            full((2 * STRIDE, feat)),
            full(conv_weight.shape),
            full((1, model_width)),
            full(qkv_weight.shape),
        ],
        out_specs=[rows_spec, rows_spec, rows_spec, rows_spec, state_spec],
        out_shape=[jax.ShapeDtypeStruct((token_count, model_width), jnp.bfloat16)] * 4 + [
            jax.ShapeDtypeStruct((blocks, pairs, head_size, PAIR), jnp.float32),
        ],
        scratch_shapes=[pltpu.VMEM((block_ticks + STRIDE, feat), jnp.float32)],
        compiler_params=pltpu.CompilerParams(dimension_semantics=("arbitrary",)),
    )(ticks, prev, conv_weight, norm_gain.reshape(1, model_width), qkv_weight)

    halves = 2
    piece_width = model_width // halves

    def inside_block(piece, earlier, q, k, v):
        block, half = divmod(piece, halves)
        spec = pl.BlockSpec((BLK, piece_width), lambda p, block=block, half=half: (block, half + p))
        in_specs, operands, aliases = [spec, spec, spec], [q, k, v], {}
        kernel = inside_kernel
        if earlier is not None:
            in_specs.append(pl.BlockSpec(memory_space=pl.ANY))
            operands.append(earlier)
            aliases = {3: 0}
        else:
            kernel = first_inside_kernel
        return pl.pallas_call(
            kernel,
            grid=(1,),
            in_specs=in_specs,
            out_specs=spec,
            out_shape=jax.ShapeDtypeStruct((token_count, model_width), jnp.float32),
            input_output_aliases=aliases,
            cost_estimate=pl.CostEstimate(flops=8 * BLK * BLK * piece_width, transcendentals=0,
                                          bytes_accessed=10 * BLK * piece_width),
        )(*operands)

    local = states[0]
    for block in range(1, blocks):
        local = local + states[block]
    count = lax.axis_size("inner")
    inside = None
    total, steps, block = local, 1, 0
    while steps < count:
        if block < blocks * halves:
            total, q_in, k_in, v_in = lax.optimization_barrier((total, queries, keys, values))
        received = from_behind(total, "inner", steps)
        if block < blocks * halves:
            inside = inside_block(block, inside, q_in, k_in, v_in)
            received, inside = lax.optimization_barrier((received, inside))
            block += 1
        total = total + received
        steps *= 2
    while block < blocks * halves:
        inside = inside_block(block, inside, queries, keys, values)
        block += 1
    prefix = total - local
    packed_in = state_in.reshape(pairs, 2, head_size, head_size).transpose(0, 2, 1, 3)
    carried = packed_in.reshape(pairs, head_size, PAIR) + prefix
    before = [carried]
    for block in range(1, blocks):
        before.append(before[-1] + states[block - 1])
    before = jnp.stack(before)

    return pl.pallas_call(
        out_kernel,
        grid=(blocks,),
        in_specs=[
            rows_spec,
            state_spec,
            rows_spec,
            rows_spec,
            full((1, model_width)),
            full(out_weight.shape),
        ],
        out_specs=rows_spec,
        out_shape=jax.ShapeDtypeStruct((token_count, model_width), jnp.bfloat16),
        scratch_shapes=[pltpu.VMEM((BLK, model_width), jnp.bfloat16)],
        compiler_params=pltpu.CompilerParams(dimension_semantics=("arbitrary",)),
    )(queries, before, inside, emb, head_gain.reshape(1, model_width), out_weight)


def solution(mesh):
    in_specs = (P(("groups", "inner"), None), P(), P(), P(), P(), P(), P("groups", None, None))
    out_specs = P(("groups", "inner"), None)
    return jax.shard_map(shards, mesh=mesh, in_specs=in_specs, out_specs=out_specs, check_vma=False)
```

```python
import functools

import jax
import jax.numpy as jnp
from jax import lax
from jax.experimental import pallas as pl
from jax.experimental.pallas import tpu as pltpu
from jax.sharding import PartitionSpec as P

STRIDE = 8
BLK = 512
PAIR = 128


def from_behind(value, axis, steps):
    count = lax.axis_size(axis)
    initial, last = (max(0, -steps), min(count, count - steps))
    return lax.ppermute(value, axis, [(source, source + steps) for source in range(initial, last)])


def exclusive_scan(value, axis):
    count = lax.axis_size(axis)
    total = value
    steps = 1
    while steps < count:
        total = total + from_behind(total, axis, steps)
        steps *= 2
    return total - value


def embed_kernel(ticks_ref, prev_ref, conv_ref, gain_ref, qkv_w_ref,
                 emb_ref, q_ref, k_ref, v_ref, state_ref, wide_ref):
    b = pl.program_id(0)
    block_ticks = ticks_ref.shape[0]
    tokens = block_ticks // STRIDE
    model_width = emb_ref.shape[1]

    @pl.when(b == 0)
    def _():
        wide_ref[0:STRIDE, :] = prev_ref[STRIDE : 2 * STRIDE, :].astype(jnp.float32)

    @pl.when(b > 0)
    def _():
        wide_ref[0:STRIDE, :] = wide_ref[block_ticks : block_ticks + STRIDE, :]

    wide_ref[STRIDE:, :] = ticks_ref[...].astype(jnp.float32)
    pieces = [wide_ref[pl.ds(j, tokens, stride=STRIDE), :] for j in range(2 * STRIDE)]
    lhs = jnp.concatenate(pieces, axis=1).astype(jnp.bfloat16)
    emb = jnp.dot(lhs, conv_ref[...], preferred_element_type=jnp.float32).astype(jnp.bfloat16)
    emb_ref[...] = emb
    embed_f = emb.astype(jnp.float32)
    mean_sq = jnp.mean(embed_f * embed_f, axis=-1, keepdims=True)
    normed = (embed_f * lax.rsqrt(mean_sq + 1e-05) * gain_ref[...]).astype(jnp.bfloat16)

    def project(part):
        weight = qkv_w_ref[:, part * model_width : (part + 1) * model_width]
        return jnp.dot(normed, weight, preferred_element_type=jnp.float32).astype(jnp.bfloat16)

    queries, keys, values = project(0), project(1), project(2)
    q_ref[...] = queries
    k_ref[...] = keys
    v_ref[...] = values
    lane = lax.broadcasted_iota(jnp.int32, (1, PAIR), 1)
    first = lane < PAIR // 2
    for pair in range(model_width // PAIR):
        cols = slice(pair * PAIR, (pair + 1) * PAIR)
        kv = lax.dot_general(keys[:, cols], values[:, cols], (((0,), (0,)), ((), ())),
                             preferred_element_type=jnp.float32)
        half = PAIR // 2
        state_ref[0, pair] = jnp.where(first, kv[:half], kv[half:])


def inside_kernel(q_ref, k_ref, v_ref, earlier_ref, inside_ref):
    del earlier_ref
    first_inside_kernel(q_ref, k_ref, v_ref, inside_ref)


def first_inside_kernel(q_ref, k_ref, v_ref, inside_ref):
    tokens = q_ref.shape[0]
    part = tokens // 2
    lane = lax.broadcasted_iota(jnp.int32, (1, PAIR), 1)
    first = lane < PAIR // 2
    zero = jnp.zeros((), jnp.bfloat16)
    for pair in range(q_ref.shape[1] // PAIR):
        cols = slice(pair * PAIR, (pair + 1) * PAIR)
        for rows_at in (0, part):
            seen = rows_at + part
            q_rows = q_ref[rows_at : rows_at + part, cols]
            k_seen, v_seen = k_ref[0:seen, cols], v_ref[0:seen, cols]
            causal = (lax.broadcasted_iota(jnp.int32, (part, seen), 0) + rows_at
                      >= lax.broadcasted_iota(jnp.int32, (part, seen), 1))
            inside = None
            for use in (first, ~first):
                q_one = jnp.where(use, q_rows, zero)
                scores = lax.dot_general(q_one, k_seen, (((1,), (1,)), ((), ())),
                                         preferred_element_type=jnp.float32)
                scores = jnp.where(causal, scores, 0.0).astype(jnp.bfloat16)
                term = jnp.dot(scores, jnp.where(use, v_seen, zero), preferred_element_type=jnp.float32)
                inside = term if inside is None else inside + term
            inside_ref[rows_at : rows_at + part, cols] = inside


def out_kernel(q_ref, state_ref, inside_ref, emb_ref, hgain_ref, out_w_ref, out_ref, att_ref):
    model_width = out_ref.shape[1]
    lane = lax.broadcasted_iota(jnp.int32, (1, PAIR), 1)
    first = lane < PAIR // 2
    head_size = PAIR // 2
    for pair in range(model_width // PAIR):
        cols = slice(pair * PAIR, (pair + 1) * PAIR)
        packed = state_ref[0, pair]
        diag = jnp.concatenate([jnp.where(first, packed, 0.0), jnp.where(first, 0.0, packed)], axis=0)
        high = diag.astype(jnp.bfloat16)
        low = (diag - high.astype(jnp.float32)).astype(jnp.bfloat16)
        q_pair = q_ref[:, cols]
        carried = (jnp.dot(q_pair, high, preferred_element_type=jnp.float32)
                   + jnp.dot(q_pair, low, preferred_element_type=jnp.float32))
        combined = inside_ref[:, cols] + carried
        square = combined * combined
        sum_first = jnp.sum(jnp.where(first, square, 0.0), axis=-1, keepdims=True)
        sum_second = jnp.sum(jnp.where(first, 0.0, square), axis=-1, keepdims=True)
        scale = jnp.where(first, lax.rsqrt(sum_first / head_size + 1e-06),
                          lax.rsqrt(sum_second / head_size + 1e-06))
        att_ref[:, cols] = (combined * scale * hgain_ref[:, cols]).astype(jnp.bfloat16)
    out = emb_ref[...].astype(jnp.float32) + jnp.dot(att_ref[...], out_w_ref[...],
                                                     preferred_element_type=jnp.float32)
    out_ref[...] = out.astype(jnp.bfloat16)


def full(shape):
    return pl.BlockSpec(shape, lambda b: (0,) * len(shape))


def shards(ticks, conv_weight, norm_gain, qkv_weight, head_gain, out_weight, state_in):
    tick_count, feat = ticks.shape
    token_count = tick_count // STRIDE
    model_width = conv_weight.shape[1]
    head_count, head_size = state_in.shape[0], state_in.shape[1]
    pairs = model_width // PAIR
    blocks = token_count // BLK
    block_ticks = BLK * STRIDE

    prev = from_behind(ticks[tick_count - 2 * STRIDE :], "inner", 1)
    rows_spec = pl.BlockSpec((BLK, model_width), lambda b: (b, 0))
    state_spec = pl.BlockSpec((1, pairs, head_size, PAIR), lambda b: (b, 0, 0, 0))
    emb, queries, keys, values, states = pl.pallas_call(
        embed_kernel,
        grid=(blocks,),
        in_specs=[
            pl.BlockSpec((block_ticks, feat), lambda b: (b, 0)),
            full((2 * STRIDE, feat)),
            full(conv_weight.shape),
            full((1, model_width)),
            full(qkv_weight.shape),
        ],
        out_specs=[rows_spec, rows_spec, rows_spec, rows_spec, state_spec],
        out_shape=[jax.ShapeDtypeStruct((token_count, model_width), jnp.bfloat16)] * 4 + [
            jax.ShapeDtypeStruct((blocks, pairs, head_size, PAIR), jnp.float32),
        ],
        scratch_shapes=[pltpu.VMEM((block_ticks + STRIDE, feat), jnp.float32)],
        compiler_params=pltpu.CompilerParams(dimension_semantics=("arbitrary",)),
    )(ticks, prev, conv_weight, norm_gain.reshape(1, model_width), qkv_weight)

    halves = 2
    piece_width = model_width // halves

    def inside_block(piece, earlier, q, k, v):
        block, half = divmod(piece, halves)
        spec = pl.BlockSpec((BLK, piece_width), lambda p, block=block, half=half: (block, half + p))
        in_specs, operands, aliases = [spec, spec, spec], [q, k, v], {}
        kernel = inside_kernel
        if earlier is not None:
            in_specs.append(pl.BlockSpec(memory_space=pl.ANY))
            operands.append(earlier)
            aliases = {3: 0}
        else:
            kernel = first_inside_kernel
        return pl.pallas_call(
            kernel,
            grid=(1,),
            in_specs=in_specs,
            out_specs=spec,
            out_shape=jax.ShapeDtypeStruct((token_count, model_width), jnp.float32),
            input_output_aliases=aliases,
            cost_estimate=pl.CostEstimate(flops=8 * BLK * BLK * piece_width, transcendentals=0,
                                          bytes_accessed=10 * BLK * piece_width),
        )(*operands)

    local = states[0]
    for block in range(1, blocks):
        local = local + states[block]
    count = lax.axis_size("inner")
    inside = None
    total, steps, block = local, 1, 0
    while steps < count:
        if block < blocks * halves:
            total, q_in, k_in, v_in = lax.optimization_barrier((total, queries, keys, values))
        received = from_behind(total, "inner", steps)
        if block < blocks * halves:
            inside = inside_block(block, inside, q_in, k_in, v_in)
            received, inside = lax.optimization_barrier((received, inside))
            block += 1
        total = total + received
        steps *= 2
    while block < blocks * halves:
        inside = inside_block(block, inside, queries, keys, values)
        block += 1
    prefix = total - local
    packed_in = state_in.reshape(pairs, 2, head_size, head_size).transpose(0, 2, 1, 3)
    carried = packed_in.reshape(pairs, head_size, PAIR) + prefix
    before = [carried]
    for block in range(1, blocks):
        before.append(before[-1] + states[block - 1])
    before = jnp.stack(before)

    return pl.pallas_call(
        out_kernel,
        grid=(blocks,),
        in_specs=[
            rows_spec,
            state_spec,
            rows_spec,
            rows_spec,
            full((1, model_width)),
            full(out_weight.shape),
        ],
        out_specs=rows_spec,
        out_shape=jax.ShapeDtypeStruct((token_count, model_width), jnp.bfloat16),
        scratch_shapes=[pltpu.VMEM((BLK, model_width), jnp.bfloat16)],
        compiler_params=pltpu.CompilerParams(dimension_semantics=("arbitrary",)),
    )(queries, before, inside, emb, head_gain.reshape(1, model_width), out_weight)


def solution(mesh):
    in_specs = (P(("groups", "inner"), None), P(), P(), P(), P(), P(), P("groups", None, None))
    out_specs = P(("groups", "inner"), None)
    return jax.shard_map(shards, mesh=mesh, in_specs=in_specs, out_specs=out_specs, check_vma=False)
```

```python
import functools

import jax
import jax.numpy as jnp
from jax import lax
from jax.experimental import pallas as pl
from jax.experimental.pallas import tpu as pltpu
from jax.sharding import PartitionSpec as P

STRIDE = 8
BLK = 512
PAIR = 128


def from_behind(value, axis, steps):
    count = lax.axis_size(axis)
    initial, last = (max(0, -steps), min(count, count - steps))
    return lax.ppermute(value, axis, [(source, source + steps) for source in range(initial, last)])


def exclusive_scan(value, axis):
    count = lax.axis_size(axis)
    total = value
    steps = 1
    while steps < count:
        total = total + from_behind(total, axis, steps)
        steps *= 2
    return total - value


def embed_kernel(ticks_ref, prev_ref, conv_ref, gain_ref, qkv_w_ref,
                 emb_ref, q_ref, k_ref, v_ref, total_ref, first_ref, wide_ref):
    b = pl.program_id(0)
    block_ticks = ticks_ref.shape[0]
    tokens = block_ticks // STRIDE
    model_width = emb_ref.shape[1]

    @pl.when(b == 0)
    def _():
        wide_ref[0:STRIDE, :] = prev_ref[STRIDE : 2 * STRIDE, :].astype(jnp.float32)

    @pl.when(b > 0)
    def _():
        wide_ref[0:STRIDE, :] = wide_ref[block_ticks : block_ticks + STRIDE, :]

    wide_ref[STRIDE:, :] = ticks_ref[...].astype(jnp.float32)
    pieces = [wide_ref[pl.ds(j, tokens, stride=STRIDE), :] for j in range(2 * STRIDE)]
    lhs = jnp.concatenate(pieces, axis=1).astype(jnp.bfloat16)
    emb = jnp.dot(lhs, conv_ref[...], preferred_element_type=jnp.float32).astype(jnp.bfloat16)
    emb_ref[...] = emb
    embed_f = emb.astype(jnp.float32)
    mean_sq = jnp.mean(embed_f * embed_f, axis=-1, keepdims=True)
    normed = (embed_f * lax.rsqrt(mean_sq + 1e-05) * gain_ref[...]).astype(jnp.bfloat16)

    def project(part):
        weight = qkv_w_ref[:, part * model_width : (part + 1) * model_width]
        return jnp.dot(normed, weight, preferred_element_type=jnp.float32).astype(jnp.bfloat16)

    queries, keys, values = project(0), project(1), project(2)
    q_ref[...] = queries
    k_ref[...] = keys
    v_ref[...] = values
    lane = lax.broadcasted_iota(jnp.int32, (1, PAIR), 1)
    first = lane < PAIR // 2
    for pair in range(model_width // PAIR):
        cols = slice(pair * PAIR, (pair + 1) * PAIR)
        kv = lax.dot_general(keys[:, cols], values[:, cols], (((0,), (0,)), ((), ())),
                             preferred_element_type=jnp.float32)
        half = PAIR // 2
        packed = jnp.where(first, kv[:half], kv[half:])
        total_ref[pair] = jnp.where(b > 0, total_ref[pair], 0.0) + packed
        first_ref[pair] = jnp.where(b > 0, first_ref[pair], packed)


def inside_kernel(q_ref, k_ref, v_ref, earlier_ref, inside_ref):
    del earlier_ref
    first_inside_kernel(q_ref, k_ref, v_ref, inside_ref)


def first_inside_kernel(q_ref, k_ref, v_ref, inside_ref):
    tokens = q_ref.shape[0]
    part = tokens // 2
    lane = lax.broadcasted_iota(jnp.int32, (1, PAIR), 1)
    first = lane < PAIR // 2
    zero = jnp.zeros((), jnp.bfloat16)
    for pair in range(q_ref.shape[1] // PAIR):
        cols = slice(pair * PAIR, (pair + 1) * PAIR)
        for rows_at in (0, part):
            seen = rows_at + part
            q_rows = q_ref[rows_at : rows_at + part, cols]
            k_seen, v_seen = k_ref[0:seen, cols], v_ref[0:seen, cols]
            causal = (lax.broadcasted_iota(jnp.int32, (part, seen), 0) + rows_at
                      >= lax.broadcasted_iota(jnp.int32, (part, seen), 1))
            inside = None
            for use in (first, ~first):
                q_one = jnp.where(use, q_rows, zero)
                scores = lax.dot_general(q_one, k_seen, (((1,), (1,)), ((), ())),
                                         preferred_element_type=jnp.float32)
                scores = jnp.where(causal, scores, 0.0).astype(jnp.bfloat16)
                term = jnp.dot(scores, jnp.where(use, v_seen, zero), preferred_element_type=jnp.float32)
                inside = term if inside is None else inside + term
            inside_ref[rows_at : rows_at + part, cols] = inside


def out_kernel(q_ref, start_ref, total_ref, local_ref, first_ref, inside_ref, emb_ref, hgain_ref, out_w_ref,
               out_ref, att_ref):
    b = pl.program_id(0)
    model_width = out_ref.shape[1]
    lane = lax.broadcasted_iota(jnp.int32, (1, PAIR), 1)
    first = lane < PAIR // 2
    head_size = PAIR // 2
    for pair in range(model_width // PAIR):
        cols = slice(pair * PAIR, (pair + 1) * PAIR)
        packed = (start_ref[pair] + (total_ref[pair] - local_ref[pair])
                  + jnp.where(b > 0, first_ref[pair], 0.0))
        diag = jnp.concatenate([jnp.where(first, packed, 0.0), jnp.where(first, 0.0, packed)], axis=0)
        high = diag.astype(jnp.bfloat16)
        low = (diag - high.astype(jnp.float32)).astype(jnp.bfloat16)
        q_pair = q_ref[:, cols]
        carried = (jnp.dot(q_pair, high, preferred_element_type=jnp.float32)
                   + jnp.dot(q_pair, low, preferred_element_type=jnp.float32))
        combined = inside_ref[:, cols] + carried
        square = combined * combined
        sum_first = jnp.sum(jnp.where(first, square, 0.0), axis=-1, keepdims=True)
        sum_second = jnp.sum(jnp.where(first, 0.0, square), axis=-1, keepdims=True)
        scale = jnp.where(first, lax.rsqrt(sum_first / head_size + 1e-06),
                          lax.rsqrt(sum_second / head_size + 1e-06))
        att_ref[:, cols] = (combined * scale * hgain_ref[:, cols]).astype(jnp.bfloat16)
    out = emb_ref[...].astype(jnp.float32) + jnp.dot(att_ref[...], out_w_ref[...],
                                                     preferred_element_type=jnp.float32)
    out_ref[...] = out.astype(jnp.bfloat16)


def full(shape):
    return pl.BlockSpec(shape, lambda b: (0,) * len(shape))


def shards(ticks, conv_weight, norm_gain, qkv_weight, head_gain, out_weight, state_in):
    tick_count, feat = ticks.shape
    token_count = tick_count // STRIDE
    model_width = conv_weight.shape[1]
    head_count, head_size = state_in.shape[0], state_in.shape[1]
    pairs = model_width // PAIR
    blocks = token_count // BLK
    block_ticks = BLK * STRIDE

    prev = from_behind(ticks[tick_count - 2 * STRIDE :], "inner", 1)
    rows_spec = pl.BlockSpec((BLK, model_width), lambda b: (b, 0))
    state_spec = full((pairs, head_size, PAIR))
    emb, queries, keys, values, local, first_state = pl.pallas_call(
        embed_kernel,
        grid=(blocks,),
        in_specs=[
            pl.BlockSpec((block_ticks, feat), lambda b: (b, 0)),
            full((2 * STRIDE, feat)),
            full(conv_weight.shape),
            full((1, model_width)),
            full(qkv_weight.shape),
        ],
        out_specs=[rows_spec, rows_spec, rows_spec, rows_spec, state_spec, state_spec],
        out_shape=[jax.ShapeDtypeStruct((token_count, model_width), jnp.bfloat16)] * 4 + [
            jax.ShapeDtypeStruct((pairs, head_size, PAIR), jnp.float32),
        ] * 2,
        scratch_shapes=[pltpu.VMEM((block_ticks + STRIDE, feat), jnp.float32)],
        compiler_params=pltpu.CompilerParams(dimension_semantics=("arbitrary",)),
    )(ticks, prev, conv_weight, norm_gain.reshape(1, model_width), qkv_weight)

    halves = 2
    piece_width = model_width // halves

    def inside_block(piece, earlier, q, k, v):
        block, half = divmod(piece, halves)
        spec = pl.BlockSpec((BLK, piece_width), lambda p, block=block, half=half: (block, half + p))
        in_specs, operands, aliases = [spec, spec, spec], [q, k, v], {}
        kernel = inside_kernel
        if earlier is not None:
            in_specs.append(pl.BlockSpec(memory_space=pl.ANY))
            operands.append(earlier)
            aliases = {3: 0}
        else:
            kernel = first_inside_kernel
        return pl.pallas_call(
            kernel,
            grid=(1,),
            in_specs=in_specs,
            out_specs=spec,
            out_shape=jax.ShapeDtypeStruct((token_count, model_width), jnp.float32),
            input_output_aliases=aliases,
            cost_estimate=pl.CostEstimate(flops=8 * BLK * BLK * piece_width, transcendentals=0,
                                          bytes_accessed=10 * BLK * piece_width),
        )(*operands)

    count = lax.axis_size("inner")
    inside = None
    total, steps, block = local, 1, 0
    while steps < count:
        if block < blocks * halves:
            total, q_in, k_in, v_in = lax.optimization_barrier((total, queries, keys, values))
        received = from_behind(total, "inner", steps)
        if block < blocks * halves:
            inside = inside_block(block, inside, q_in, k_in, v_in)
            received, inside = lax.optimization_barrier((received, inside))
            block += 1
        total = total + received
        steps *= 2
    while block < blocks * halves:
        inside = inside_block(block, inside, queries, keys, values)
        block += 1
    packed_in = state_in.reshape(pairs, 2, head_size, head_size).transpose(0, 2, 1, 3)
    packed_in = packed_in.reshape(pairs, head_size, PAIR)

    return pl.pallas_call(
        out_kernel,
        grid=(blocks,),
        in_specs=[
            rows_spec,
            state_spec,
            state_spec,
            state_spec,
            state_spec,
            rows_spec,
            rows_spec,
            full((1, model_width)),
            full(out_weight.shape),
        ],
        out_specs=rows_spec,
        out_shape=jax.ShapeDtypeStruct((token_count, model_width), jnp.bfloat16),
        scratch_shapes=[pltpu.VMEM((BLK, model_width), jnp.bfloat16)],
        compiler_params=pltpu.CompilerParams(dimension_semantics=("arbitrary",)),
    )(queries, packed_in, total, local, first_state, inside, emb, head_gain.reshape(1, model_width), out_weight)


def solution(mesh):
    in_specs = (P(("groups", "inner"), None), P(), P(), P(), P(), P(), P("groups", None, None))
    out_specs = P(("groups", "inner"), None)
    return jax.shard_map(shards, mesh=mesh, in_specs=in_specs, out_specs=out_specs, check_vma=False)
```

```python
import functools

import jax
import jax.numpy as jnp
from jax import lax
from jax.experimental import pallas as pl
from jax.experimental.pallas import tpu as pltpu
from jax.sharding import PartitionSpec as P

STRIDE = 8
BLK = 512
PAIR = 128


def from_behind(value, axis, steps):
    count = lax.axis_size(axis)
    initial, last = (max(0, -steps), min(count, count - steps))
    return lax.ppermute(value, axis, [(source, source + steps) for source in range(initial, last)])


def exclusive_scan(value, axis):
    count = lax.axis_size(axis)
    total = value
    steps = 1
    while steps < count:
        total = total + from_behind(total, axis, steps)
        steps *= 2
    return total - value


def embed_kernel(ticks_ref, prev_ref, conv_ref, gain_ref, qkv_w_ref,
                 emb_ref, q_ref, k_ref, v_ref, total_ref, first_ref, wide_ref):
    b = pl.program_id(0)
    block_ticks = ticks_ref.shape[0]
    tokens = block_ticks // STRIDE
    model_width = emb_ref.shape[1]

    @pl.when(b == 0)
    def _():
        wide_ref[0:STRIDE, :] = prev_ref[STRIDE : 2 * STRIDE, :].astype(jnp.float32)

    @pl.when(b > 0)
    def _():
        wide_ref[0:STRIDE, :] = wide_ref[block_ticks : block_ticks + STRIDE, :]

    wide_ref[STRIDE:, :] = ticks_ref[...].astype(jnp.float32)
    pieces = [wide_ref[pl.ds(j, tokens, stride=STRIDE), :] for j in range(2 * STRIDE)]
    lhs = jnp.concatenate(pieces, axis=1).astype(jnp.bfloat16)
    emb = jnp.dot(lhs, conv_ref[...], preferred_element_type=jnp.float32).astype(jnp.bfloat16)
    emb_ref[...] = emb
    embed_f = emb.astype(jnp.float32)
    mean_sq = jnp.mean(embed_f * embed_f, axis=-1, keepdims=True)
    normed = (embed_f * lax.rsqrt(mean_sq + 1e-05) * gain_ref[...][None, :]).astype(jnp.bfloat16)

    def project(part):
        weight = qkv_w_ref[:, part * model_width : (part + 1) * model_width]
        return jnp.dot(normed, weight, preferred_element_type=jnp.float32).astype(jnp.bfloat16)

    queries, keys, values = project(0), project(1), project(2)
    q_ref[...] = queries
    k_ref[...] = keys
    v_ref[...] = values
    lane = lax.broadcasted_iota(jnp.int32, (1, PAIR), 1)
    first = lane < PAIR // 2
    for pair in range(model_width // PAIR):
        cols = slice(pair * PAIR, (pair + 1) * PAIR)
        kv = lax.dot_general(keys[:, cols], values[:, cols], (((0,), (0,)), ((), ())),
                             preferred_element_type=jnp.float32)
        half = PAIR // 2
        packed = jnp.where(first, kv[:half], kv[half:])
        total_ref[pair] = jnp.where(b > 0, total_ref[pair], 0.0) + packed
        first_ref[pair] = jnp.where(b > 0, first_ref[pair], packed)


def inside_kernel(q_ref, k_ref, v_ref, earlier_ref, inside_ref):
    del earlier_ref
    first_inside_kernel(q_ref, k_ref, v_ref, inside_ref)


def first_inside_kernel(q_ref, k_ref, v_ref, inside_ref):
    tokens = q_ref.shape[0]
    part = tokens // 2
    lane = lax.broadcasted_iota(jnp.int32, (1, PAIR), 1)
    first = lane < PAIR // 2
    zero = jnp.zeros((), jnp.bfloat16)
    for pair in range(q_ref.shape[1] // PAIR):
        cols = slice(pair * PAIR, (pair + 1) * PAIR)
        for rows_at in (0, part):
            seen = rows_at + part
            q_rows = q_ref[rows_at : rows_at + part, cols]
            k_seen, v_seen = k_ref[0:seen, cols], v_ref[0:seen, cols]
            causal = (lax.broadcasted_iota(jnp.int32, (part, seen), 0) + rows_at
                      >= lax.broadcasted_iota(jnp.int32, (part, seen), 1))
            inside = None
            for use in (first, ~first):
                q_one = jnp.where(use, q_rows, zero)
                scores = lax.dot_general(q_one, k_seen, (((1,), (1,)), ((), ())),
                                         preferred_element_type=jnp.float32)
                scores = jnp.where(causal, scores, 0.0).astype(jnp.bfloat16)
                term = jnp.dot(scores, jnp.where(use, v_seen, zero), preferred_element_type=jnp.float32)
                inside = term if inside is None else inside + term
            inside_ref[rows_at : rows_at + part, cols] = inside


def out_kernel(q_ref, start_ref, total_ref, received_ref, local_ref, first_ref, inside_ref, emb_ref, hgain_ref, out_w_ref,
               out_ref, att_ref):
    b = pl.program_id(0)
    model_width = out_ref.shape[1]
    lane = lax.broadcasted_iota(jnp.int32, (1, PAIR), 1)
    first = lane < PAIR // 2
    head_size = PAIR // 2
    for pair in range(model_width // PAIR):
        cols = slice(pair * PAIR, (pair + 1) * PAIR)
        packed = (start_ref[pair] + (total_ref[pair] + received_ref[pair] - local_ref[pair])
                  + jnp.where(b > 0, first_ref[pair], 0.0))
        diag = jnp.concatenate([jnp.where(first, packed, 0.0), jnp.where(first, 0.0, packed)], axis=0)
        high = diag.astype(jnp.bfloat16)
        low = (diag - high.astype(jnp.float32)).astype(jnp.bfloat16)
        q_pair = q_ref[:, cols]
        carried = (jnp.dot(q_pair, high, preferred_element_type=jnp.float32)
                   + jnp.dot(q_pair, low, preferred_element_type=jnp.float32))
        combined = inside_ref[:, cols] + carried
        square = combined * combined
        sum_first = jnp.sum(jnp.where(first, square, 0.0), axis=-1, keepdims=True)
        sum_second = jnp.sum(jnp.where(first, 0.0, square), axis=-1, keepdims=True)
        scale = jnp.where(first, lax.rsqrt(sum_first / head_size + 1e-06),
                          lax.rsqrt(sum_second / head_size + 1e-06))
        att_ref[:, cols] = (combined * scale * hgain_ref[:, cols]).astype(jnp.bfloat16)
    out = emb_ref[...].astype(jnp.float32) + jnp.dot(att_ref[...], out_w_ref[...],
                                                     preferred_element_type=jnp.float32)
    out_ref[...] = out.astype(jnp.bfloat16)


def full(shape):
    return pl.BlockSpec(shape, lambda b: (0,) * len(shape))


def shards(ticks, conv_weight, norm_gain, qkv_weight, head_gain, out_weight, state_in):
    tick_count, feat = ticks.shape
    token_count = tick_count // STRIDE
    model_width = conv_weight.shape[1]
    head_count, head_size = state_in.shape[0], state_in.shape[1]
    pairs = model_width // PAIR
    blocks = token_count // BLK
    block_ticks = BLK * STRIDE

    prev = from_behind(ticks[tick_count - 2 * STRIDE :], "inner", 1)
    rows_spec = pl.BlockSpec((BLK, model_width), lambda b: (b, 0))
    state_spec = full((pairs, head_size, PAIR))
    emb, queries, keys, values, local, first_state = pl.pallas_call(
        embed_kernel,
        grid=(blocks,),
        in_specs=[
            pl.BlockSpec((block_ticks, feat), lambda b: (b, 0)),
            full((2 * STRIDE, feat)),
            full(conv_weight.shape),
            full((model_width,)),
            full(qkv_weight.shape),
        ],
        out_specs=[rows_spec, rows_spec, rows_spec, rows_spec, state_spec, state_spec],
        out_shape=[jax.ShapeDtypeStruct((token_count, model_width), jnp.bfloat16)] * 4 + [
            jax.ShapeDtypeStruct((pairs, head_size, PAIR), jnp.float32),
        ] * 2,
        scratch_shapes=[pltpu.VMEM((block_ticks + STRIDE, feat), jnp.float32)],
        compiler_params=pltpu.CompilerParams(dimension_semantics=("arbitrary",)),
    )(ticks, prev, conv_weight, norm_gain, qkv_weight)

    halves = 2
    piece_width = model_width // halves

    def inside_block(piece, earlier, q, k, v):
        block, half = divmod(piece, halves)
        spec = pl.BlockSpec((BLK, piece_width), lambda p, block=block, half=half: (block, half + p))
        in_specs, operands, aliases = [spec, spec, spec], [q, k, v], {}
        kernel = inside_kernel
        if earlier is not None:
            in_specs.append(pl.BlockSpec(memory_space=pl.ANY))
            operands.append(earlier)
            aliases = {3: 0}
        else:
            kernel = first_inside_kernel
        return pl.pallas_call(
            kernel,
            grid=(1,),
            in_specs=in_specs,
            out_specs=spec,
            out_shape=jax.ShapeDtypeStruct((token_count, model_width), jnp.float32),
            input_output_aliases=aliases,
            cost_estimate=pl.CostEstimate(flops=8 * BLK * BLK * piece_width, transcendentals=0,
                                          bytes_accessed=10 * BLK * piece_width),
        )(*operands)

    count = lax.axis_size("inner")
    inside = None
    total, steps, block = local, 1, 0
    received = jnp.zeros_like(local)
    while steps < count:
        if block < blocks * halves:
            total, q_in, k_in, v_in = lax.optimization_barrier((total, queries, keys, values))
        received = from_behind(total, "inner", steps)
        if block < blocks * halves:
            inside = inside_block(block, inside, q_in, k_in, v_in)
            received, inside = lax.optimization_barrier((received, inside))
            block += 1
        steps *= 2
        if steps >= count:
            break
        total = total + received
    while block < blocks * halves:
        inside = inside_block(block, inside, queries, keys, values)
        block += 1
    packed_in = state_in.reshape(pairs, 2, head_size, head_size).transpose(0, 2, 1, 3)
    packed_in = packed_in.reshape(pairs, head_size, PAIR)

    return pl.pallas_call(
        out_kernel,
        grid=(blocks,),
        in_specs=[
            rows_spec,
            state_spec,
            state_spec,
            state_spec,
            state_spec,
            state_spec,
            rows_spec,
            rows_spec,
            full((1, model_width)),
            full(out_weight.shape),
        ],
        out_specs=rows_spec,
        out_shape=jax.ShapeDtypeStruct((token_count, model_width), jnp.bfloat16),
        scratch_shapes=[pltpu.VMEM((BLK, model_width), jnp.bfloat16)],
        compiler_params=pltpu.CompilerParams(dimension_semantics=("arbitrary",)),
    )(queries, packed_in, total, received, local, first_state, inside, emb, head_gain.reshape(1, model_width), out_weight)


def solution(mesh):
    in_specs = (P(("groups", "inner"), None), P(), P(), P(), P(), P(), P("groups", None, None))
    out_specs = P(("groups", "inner"), None)
    return jax.shard_map(shards, mesh=mesh, in_specs=in_specs, out_specs=out_specs, check_vma=False)
```

```python
import functools

import jax
import jax.numpy as jnp
from jax import lax
from jax.experimental import pallas as pl
from jax.experimental.pallas import tpu as pltpu
from jax.sharding import PartitionSpec as P

STRIDE = 8
BLK = 512
PAIR = 128


def from_behind(value, axis, steps):
    count = lax.axis_size(axis)
    initial, last = (max(0, -steps), min(count, count - steps))
    return lax.ppermute(value, axis, [(source, source + steps) for source in range(initial, last)])


def exclusive_scan(value, axis):
    count = lax.axis_size(axis)
    total = value
    steps = 1
    while steps < count:
        total = total + from_behind(total, axis, steps)
        steps *= 2
    return total - value


def embed_kernel(ticks_ref, prev_ref, conv_ref, gain_ref, qkv_hbm,
                 emb_ref, q_ref, k_ref, v_ref, total_ref, first_ref, wide_ref, qkv_w_ref, copy_sem):
    b = pl.program_id(0)
    block_ticks = ticks_ref.shape[0]
    tokens = block_ticks // STRIDE
    model_width = emb_ref.shape[1]

    weight_copy = pltpu.make_async_copy(qkv_hbm, qkv_w_ref, copy_sem)

    @pl.when(b == 0)
    def _():
        weight_copy.start()
        wide_ref[0:STRIDE, :] = prev_ref[STRIDE : 2 * STRIDE, :].astype(jnp.float32)

    @pl.when(b > 0)
    def _():
        wide_ref[0:STRIDE, :] = wide_ref[block_ticks : block_ticks + STRIDE, :]

    wide_ref[STRIDE:, :] = ticks_ref[...].astype(jnp.float32)
    pieces = [wide_ref[pl.ds(j, tokens, stride=STRIDE), :] for j in range(2 * STRIDE)]
    lhs = jnp.concatenate(pieces, axis=1).astype(jnp.bfloat16)
    emb = jnp.dot(lhs, conv_ref[...], preferred_element_type=jnp.float32).astype(jnp.bfloat16)
    emb_ref[...] = emb
    embed_f = emb.astype(jnp.float32)
    mean_sq = jnp.mean(embed_f * embed_f, axis=-1, keepdims=True)
    normed = (embed_f * lax.rsqrt(mean_sq + 1e-05) * gain_ref[...][None, :]).astype(jnp.bfloat16)

    @pl.when(b == 0)
    def _():
        weight_copy.wait()

    def project(part):
        weight = qkv_w_ref[:, part * model_width : (part + 1) * model_width]
        return jnp.dot(normed, weight, preferred_element_type=jnp.float32).astype(jnp.bfloat16)

    queries, keys, values = project(0), project(1), project(2)
    q_ref[...] = queries
    k_ref[...] = keys
    v_ref[...] = values
    lane = lax.broadcasted_iota(jnp.int32, (1, PAIR), 1)
    first = lane < PAIR // 2
    for pair in range(model_width // PAIR):
        cols = slice(pair * PAIR, (pair + 1) * PAIR)
        kv = lax.dot_general(keys[:, cols], values[:, cols], (((0,), (0,)), ((), ())),
                             preferred_element_type=jnp.float32)
        half = PAIR // 2
        packed = jnp.where(first, kv[:half], kv[half:])
        total_ref[pair] = jnp.where(b > 0, total_ref[pair], 0.0) + packed
        first_ref[pair] = jnp.where(b > 0, first_ref[pair], packed)


def inside_kernel(q_ref, k_ref, v_ref, earlier_ref, inside_ref):
    del earlier_ref
    first_inside_kernel(q_ref, k_ref, v_ref, inside_ref)


def first_inside_kernel(q_ref, k_ref, v_ref, inside_ref):
    tokens = q_ref.shape[0]
    part = tokens // 2
    lane = lax.broadcasted_iota(jnp.int32, (1, PAIR), 1)
    first = lane < PAIR // 2
    zero = jnp.zeros((), jnp.bfloat16)
    for pair in range(q_ref.shape[1] // PAIR):
        cols = slice(pair * PAIR, (pair + 1) * PAIR)
        for rows_at in (0, part):
            seen = rows_at + part
            q_rows = q_ref[rows_at : rows_at + part, cols]
            k_seen, v_seen = k_ref[0:seen, cols], v_ref[0:seen, cols]
            causal = (lax.broadcasted_iota(jnp.int32, (part, seen), 0) + rows_at
                      >= lax.broadcasted_iota(jnp.int32, (part, seen), 1))
            inside = None
            for use in (first, ~first):
                q_one = jnp.where(use, q_rows, zero)
                scores = lax.dot_general(q_one, k_seen, (((1,), (1,)), ((), ())),
                                         preferred_element_type=jnp.float32)
                scores = jnp.where(causal, scores, 0.0).astype(jnp.bfloat16)
                term = jnp.dot(scores, jnp.where(use, v_seen, zero), preferred_element_type=jnp.float32)
                inside = term if inside is None else inside + term
            inside_ref[rows_at : rows_at + part, cols] = inside


def out_kernel(q_ref, start_ref, total_ref, received_ref, local_ref, first_ref, inside_ref, emb_ref, hgain_ref, out_hbm,
               out_ref, att_ref, out_w_ref, copy_sem):
    b = pl.program_id(0)
    weight_copy = pltpu.make_async_copy(out_hbm, out_w_ref, copy_sem)

    @pl.when(b == 0)
    def _():
        weight_copy.start()

    model_width = out_ref.shape[1]
    lane = lax.broadcasted_iota(jnp.int32, (1, PAIR), 1)
    first = lane < PAIR // 2
    head_size = PAIR // 2
    for pair in range(model_width // PAIR):
        cols = slice(pair * PAIR, (pair + 1) * PAIR)
        packed = (start_ref[pair] + (total_ref[pair] + received_ref[pair] - local_ref[pair])
                  + jnp.where(b > 0, first_ref[pair], 0.0))
        diag = jnp.concatenate([jnp.where(first, packed, 0.0), jnp.where(first, 0.0, packed)], axis=0)
        high = diag.astype(jnp.bfloat16)
        low = (diag - high.astype(jnp.float32)).astype(jnp.bfloat16)
        q_pair = q_ref[:, cols]
        carried = (jnp.dot(q_pair, high, preferred_element_type=jnp.float32)
                   + jnp.dot(q_pair, low, preferred_element_type=jnp.float32))
        combined = inside_ref[:, cols] + carried
        square = combined * combined
        sum_first = jnp.sum(jnp.where(first, square, 0.0), axis=-1, keepdims=True)
        sum_second = jnp.sum(jnp.where(first, 0.0, square), axis=-1, keepdims=True)
        scale = jnp.where(first, lax.rsqrt(sum_first / head_size + 1e-06),
                          lax.rsqrt(sum_second / head_size + 1e-06))
        att_ref[:, cols] = (combined * scale * hgain_ref[:, cols]).astype(jnp.bfloat16)

    @pl.when(b == 0)
    def _():
        weight_copy.wait()

    out = emb_ref[...].astype(jnp.float32) + jnp.dot(att_ref[...], out_w_ref[...],
                                                     preferred_element_type=jnp.float32)
    out_ref[...] = out.astype(jnp.bfloat16)


def full(shape):
    return pl.BlockSpec(shape, lambda b: (0,) * len(shape))


def shards(ticks, conv_weight, norm_gain, qkv_weight, head_gain, out_weight, state_in):
    tick_count, feat = ticks.shape
    token_count = tick_count // STRIDE
    model_width = conv_weight.shape[1]
    head_count, head_size = state_in.shape[0], state_in.shape[1]
    pairs = model_width // PAIR
    blocks = token_count // BLK
    block_ticks = BLK * STRIDE

    prev = from_behind(ticks[tick_count - 2 * STRIDE :], "inner", 1)
    rows_spec = pl.BlockSpec((BLK, model_width), lambda b: (b, 0))
    state_spec = full((pairs, head_size, PAIR))
    emb, queries, keys, values, local, first_state = pl.pallas_call(
        embed_kernel,
        grid=(blocks,),
        in_specs=[
            pl.BlockSpec((block_ticks, feat), lambda b: (b, 0)),
            full((2 * STRIDE, feat)),
            full(conv_weight.shape),
            full((model_width,)),
            pl.BlockSpec(memory_space=pl.ANY),
        ],
        out_specs=[rows_spec, rows_spec, rows_spec, rows_spec, state_spec, state_spec],
        out_shape=[jax.ShapeDtypeStruct((token_count, model_width), jnp.bfloat16)] * 4 + [
            jax.ShapeDtypeStruct((pairs, head_size, PAIR), jnp.float32),
        ] * 2,
        scratch_shapes=[pltpu.VMEM((block_ticks + STRIDE, feat), jnp.float32),
                        pltpu.VMEM(qkv_weight.shape, qkv_weight.dtype),
                        pltpu.SemaphoreType.DMA(())],
        compiler_params=pltpu.CompilerParams(dimension_semantics=("arbitrary",)),
    )(ticks, prev, conv_weight, norm_gain, qkv_weight)

    halves = 2
    piece_width = model_width // halves

    def inside_block(piece, earlier, q, k, v):
        block, half = divmod(piece, halves)
        spec = pl.BlockSpec((BLK, piece_width), lambda p, block=block, half=half: (block, half + p))
        in_specs, operands, aliases = [spec, spec, spec], [q, k, v], {}
        kernel = inside_kernel
        if earlier is not None:
            in_specs.append(pl.BlockSpec(memory_space=pl.ANY))
            operands.append(earlier)
            aliases = {3: 0}
        else:
            kernel = first_inside_kernel
        return pl.pallas_call(
            kernel,
            grid=(1,),
            in_specs=in_specs,
            out_specs=spec,
            out_shape=jax.ShapeDtypeStruct((token_count, model_width), jnp.float32),
            input_output_aliases=aliases,
            cost_estimate=pl.CostEstimate(flops=8 * BLK * BLK * piece_width, transcendentals=0,
                                          bytes_accessed=10 * BLK * piece_width),
        )(*operands)

    count = lax.axis_size("inner")
    inside = None
    total, steps, block = local, 1, 0
    received = jnp.zeros_like(local)
    while steps < count:
        if block < blocks * halves:
            total, q_in, k_in, v_in = lax.optimization_barrier((total, queries, keys, values))
        received = from_behind(total, "inner", steps)
        if block < blocks * halves:
            inside = inside_block(block, inside, q_in, k_in, v_in)
            received, inside = lax.optimization_barrier((received, inside))
            block += 1
        steps *= 2
        if steps >= count:
            break
        total = total + received
    while block < blocks * halves:
        inside = inside_block(block, inside, queries, keys, values)
        block += 1
    packed_in = state_in.reshape(pairs, 2, head_size, head_size).transpose(0, 2, 1, 3)
    packed_in = packed_in.reshape(pairs, head_size, PAIR)

    return pl.pallas_call(
        out_kernel,
        grid=(blocks,),
        in_specs=[
            rows_spec,
            state_spec,
            state_spec,
            state_spec,
            state_spec,
            state_spec,
            rows_spec,
            rows_spec,
            full((1, model_width)),
            pl.BlockSpec(memory_space=pl.ANY),
        ],
        out_specs=rows_spec,
        out_shape=jax.ShapeDtypeStruct((token_count, model_width), jnp.bfloat16),
        scratch_shapes=[pltpu.VMEM((BLK, model_width), jnp.bfloat16),
                        pltpu.VMEM(out_weight.shape, out_weight.dtype),
                        pltpu.SemaphoreType.DMA(())],
        compiler_params=pltpu.CompilerParams(dimension_semantics=("arbitrary",)),
    )(queries, packed_in, total, received, local, first_state, inside, emb, head_gain.reshape(1, model_width), out_weight)


def solution(mesh):
    in_specs = (P(("groups", "inner"), None), P(), P(), P(), P(), P(), P("groups", None, None))
    out_specs = P(("groups", "inner"), None)
    return jax.shard_map(shards, mesh=mesh, in_specs=in_specs, out_specs=out_specs, check_vma=False)
```

```python
import functools

import jax
import jax.numpy as jnp
from jax import lax
from jax.experimental import pallas as pl
from jax.experimental.pallas import tpu as pltpu
from jax.sharding import PartitionSpec as P

STRIDE = 8
BLK = 512
PAIR = 128


def from_behind(value, axis, steps):
    count = lax.axis_size(axis)
    initial, last = (max(0, -steps), min(count, count - steps))
    return lax.ppermute(value, axis, [(source, source + steps) for source in range(initial, last)])


def exclusive_scan(value, axis):
    count = lax.axis_size(axis)
    total = value
    steps = 1
    while steps < count:
        total = total + from_behind(total, axis, steps)
        steps *= 2
    return total - value


def embed_kernel(ticks_ref, prev_ref, conv_hbm, gain_ref, qkv_hbm,
                 emb_ref, q_ref, k_ref, v_ref, total_ref, first_ref, wide_ref, qkv_w_ref, copy_sem,
                 conv_ref, conv_sems):
    b = pl.program_id(0)
    block_ticks = ticks_ref.shape[0]
    tokens = block_ticks // STRIDE
    model_width = emb_ref.shape[1]

    weight_copy = pltpu.make_async_copy(qkv_hbm, qkv_w_ref, copy_sem)
    width = conv_hbm.shape[0] // 2
    conv_copies = [pltpu.make_async_copy(conv_hbm.at[pl.ds(part * width, width)],
                                         conv_ref.at[pl.ds(part * width, width)], conv_sems.at[part])
                   for part in range(2)]

    @pl.when(b == 0)
    def _():
        for copy in conv_copies:
            copy.start()
        weight_copy.start()
        wide_ref[0:STRIDE, :] = prev_ref[STRIDE : 2 * STRIDE, :].astype(jnp.float32)

    @pl.when(b > 0)
    def _():
        wide_ref[0:STRIDE, :] = wide_ref[block_ticks : block_ticks + STRIDE, :]

    wide_ref[STRIDE:, :] = ticks_ref[...].astype(jnp.float32)
    pieces = [wide_ref[pl.ds(j, tokens, stride=STRIDE), :] for j in range(2 * STRIDE)]
    lhs = jnp.concatenate(pieces, axis=1).astype(jnp.bfloat16)

    @pl.when(b == 0)
    def _():
        conv_copies[0].wait()

    emb_f = jnp.dot(lhs[:, :width], conv_ref[:width, :], preferred_element_type=jnp.float32)

    @pl.when(b == 0)
    def _():
        conv_copies[1].wait()

    emb_f = emb_f + jnp.dot(lhs[:, width:], conv_ref[width:, :], preferred_element_type=jnp.float32)
    emb = emb_f.astype(jnp.bfloat16)
    emb_ref[...] = emb
    embed_f = emb.astype(jnp.float32)
    mean_sq = jnp.mean(embed_f * embed_f, axis=-1, keepdims=True)
    normed = (embed_f * lax.rsqrt(mean_sq + 1e-05) * gain_ref[...][None, :]).astype(jnp.bfloat16)

    @pl.when(b == 0)
    def _():
        weight_copy.wait()

    def project(part):
        weight = qkv_w_ref[:, part * model_width : (part + 1) * model_width]
        return jnp.dot(normed, weight, preferred_element_type=jnp.float32).astype(jnp.bfloat16)

    queries, keys, values = project(0), project(1), project(2)
    q_ref[...] = queries
    k_ref[...] = keys
    v_ref[...] = values
    lane = lax.broadcasted_iota(jnp.int32, (1, PAIR), 1)
    first = lane < PAIR // 2
    for pair in range(model_width // PAIR):
        cols = slice(pair * PAIR, (pair + 1) * PAIR)
        kv = lax.dot_general(keys[:, cols], values[:, cols], (((0,), (0,)), ((), ())),
                             preferred_element_type=jnp.float32)
        half = PAIR // 2
        packed = jnp.where(first, kv[:half], kv[half:])
        total_ref[pair] = jnp.where(b > 0, total_ref[pair], 0.0) + packed
        first_ref[pair] = jnp.where(b > 0, first_ref[pair], packed)


def inside_kernel(q_ref, k_ref, v_ref, earlier_ref, inside_ref):
    del earlier_ref
    first_inside_kernel(q_ref, k_ref, v_ref, inside_ref)


def first_inside_kernel(q_ref, k_ref, v_ref, inside_ref):
    tokens = q_ref.shape[0]
    part = tokens // 2
    lane = lax.broadcasted_iota(jnp.int32, (1, PAIR), 1)
    first = lane < PAIR // 2
    zero = jnp.zeros((), jnp.bfloat16)
    for pair in range(q_ref.shape[1] // PAIR):
        cols = slice(pair * PAIR, (pair + 1) * PAIR)
        for rows_at in (0, part):
            seen = rows_at + part
            q_rows = q_ref[rows_at : rows_at + part, cols]
            k_seen, v_seen = k_ref[0:seen, cols], v_ref[0:seen, cols]
            causal = (lax.broadcasted_iota(jnp.int32, (part, seen), 0) + rows_at
                      >= lax.broadcasted_iota(jnp.int32, (part, seen), 1))
            inside = None
            for use in (first, ~first):
                q_one = jnp.where(use, q_rows, zero)
                scores = lax.dot_general(q_one, k_seen, (((1,), (1,)), ((), ())),
                                         preferred_element_type=jnp.float32)
                scores = jnp.where(causal, scores, 0.0).astype(jnp.bfloat16)
                term = jnp.dot(scores, jnp.where(use, v_seen, zero), preferred_element_type=jnp.float32)
                inside = term if inside is None else inside + term
            inside_ref[rows_at : rows_at + part, cols] = inside


def out_kernel(q_ref, start_ref, total_ref, received_ref, local_ref, first_ref, inside_ref, emb_ref, hgain_ref, out_w_ref,
               out_ref, att_ref):
    b = pl.program_id(0)
    model_width = out_ref.shape[1]
    lane = lax.broadcasted_iota(jnp.int32, (1, PAIR), 1)
    first = lane < PAIR // 2
    head_size = PAIR // 2
    for pair in range(model_width // PAIR):
        cols = slice(pair * PAIR, (pair + 1) * PAIR)
        packed = (start_ref[pair] + (total_ref[pair] + received_ref[pair] - local_ref[pair])
                  + jnp.where(b > 0, first_ref[pair], 0.0))
        diag = jnp.concatenate([jnp.where(first, packed, 0.0), jnp.where(first, 0.0, packed)], axis=0)
        high = diag.astype(jnp.bfloat16)
        low = (diag - high.astype(jnp.float32)).astype(jnp.bfloat16)
        q_pair = q_ref[:, cols]
        carried = (jnp.dot(q_pair, high, preferred_element_type=jnp.float32)
                   + jnp.dot(q_pair, low, preferred_element_type=jnp.float32))
        combined = inside_ref[:, cols] + carried
        square = combined * combined
        sum_first = jnp.sum(jnp.where(first, square, 0.0), axis=-1, keepdims=True)
        sum_second = jnp.sum(jnp.where(first, 0.0, square), axis=-1, keepdims=True)
        scale = jnp.where(first, lax.rsqrt(sum_first / head_size + 1e-06),
                          lax.rsqrt(sum_second / head_size + 1e-06))
        att_ref[:, cols] = (combined * scale * hgain_ref[:, cols]).astype(jnp.bfloat16)
    out = emb_ref[...].astype(jnp.float32) + jnp.dot(att_ref[...], out_w_ref[...],
                                                     preferred_element_type=jnp.float32)
    out_ref[...] = out.astype(jnp.bfloat16)


def full(shape):
    return pl.BlockSpec(shape, lambda b: (0,) * len(shape))


def shards(ticks, conv_weight, norm_gain, qkv_weight, head_gain, out_weight, state_in):
    tick_count, feat = ticks.shape
    token_count = tick_count // STRIDE
    model_width = conv_weight.shape[1]
    head_count, head_size = state_in.shape[0], state_in.shape[1]
    pairs = model_width // PAIR
    blocks = token_count // BLK
    block_ticks = BLK * STRIDE

    prev = from_behind(ticks[tick_count - 2 * STRIDE :], "inner", 1)
    rows_spec = pl.BlockSpec((BLK, model_width), lambda b: (b, 0))
    state_spec = full((pairs, head_size, PAIR))
    emb, queries, keys, values, local, first_state = pl.pallas_call(
        embed_kernel,
        grid=(blocks,),
        in_specs=[
            pl.BlockSpec((block_ticks, feat), lambda b: (b, 0)),
            full((2 * STRIDE, feat)),
            pl.BlockSpec(memory_space=pl.ANY),
            full((model_width,)),
            pl.BlockSpec(memory_space=pl.ANY),
        ],
        out_specs=[rows_spec, rows_spec, rows_spec, rows_spec, state_spec, state_spec],
        out_shape=[jax.ShapeDtypeStruct((token_count, model_width), jnp.bfloat16)] * 4 + [
            jax.ShapeDtypeStruct((pairs, head_size, PAIR), jnp.float32),
        ] * 2,
        scratch_shapes=[pltpu.VMEM((block_ticks + STRIDE, feat), jnp.float32),
                        pltpu.VMEM(qkv_weight.shape, qkv_weight.dtype),
                        pltpu.SemaphoreType.DMA(()),
                        pltpu.VMEM(conv_weight.shape, conv_weight.dtype),
                        pltpu.SemaphoreType.DMA((2,))],
        compiler_params=pltpu.CompilerParams(dimension_semantics=("arbitrary",)),
    )(ticks, prev, conv_weight, norm_gain, qkv_weight)

    halves = 2
    piece_width = model_width // halves

    def inside_block(piece, earlier, q, k, v):
        block, half = divmod(piece, halves)
        spec = pl.BlockSpec((BLK, piece_width), lambda p, block=block, half=half: (block, half + p))
        in_specs, operands, aliases = [spec, spec, spec], [q, k, v], {}
        kernel = inside_kernel
        if earlier is not None:
            in_specs.append(pl.BlockSpec(memory_space=pl.ANY))
            operands.append(earlier)
            aliases = {3: 0}
        else:
            kernel = first_inside_kernel
        return pl.pallas_call(
            kernel,
            grid=(1,),
            in_specs=in_specs,
            out_specs=spec,
            out_shape=jax.ShapeDtypeStruct((token_count, model_width), jnp.float32),
            input_output_aliases=aliases,
            cost_estimate=pl.CostEstimate(flops=8 * BLK * BLK * piece_width, transcendentals=0,
                                          bytes_accessed=10 * BLK * piece_width),
        )(*operands)

    count = lax.axis_size("inner")
    inside = None
    total, steps, block = local, 1, 0
    received = jnp.zeros_like(local)
    while steps < count:
        if block < blocks * halves:
            total, q_in, k_in, v_in = lax.optimization_barrier((total, queries, keys, values))
        received = from_behind(total, "inner", steps)
        if block < blocks * halves:
            inside = inside_block(block, inside, q_in, k_in, v_in)
            received, inside = lax.optimization_barrier((received, inside))
            block += 1
        steps *= 2
        if steps >= count:
            break
        total = total + received
    while block < blocks * halves:
        inside = inside_block(block, inside, queries, keys, values)
        block += 1
    packed_in = state_in.reshape(pairs, 2, head_size, head_size).transpose(0, 2, 1, 3)
    packed_in = packed_in.reshape(pairs, head_size, PAIR)

    return pl.pallas_call(
        out_kernel,
        grid=(blocks,),
        in_specs=[
            rows_spec,
            state_spec,
            state_spec,
            state_spec,
            state_spec,
            state_spec,
            rows_spec,
            rows_spec,
            full((1, model_width)),
            full(out_weight.shape),
        ],
        out_specs=rows_spec,
        out_shape=jax.ShapeDtypeStruct((token_count, model_width), jnp.bfloat16),
        scratch_shapes=[pltpu.VMEM((BLK, model_width), jnp.bfloat16)],
        compiler_params=pltpu.CompilerParams(dimension_semantics=("arbitrary",)),
    )(queries, packed_in, total, received, local, first_state, inside, emb, head_gain.reshape(1, model_width), out_weight)


def solution(mesh):
    in_specs = (P(("groups", "inner"), None), P(), P(), P(), P(), P(), P("groups", None, None))
    out_specs = P(("groups", "inner"), None)
    return jax.shard_map(shards, mesh=mesh, in_specs=in_specs, out_specs=out_specs, check_vma=False)
```

```python
import functools

import jax
import jax.numpy as jnp
from jax import lax
from jax.experimental import pallas as pl
from jax.experimental.pallas import tpu as pltpu
from jax.sharding import PartitionSpec as P

STRIDE = 8
BLK = 512
PAIR = 128


def from_behind(value, axis, steps):
    count = lax.axis_size(axis)
    initial, last = (max(0, -steps), min(count, count - steps))
    return lax.ppermute(value, axis, [(source, source + steps) for source in range(initial, last)])


def exclusive_scan(value, axis):
    count = lax.axis_size(axis)
    total = value
    steps = 1
    while steps < count:
        total = total + from_behind(total, axis, steps)
        steps *= 2
    return total - value


def embed_kernel(ticks_ref, prev_ref, conv_ref, gain_ref, qkv_hbm,
                 emb_ref, q_ref, k_ref, v_ref, total_ref, first_ref, wide_ref, qkv_w_ref, copy_sem):
    b = pl.program_id(0)
    block_ticks = ticks_ref.shape[0]
    tokens = block_ticks // STRIDE
    model_width = emb_ref.shape[1]

    weight_copy = pltpu.make_async_copy(qkv_hbm, qkv_w_ref, copy_sem)

    @pl.when(b == 0)
    def _():
        weight_copy.start()
        wide_ref[0:STRIDE, :] = prev_ref[STRIDE : 2 * STRIDE, :].astype(jnp.float32)

    @pl.when(b > 0)
    def _():
        wide_ref[0:STRIDE, :] = wide_ref[block_ticks : block_ticks + STRIDE, :]

    wide_ref[STRIDE:, :] = ticks_ref[...].astype(jnp.float32)
    pieces = [wide_ref[pl.ds(j, tokens, stride=STRIDE), :] for j in range(2 * STRIDE)]
    lhs = jnp.concatenate(pieces, axis=1).astype(jnp.bfloat16)
    emb = jnp.dot(lhs, conv_ref[...], preferred_element_type=jnp.float32).astype(jnp.bfloat16)
    emb_ref[...] = emb
    embed_f = emb.astype(jnp.float32)
    mean_sq = jnp.mean(embed_f * embed_f, axis=-1, keepdims=True)
    normed = (embed_f * lax.rsqrt(mean_sq + 1e-05) * gain_ref[...][None, :]).astype(jnp.bfloat16)

    @pl.when(b == 0)
    def _():
        weight_copy.wait()

    def project(part):
        weight = qkv_w_ref[:, part * model_width : (part + 1) * model_width]
        return jnp.dot(normed, weight, preferred_element_type=jnp.float32).astype(jnp.bfloat16)

    queries, keys, values = project(0), project(1), project(2)
    q_ref[...] = queries
    k_ref[...] = keys
    v_ref[...] = values
    lane = lax.broadcasted_iota(jnp.int32, (1, PAIR), 1)
    first = lane < PAIR // 2
    for pair in range(model_width // PAIR):
        cols = slice(pair * PAIR, (pair + 1) * PAIR)
        kv = lax.dot_general(keys[:, cols], values[:, cols], (((0,), (0,)), ((), ())),
                             preferred_element_type=jnp.float32)
        half = PAIR // 2
        packed = jnp.where(first, kv[:half], kv[half:])
        total_ref[pair] = jnp.where(b > 0, total_ref[pair], 0.0) + packed
        first_ref[pair] = jnp.where(b > 0, first_ref[pair], packed)


def inside_kernel(q_ref, k_ref, v_ref, earlier_ref, inside_ref):
    del earlier_ref
    first_inside_kernel(q_ref, k_ref, v_ref, inside_ref)


def first_inside_kernel(q_ref, k_ref, v_ref, inside_ref):
    tokens = q_ref.shape[0]
    part = tokens // 2
    lane = lax.broadcasted_iota(jnp.int32, (1, PAIR), 1)
    first = lane < PAIR // 2
    zero = jnp.zeros((), jnp.bfloat16)
    for pair in range(q_ref.shape[1] // PAIR):
        cols = slice(pair * PAIR, (pair + 1) * PAIR)
        for rows_at in (0, part):
            seen = rows_at + part
            q_rows = q_ref[rows_at : rows_at + part, cols]
            k_seen, v_seen = k_ref[0:seen, cols], v_ref[0:seen, cols]
            causal = (lax.broadcasted_iota(jnp.int32, (part, seen), 0) + rows_at
                      >= lax.broadcasted_iota(jnp.int32, (part, seen), 1))
            inside = None
            for use in (first, ~first):
                q_one = jnp.where(use, q_rows, zero)
                scores = lax.dot_general(q_one, k_seen, (((1,), (1,)), ((), ())),
                                         preferred_element_type=jnp.float32)
                scores = jnp.where(causal, scores, 0.0).astype(jnp.bfloat16)
                term = jnp.dot(scores, jnp.where(use, v_seen, zero), preferred_element_type=jnp.float32)
                inside = term if inside is None else inside + term
            inside_ref[rows_at : rows_at + part, cols] = inside


def out_kernel(q_ref, start_ref, total_ref, received_ref, local_ref, first_ref, inside_ref, emb_ref, hgain_ref, out_w_ref,
               out_ref, att_ref):
    b = pl.program_id(0)
    model_width = out_ref.shape[1]
    lane = lax.broadcasted_iota(jnp.int32, (1, PAIR), 1)
    first = lane < PAIR // 2
    head_size = PAIR // 2
    for pair in range(model_width // PAIR):
        cols = slice(pair * PAIR, (pair + 1) * PAIR)
        packed = (start_ref[pair] + (total_ref[pair] + received_ref[pair] - local_ref[pair])
                  + jnp.where(b > 0, first_ref[pair], 0.0))
        diag = jnp.concatenate([jnp.where(first, packed, 0.0), jnp.where(first, 0.0, packed)], axis=0)
        high = diag.astype(jnp.bfloat16)
        low = (diag - high.astype(jnp.float32)).astype(jnp.bfloat16)
        q_pair = q_ref[:, cols]
        carried = (jnp.dot(q_pair, high, preferred_element_type=jnp.float32)
                   + jnp.dot(q_pair, low, preferred_element_type=jnp.float32))
        combined = inside_ref[:, cols] + carried
        square = combined * combined
        sum_first = jnp.sum(jnp.where(first, square, 0.0), axis=-1, keepdims=True)
        sum_second = jnp.sum(jnp.where(first, 0.0, square), axis=-1, keepdims=True)
        scale = jnp.where(first, lax.rsqrt(sum_first / head_size + 1e-06),
                          lax.rsqrt(sum_second / head_size + 1e-06))
        att_ref[:, cols] = (combined * scale * hgain_ref[:, cols]).astype(jnp.bfloat16)
    out = emb_ref[...].astype(jnp.float32) + jnp.dot(att_ref[...], out_w_ref[...],
                                                     preferred_element_type=jnp.float32)
    out_ref[...] = out.astype(jnp.bfloat16)


def full(shape):
    return pl.BlockSpec(shape, lambda b: (0,) * len(shape))


def shards(ticks, conv_weight, norm_gain, qkv_weight, head_gain, out_weight, state_in):
    tick_count, feat = ticks.shape
    token_count = tick_count // STRIDE
    model_width = conv_weight.shape[1]
    head_count, head_size = state_in.shape[0], state_in.shape[1]
    pairs = model_width // PAIR
    blocks = token_count // BLK
    block_ticks = BLK * STRIDE

    prev = from_behind(ticks[tick_count - 2 * STRIDE :], "inner", 1)
    rows_spec = pl.BlockSpec((BLK, model_width), lambda b: (b, 0))
    state_spec = full((pairs, head_size, PAIR))
    emb, queries, keys, values, local, first_state = pl.pallas_call(
        embed_kernel,
        grid=(blocks,),
        in_specs=[
            pl.BlockSpec((block_ticks, feat), lambda b: (b, 0)),
            full((2 * STRIDE, feat)),
            full(conv_weight.shape),
            full((model_width,)),
            pl.BlockSpec(memory_space=pl.ANY),
        ],
        out_specs=[rows_spec, rows_spec, rows_spec, rows_spec, state_spec, state_spec],
        out_shape=[jax.ShapeDtypeStruct((token_count, model_width), jnp.bfloat16)] * 4 + [
            jax.ShapeDtypeStruct((pairs, head_size, PAIR), jnp.float32),
        ] * 2,
        scratch_shapes=[pltpu.VMEM((block_ticks + STRIDE, feat), jnp.float32),
                        pltpu.VMEM(qkv_weight.shape, qkv_weight.dtype),
                        pltpu.SemaphoreType.DMA(())],
        compiler_params=pltpu.CompilerParams(dimension_semantics=("arbitrary",)),
    )(ticks, prev, conv_weight, norm_gain, qkv_weight)

    halves = 2
    piece_width = model_width // halves

    def inside_block(piece, earlier, q, k, v):
        block, half = divmod(piece, halves)
        spec = pl.BlockSpec((BLK, piece_width), lambda p, block=block, half=half: (block, half + p))
        in_specs, operands, aliases = [spec, spec, spec], [q, k, v], {}
        kernel = inside_kernel
        if earlier is not None:
            in_specs.append(pl.BlockSpec(memory_space=pl.ANY))
            operands.append(earlier)
            aliases = {3: 0}
        else:
            kernel = first_inside_kernel
        return pl.pallas_call(
            kernel,
            grid=(1,),
            in_specs=in_specs,
            out_specs=spec,
            out_shape=jax.ShapeDtypeStruct((token_count, model_width), jnp.float32),
            input_output_aliases=aliases,
            cost_estimate=pl.CostEstimate(flops=8 * BLK * BLK * piece_width, transcendentals=0,
                                          bytes_accessed=10 * BLK * piece_width),
        )(*operands)

    count = lax.axis_size("inner")
    inside = None
    total, steps, block = local, 1, 0
    received = jnp.zeros_like(local)
    while steps < count:
        if block < blocks * halves:
            total, q_in, k_in, v_in = lax.optimization_barrier((total, queries, keys, values))
        received = from_behind(total, "inner", steps)
        if block < blocks * halves:
            inside = inside_block(block, inside, q_in, k_in, v_in)
            received, inside = lax.optimization_barrier((received, inside))
            block += 1
        steps *= 2
        if steps >= count:
            break
        total = total + received
    while block < blocks * halves:
        inside = inside_block(block, inside, queries, keys, values)
        block += 1
    packed_in = state_in.reshape(pairs, 2, head_size, head_size).transpose(0, 2, 1, 3)
    packed_in = packed_in.reshape(pairs, head_size, PAIR)

    return pl.pallas_call(
        out_kernel,
        grid=(blocks,),
        in_specs=[
            rows_spec,
            state_spec,
            state_spec,
            state_spec,
            state_spec,
            state_spec,
            rows_spec,
            rows_spec,
            full((1, model_width)),
            full(out_weight.shape),
        ],
        out_specs=rows_spec,
        out_shape=jax.ShapeDtypeStruct((token_count, model_width), jnp.bfloat16),
        scratch_shapes=[pltpu.VMEM((BLK, model_width), jnp.bfloat16)],
        compiler_params=pltpu.CompilerParams(dimension_semantics=("arbitrary",)),
    )(queries, packed_in, total, received, local, first_state, inside, emb, head_gain.reshape(1, model_width), out_weight)


def solution(mesh):
    in_specs = (P(("groups", "inner"), None), P(), P(), P(), P(), P(), P("groups", None, None))
    out_specs = P(("groups", "inner"), None)
    return jax.shard_map(shards, mesh=mesh, in_specs=in_specs, out_specs=out_specs, check_vma=False)
```

```python
import functools

import jax
import jax.numpy as jnp
from jax import lax
from jax.experimental import pallas as pl
from jax.experimental.pallas import tpu as pltpu
from jax.sharding import PartitionSpec as P

STRIDE = 8
BLK = 512
PAIR = 128


def from_behind(value, axis, steps):
    count = lax.axis_size(axis)
    initial, last = (max(0, -steps), min(count, count - steps))
    return lax.ppermute(value, axis, [(source, source + steps) for source in range(initial, last)])


def exclusive_scan(value, axis):
    count = lax.axis_size(axis)
    total = value
    steps = 1
    while steps < count:
        total = total + from_behind(total, axis, steps)
        steps *= 2
    return total - value


def embed_kernel(ticks_ref, prev_ref, conv_ref, gain_ref, qkv_hbm,
                 emb_ref, q_ref, k_ref, v_ref, total_ref, first_ref, wide_ref, qkv_w_ref, copy_sem):
    b = pl.program_id(0)
    block_ticks = ticks_ref.shape[0]
    tokens = block_ticks // STRIDE
    model_width = emb_ref.shape[1]

    weight_copy = pltpu.make_async_copy(qkv_hbm, qkv_w_ref, copy_sem)

    @pl.when(b == 0)
    def _():
        weight_copy.start()
        wide_ref[0:STRIDE, :] = prev_ref[STRIDE : 2 * STRIDE, :].astype(jnp.float32)

    @pl.when(b > 0)
    def _():
        wide_ref[0:STRIDE, :] = wide_ref[block_ticks : block_ticks + STRIDE, :]

    wide_ref[STRIDE:, :] = ticks_ref[...].astype(jnp.float32)
    pieces = [wide_ref[pl.ds(j, tokens, stride=STRIDE), :] for j in range(2 * STRIDE)]
    lhs = jnp.concatenate(pieces, axis=1).astype(jnp.bfloat16)
    emb = jnp.dot(lhs, conv_ref[...], preferred_element_type=jnp.float32).astype(jnp.bfloat16)
    emb_ref[...] = emb
    embed_f = emb.astype(jnp.float32)
    mean_sq = jnp.mean(embed_f * embed_f, axis=-1, keepdims=True)
    normed = (embed_f * lax.rsqrt(mean_sq + 1e-05) * gain_ref[...][None, :]).astype(jnp.bfloat16)

    @pl.when(b == 0)
    def _():
        weight_copy.wait()

    def project(part):
        weight = qkv_w_ref[:, part * model_width : (part + 1) * model_width]
        return jnp.dot(normed, weight, preferred_element_type=jnp.float32).astype(jnp.bfloat16)

    queries, keys, values = project(0), project(1), project(2)
    q_ref[...] = queries
    k_ref[...] = keys
    v_ref[...] = values
    lane = lax.broadcasted_iota(jnp.int32, (1, PAIR), 1)
    first = lane < PAIR // 2
    for pair in range(model_width // PAIR):
        cols = slice(pair * PAIR, (pair + 1) * PAIR)
        kv = lax.dot_general(keys[:, cols], values[:, cols], (((0,), (0,)), ((), ())),
                             preferred_element_type=jnp.float32)
        half = PAIR // 2
        packed = jnp.where(first, kv[:half], kv[half:])
        total_ref[pair] = jnp.where(b > 0, total_ref[pair], 0.0) + packed
        first_ref[pair] = jnp.where(b > 0, first_ref[pair], packed)


def inside_kernel(q_ref, k_ref, v_ref, earlier_ref, inside_ref):
    del earlier_ref
    first_inside_kernel(q_ref, k_ref, v_ref, inside_ref)


def first_inside_kernel(q_ref, k_ref, v_ref, inside_ref):
    tokens = q_ref.shape[0]
    part = tokens // 2
    lane = lax.broadcasted_iota(jnp.int32, (1, PAIR), 1)
    first = lane < PAIR // 2
    zero = jnp.zeros((), jnp.bfloat16)
    for pair in range(q_ref.shape[1] // PAIR):
        cols = slice(pair * PAIR, (pair + 1) * PAIR)
        for rows_at in (0, part):
            seen = rows_at + part
            q_rows = q_ref[rows_at : rows_at + part, cols]
            k_seen, v_seen = k_ref[0:seen, cols], v_ref[0:seen, cols]
            causal = (lax.broadcasted_iota(jnp.int32, (part, seen), 0) + rows_at
                      >= lax.broadcasted_iota(jnp.int32, (part, seen), 1))
            inside = None
            for use in (first, ~first):
                q_one = jnp.where(use, q_rows, zero)
                scores = lax.dot_general(q_one, k_seen, (((1,), (1,)), ((), ())),
                                         preferred_element_type=jnp.float32)
                scores = jnp.where(causal, scores, 0.0).astype(jnp.bfloat16)
                term = jnp.dot(scores, jnp.where(use, v_seen, zero), preferred_element_type=jnp.float32)
                inside = term if inside is None else inside + term
            inside_ref[rows_at : rows_at + part, cols] = inside


def out_kernel(q_ref, base_ref, total_ref, received_ref, inside_ref, emb_ref, hgain_ref, out_w_ref, out_ref, att_ref):
    model_width = out_ref.shape[1]
    lane = lax.broadcasted_iota(jnp.int32, (1, PAIR), 1)
    first = lane < PAIR // 2
    head_size = PAIR // 2
    for pair in range(model_width // PAIR):
        cols = slice(pair * PAIR, (pair + 1) * PAIR)
        packed = base_ref[0, pair] + (total_ref[pair] + received_ref[pair])
        diag = jnp.concatenate([jnp.where(first, packed, 0.0), jnp.where(first, 0.0, packed)], axis=0)
        high = diag.astype(jnp.bfloat16)
        low = (diag - high.astype(jnp.float32)).astype(jnp.bfloat16)
        q_pair = q_ref[:, cols]
        carried = (jnp.dot(q_pair, high, preferred_element_type=jnp.float32)
                   + jnp.dot(q_pair, low, preferred_element_type=jnp.float32))
        combined = inside_ref[:, cols] + carried
        square = combined * combined
        sum_first = jnp.sum(jnp.where(first, square, 0.0), axis=-1, keepdims=True)
        sum_second = jnp.sum(jnp.where(first, 0.0, square), axis=-1, keepdims=True)
        scale = jnp.where(first, lax.rsqrt(sum_first / head_size + 1e-06),
                          lax.rsqrt(sum_second / head_size + 1e-06))
        att_ref[:, cols] = (combined * scale * hgain_ref[:, cols]).astype(jnp.bfloat16)
    out = emb_ref[...].astype(jnp.float32) + jnp.dot(att_ref[...], out_w_ref[...],
                                                     preferred_element_type=jnp.float32)
    out_ref[...] = out.astype(jnp.bfloat16)


def full(shape):
    return pl.BlockSpec(shape, lambda b: (0,) * len(shape))


def shards(ticks, conv_weight, norm_gain, qkv_weight, head_gain, out_weight, state_in):
    tick_count, feat = ticks.shape
    token_count = tick_count // STRIDE
    model_width = conv_weight.shape[1]
    head_count, head_size = state_in.shape[0], state_in.shape[1]
    pairs = model_width // PAIR
    blocks = token_count // BLK
    block_ticks = BLK * STRIDE

    prev = from_behind(ticks[tick_count - 2 * STRIDE :], "inner", 1)
    rows_spec = pl.BlockSpec((BLK, model_width), lambda b: (b, 0))
    state_spec = full((pairs, head_size, PAIR))
    emb, queries, keys, values, local, first_state = pl.pallas_call(
        embed_kernel,
        grid=(blocks,),
        in_specs=[
            pl.BlockSpec((block_ticks, feat), lambda b: (b, 0)),
            full((2 * STRIDE, feat)),
            full(conv_weight.shape),
            full((model_width,)),
            pl.BlockSpec(memory_space=pl.ANY),
        ],
        out_specs=[rows_spec, rows_spec, rows_spec, rows_spec, state_spec, state_spec],
        out_shape=[jax.ShapeDtypeStruct((token_count, model_width), jnp.bfloat16)] * 4 + [
            jax.ShapeDtypeStruct((pairs, head_size, PAIR), jnp.float32),
        ] * 2,
        scratch_shapes=[pltpu.VMEM((block_ticks + STRIDE, feat), jnp.float32),
                        pltpu.VMEM(qkv_weight.shape, qkv_weight.dtype),
                        pltpu.SemaphoreType.DMA(())],
        compiler_params=pltpu.CompilerParams(dimension_semantics=("arbitrary",)),
    )(ticks, prev, conv_weight, norm_gain, qkv_weight)

    halves = 2
    piece_width = model_width // halves

    def inside_block(piece, earlier, q, k, v):
        block, half = divmod(piece, halves)
        spec = pl.BlockSpec((BLK, piece_width), lambda p, block=block, half=half: (block, half + p))
        in_specs, operands, aliases = [spec, spec, spec], [q, k, v], {}
        kernel = inside_kernel
        if earlier is not None:
            in_specs.append(pl.BlockSpec(memory_space=pl.ANY))
            operands.append(earlier)
            aliases = {3: 0}
        else:
            kernel = first_inside_kernel
        return pl.pallas_call(
            kernel,
            grid=(1,),
            in_specs=in_specs,
            out_specs=spec,
            out_shape=jax.ShapeDtypeStruct((token_count, model_width), jnp.float32),
            input_output_aliases=aliases,
            cost_estimate=pl.CostEstimate(flops=8 * BLK * BLK * piece_width, transcendentals=0,
                                          bytes_accessed=10 * BLK * piece_width),
        )(*operands)

    count = lax.axis_size("inner")
    inside = None
    total, steps, block = local, 1, 0
    received = jnp.zeros_like(local)
    while steps < count:
        if block < blocks * halves:
            total, q_in, k_in, v_in = lax.optimization_barrier((total, queries, keys, values))
        received = from_behind(total, "inner", steps)
        if block < blocks * halves:
            inside = inside_block(block, inside, q_in, k_in, v_in)
            received, inside = lax.optimization_barrier((received, inside))
            block += 1
        steps *= 2
        if steps >= count:
            break
        total = total + received
    while block < blocks * halves:
        inside = inside_block(block, inside, queries, keys, values)
        block += 1
    packed_in = state_in.reshape(pairs, 2, head_size, head_size).transpose(0, 2, 1, 3)
    packed_in = packed_in.reshape(pairs, head_size, PAIR)
    base = [packed_in - local]
    for block in range(1, blocks):
        base.append(base[-1] + first_state)
    base = jnp.stack(base)
    base_spec = pl.BlockSpec((1, pairs, head_size, PAIR), lambda b: (b, 0, 0, 0))

    return pl.pallas_call(
        out_kernel,
        grid=(blocks,),
        in_specs=[
            rows_spec,
            base_spec,
            state_spec,
            state_spec,
            rows_spec,
            rows_spec,
            full((1, model_width)),
            full(out_weight.shape),
        ],
        out_specs=rows_spec,
        out_shape=jax.ShapeDtypeStruct((token_count, model_width), jnp.bfloat16),
        scratch_shapes=[pltpu.VMEM((BLK, model_width), jnp.bfloat16)],
        compiler_params=pltpu.CompilerParams(dimension_semantics=("arbitrary",)),
    )(queries, base, total, received, inside, emb, head_gain.reshape(1, model_width), out_weight)


def solution(mesh):
    in_specs = (P(("groups", "inner"), None), P(), P(), P(), P(), P(), P("groups", None, None))
    out_specs = P(("groups", "inner"), None)
    return jax.shard_map(shards, mesh=mesh, in_specs=in_specs, out_specs=out_specs, check_vma=False)
```

```python
import functools

import jax
import jax.numpy as jnp
from jax import lax
from jax.experimental import pallas as pl
from jax.experimental.pallas import tpu as pltpu
from jax.sharding import PartitionSpec as P

STRIDE = 8
BLK = 512
PAIR = 128


def from_behind(value, axis, steps):
    count = lax.axis_size(axis)
    initial, last = (max(0, -steps), min(count, count - steps))
    return lax.ppermute(value, axis, [(source, source + steps) for source in range(initial, last)])


def exclusive_scan(value, axis):
    count = lax.axis_size(axis)
    total = value
    steps = 1
    while steps < count:
        total = total + from_behind(total, axis, steps)
        steps *= 2
    return total - value


def embed_kernel(ticks_ref, prev_ref, conv_ref, gain_ref, qkv_hbm,
                 emb_ref, q_ref, k_ref, v_ref, total_ref, first_ref, wide_ref, qkv_w_ref, copy_sem):
    b = pl.program_id(0)
    block_ticks = ticks_ref.shape[0]
    tokens = block_ticks // STRIDE
    model_width = emb_ref.shape[1]

    weight_copy = pltpu.make_async_copy(qkv_hbm, qkv_w_ref, copy_sem)

    @pl.when(b == 0)
    def _():
        weight_copy.start()
        wide_ref[0:STRIDE, :] = prev_ref[STRIDE : 2 * STRIDE, :].astype(jnp.float32)

    @pl.when(b > 0)
    def _():
        wide_ref[0:STRIDE, :] = wide_ref[block_ticks : block_ticks + STRIDE, :]

    wide_ref[STRIDE:, :] = ticks_ref[...].astype(jnp.float32)
    pieces = [wide_ref[pl.ds(j, tokens, stride=STRIDE), :] for j in range(2 * STRIDE)]
    lhs = jnp.concatenate(pieces, axis=1).astype(jnp.bfloat16)
    emb = jnp.dot(lhs, conv_ref[...], preferred_element_type=jnp.float32).astype(jnp.bfloat16)
    emb_ref[...] = emb
    embed_f = emb.astype(jnp.float32)
    mean_sq = jnp.mean(embed_f * embed_f, axis=-1, keepdims=True)
    normed = (embed_f * lax.rsqrt(mean_sq + 1e-05) * gain_ref[...][None, :]).astype(jnp.bfloat16)

    @pl.when(b == 0)
    def _():
        weight_copy.wait()

    def project(part):
        weight = qkv_w_ref[:, part * model_width : (part + 1) * model_width]
        return jnp.dot(normed, weight, preferred_element_type=jnp.float32).astype(jnp.bfloat16)

    queries, keys, values = project(0), project(1), project(2)
    q_ref[...] = queries
    k_ref[...] = keys
    v_ref[...] = values
    lane = lax.broadcasted_iota(jnp.int32, (1, PAIR), 1)
    first = lane < PAIR // 2
    for pair in range(model_width // PAIR):
        cols = slice(pair * PAIR, (pair + 1) * PAIR)
        kv = lax.dot_general(keys[:, cols], values[:, cols], (((0,), (0,)), ((), ())),
                             preferred_element_type=jnp.float32)
        half = PAIR // 2
        packed = jnp.where(first, kv[:half], kv[half:])
        total_ref[pair] = jnp.where(b > 0, total_ref[pair], 0.0) + packed
        first_ref[pair] = jnp.where(b > 0, first_ref[pair], packed)


def inside_kernel(q_ref, k_ref, v_ref, earlier_ref, inside_ref):
    del earlier_ref
    first_inside_kernel(q_ref, k_ref, v_ref, inside_ref)


def first_inside_kernel(q_ref, k_ref, v_ref, inside_ref):
    tokens = q_ref.shape[0]
    part = tokens // 2
    lane = lax.broadcasted_iota(jnp.int32, (1, PAIR), 1)
    first = lane < PAIR // 2
    zero = jnp.zeros((), jnp.bfloat16)
    for pair in range(q_ref.shape[1] // PAIR):
        cols = slice(pair * PAIR, (pair + 1) * PAIR)
        for rows_at in (0, part):
            seen = rows_at + part
            q_rows = q_ref[rows_at : rows_at + part, cols]
            k_seen, v_seen = k_ref[0:seen, cols], v_ref[0:seen, cols]
            causal = (lax.broadcasted_iota(jnp.int32, (part, seen), 0) + rows_at
                      >= lax.broadcasted_iota(jnp.int32, (part, seen), 1))
            inside = None
            for use in (first, ~first):
                q_one = jnp.where(use, q_rows, zero)
                scores = lax.dot_general(q_one, k_seen, (((1,), (1,)), ((), ())),
                                         preferred_element_type=jnp.float32)
                scores = jnp.where(causal, scores, 0.0).astype(jnp.bfloat16)
                term = jnp.dot(scores, jnp.where(use, v_seen, zero), preferred_element_type=jnp.float32)
                inside = term if inside is None else inside + term
            inside_ref[rows_at : rows_at + part, cols] = inside


def out_kernel(q_ref, base_ref, total_ref, received_ref, inside_ref, emb_ref, hgain_ref, out_w_ref, out_ref, att_ref):
    model_width = out_ref.shape[1]
    lane = lax.broadcasted_iota(jnp.int32, (1, PAIR), 1)
    first = lane < PAIR // 2
    head_size = PAIR // 2
    for pair in range(model_width // PAIR):
        cols = slice(pair * PAIR, (pair + 1) * PAIR)
        packed = base_ref[0, pair] + (total_ref[pair] + received_ref[pair])
        diag = jnp.concatenate([jnp.where(first, packed, 0.0), jnp.where(first, 0.0, packed)], axis=0)
        high = diag.astype(jnp.bfloat16)
        low = (diag - high.astype(jnp.float32)).astype(jnp.bfloat16)
        q_pair = q_ref[:, cols]
        carried = (jnp.dot(q_pair, high, preferred_element_type=jnp.float32)
                   + jnp.dot(q_pair, low, preferred_element_type=jnp.float32))
        combined = inside_ref[:, cols] + carried
        square = combined * combined
        sum_first = jnp.sum(jnp.where(first, square, 0.0), axis=-1, keepdims=True)
        sum_second = jnp.sum(jnp.where(first, 0.0, square), axis=-1, keepdims=True)
        scale = jnp.where(first, lax.rsqrt(sum_first / head_size + 1e-06),
                          lax.rsqrt(sum_second / head_size + 1e-06))
        att_ref[:, cols] = (combined * scale * hgain_ref[:, cols]).astype(jnp.bfloat16)
    out = emb_ref[...].astype(jnp.float32) + jnp.dot(att_ref[...], out_w_ref[...],
                                                     preferred_element_type=jnp.float32)
    out_ref[...] = out.astype(jnp.bfloat16)


def full(shape):
    return pl.BlockSpec(shape, lambda b: (0,) * len(shape))


def shards(ticks, conv_weight, norm_gain, qkv_weight, head_gain, out_weight, state_in):
    tick_count, feat = ticks.shape
    token_count = tick_count // STRIDE
    model_width = conv_weight.shape[1]
    head_count, head_size = state_in.shape[0], state_in.shape[1]
    pairs = model_width // PAIR
    blocks = token_count // BLK
    block_ticks = BLK * STRIDE

    prev = from_behind(ticks[tick_count - 2 * STRIDE :], "inner", 1)
    rows_spec = pl.BlockSpec((BLK, model_width), lambda b: (b, 0))
    state_spec = full((pairs, head_size, PAIR))
    emb, queries, keys, values, local, first_state = pl.pallas_call(
        embed_kernel,
        grid=(blocks,),
        in_specs=[
            pl.BlockSpec((block_ticks, feat), lambda b: (b, 0)),
            full((2 * STRIDE, feat)),
            full(conv_weight.shape),
            full((model_width,)),
            pl.BlockSpec(memory_space=pl.ANY),
        ],
        out_specs=[rows_spec, rows_spec, rows_spec, rows_spec, state_spec, state_spec],
        out_shape=[jax.ShapeDtypeStruct((token_count, model_width), jnp.bfloat16)] * 4 + [
            jax.ShapeDtypeStruct((pairs, head_size, PAIR), jnp.float32),
        ] * 2,
        scratch_shapes=[pltpu.VMEM((block_ticks + STRIDE, feat), jnp.float32),
                        pltpu.VMEM(qkv_weight.shape, qkv_weight.dtype),
                        pltpu.SemaphoreType.DMA(())],
        compiler_params=pltpu.CompilerParams(dimension_semantics=("arbitrary",)),
    )(ticks, prev, conv_weight, norm_gain, qkv_weight)

    halves = 2
    piece_width = model_width // halves

    def inside_block(piece, earlier, q, k, v):
        block, half = divmod(piece, halves)
        spec = pl.BlockSpec((BLK, piece_width), lambda p, block=block, half=half: (block, half + p))
        in_specs, operands, aliases = [spec, spec, spec], [q, k, v], {}
        kernel = inside_kernel
        if earlier is not None:
            in_specs.append(pl.BlockSpec(memory_space=pl.ANY))
            operands.append(earlier)
            aliases = {3: 0}
        else:
            kernel = first_inside_kernel
        return pl.pallas_call(
            kernel,
            grid=(1,),
            in_specs=in_specs,
            out_specs=spec,
            out_shape=jax.ShapeDtypeStruct((token_count, model_width), jnp.float32),
            input_output_aliases=aliases,
            cost_estimate=pl.CostEstimate(flops=8 * BLK * BLK * piece_width, transcendentals=0,
                                          bytes_accessed=10 * BLK * piece_width),
        )(*operands)

    packed_in = state_in.reshape(pairs, 2, head_size, head_size).transpose(0, 2, 1, 3)
    packed_in = packed_in.reshape(pairs, head_size, PAIR)
    base = [packed_in - local]
    for block in range(1, blocks):
        base.append(base[-1] + first_state)
    base = jnp.stack(base)
    head_gain_row = head_gain.reshape(1, model_width)
    count = lax.axis_size("inner")
    inside = None
    total, steps, block = local, 1, 0
    received = jnp.zeros_like(local)
    while steps < count:
        if block < blocks * halves:
            total, q_in, k_in, v_in = lax.optimization_barrier((total, queries, keys, values))
        received = from_behind(total, "inner", steps)
        if block < blocks * halves:
            inside = inside_block(block, inside, q_in, k_in, v_in)
            if block == 1:
                received, inside, base, head_gain_row = lax.optimization_barrier(
                    (received, inside, base, head_gain_row))
            else:
                received, inside = lax.optimization_barrier((received, inside))
            block += 1
        steps *= 2
        if steps >= count:
            break
        total = total + received
    while block < blocks * halves:
        inside = inside_block(block, inside, queries, keys, values)
        block += 1
    base_spec = pl.BlockSpec((1, pairs, head_size, PAIR), lambda b: (b, 0, 0, 0))

    return pl.pallas_call(
        out_kernel,
        grid=(blocks,),
        in_specs=[
            rows_spec,
            base_spec,
            state_spec,
            state_spec,
            rows_spec,
            rows_spec,
            full((1, model_width)),
            full(out_weight.shape),
        ],
        out_specs=rows_spec,
        out_shape=jax.ShapeDtypeStruct((token_count, model_width), jnp.bfloat16),
        scratch_shapes=[pltpu.VMEM((BLK, model_width), jnp.bfloat16)],
        compiler_params=pltpu.CompilerParams(dimension_semantics=("arbitrary",)),
    )(queries, base, total, received, inside, emb, head_gain_row, out_weight)


def solution(mesh):
    in_specs = (P(("groups", "inner"), None), P(), P(), P(), P(), P(), P("groups", None, None))
    out_specs = P(("groups", "inner"), None)
    return jax.shard_map(shards, mesh=mesh, in_specs=in_specs, out_specs=out_specs, check_vma=False)
```

```python
import functools

import jax
import jax.numpy as jnp
from jax import lax
from jax.experimental import pallas as pl
from jax.experimental.pallas import tpu as pltpu
from jax.sharding import PartitionSpec as P

STRIDE = 8
BLK = 512
PAIR = 128


def from_behind(value, axis, steps):
    count = lax.axis_size(axis)
    initial, last = (max(0, -steps), min(count, count - steps))
    return lax.ppermute(value, axis, [(source, source + steps) for source in range(initial, last)])


def exclusive_scan(value, axis):
    count = lax.axis_size(axis)
    total = value
    steps = 1
    while steps < count:
        total = total + from_behind(total, axis, steps)
        steps *= 2
    return total - value


def embed_kernel(ticks_ref, prev_ref, conv_hbm, gain_ref, qkv_hbm,
                 emb_ref, q_ref, k_ref, v_ref, total_ref, first_ref, wide_ref, qkv_w_ref, copy_sem,
                 conv_ref, conv_sem):
    b = pl.program_id(0)
    block_ticks = ticks_ref.shape[0]
    tokens = block_ticks // STRIDE
    model_width = emb_ref.shape[1]

    weight_copy = pltpu.make_async_copy(qkv_hbm, qkv_w_ref, copy_sem)
    conv_copy = pltpu.make_async_copy(conv_hbm, conv_ref, conv_sem)

    @pl.when(b == 0)
    def _():
        conv_copy.start()
        weight_copy.start()
        wide_ref[0:STRIDE, :] = prev_ref[STRIDE : 2 * STRIDE, :].astype(jnp.float32)

    @pl.when(b > 0)
    def _():
        wide_ref[0:STRIDE, :] = wide_ref[block_ticks : block_ticks + STRIDE, :]

    wide_ref[STRIDE:, :] = ticks_ref[...].astype(jnp.float32)
    pieces = [wide_ref[pl.ds(j, tokens, stride=STRIDE), :] for j in range(2 * STRIDE)]
    lhs = jnp.concatenate(pieces, axis=1).astype(jnp.bfloat16)

    @pl.when(b == 0)
    def _():
        conv_copy.wait()

    emb = jnp.dot(lhs, conv_ref[...], preferred_element_type=jnp.float32).astype(jnp.bfloat16)
    emb_ref[...] = emb
    embed_f = emb.astype(jnp.float32)
    mean_sq = jnp.mean(embed_f * embed_f, axis=-1, keepdims=True)
    normed = (embed_f * lax.rsqrt(mean_sq + 1e-05) * gain_ref[...][None, :]).astype(jnp.bfloat16)

    @pl.when(b == 0)
    def _():
        weight_copy.wait()

    def project(part):
        weight = qkv_w_ref[:, part * model_width : (part + 1) * model_width]
        return jnp.dot(normed, weight, preferred_element_type=jnp.float32).astype(jnp.bfloat16)

    queries, keys, values = project(0), project(1), project(2)
    q_ref[...] = queries
    k_ref[...] = keys
    v_ref[...] = values
    lane = lax.broadcasted_iota(jnp.int32, (1, PAIR), 1)
    first = lane < PAIR // 2
    for pair in range(model_width // PAIR):
        cols = slice(pair * PAIR, (pair + 1) * PAIR)
        kv = lax.dot_general(keys[:, cols], values[:, cols], (((0,), (0,)), ((), ())),
                             preferred_element_type=jnp.float32)
        half = PAIR // 2
        packed = jnp.where(first, kv[:half], kv[half:])
        total_ref[pair] = jnp.where(b > 0, total_ref[pair], 0.0) + packed
        first_ref[pair] = jnp.where(b > 0, first_ref[pair], packed)


def inside_kernel(q_ref, k_ref, v_ref, earlier_ref, inside_ref):
    del earlier_ref
    first_inside_kernel(q_ref, k_ref, v_ref, inside_ref)


def first_inside_kernel(q_ref, k_ref, v_ref, inside_ref):
    tokens = q_ref.shape[0]
    part = tokens // 2
    lane = lax.broadcasted_iota(jnp.int32, (1, PAIR), 1)
    first = lane < PAIR // 2
    zero = jnp.zeros((), jnp.bfloat16)
    for pair in range(q_ref.shape[1] // PAIR):
        cols = slice(pair * PAIR, (pair + 1) * PAIR)
        for rows_at in (0, part):
            seen = rows_at + part
            q_rows = q_ref[rows_at : rows_at + part, cols]
            k_seen, v_seen = k_ref[0:seen, cols], v_ref[0:seen, cols]
            causal = (lax.broadcasted_iota(jnp.int32, (part, seen), 0) + rows_at
                      >= lax.broadcasted_iota(jnp.int32, (part, seen), 1))
            inside = None
            for use in (first, ~first):
                q_one = jnp.where(use, q_rows, zero)
                scores = lax.dot_general(q_one, k_seen, (((1,), (1,)), ((), ())),
                                         preferred_element_type=jnp.float32)
                scores = jnp.where(causal, scores, 0.0).astype(jnp.bfloat16)
                term = jnp.dot(scores, jnp.where(use, v_seen, zero), preferred_element_type=jnp.float32)
                inside = term if inside is None else inside + term
            inside_ref[rows_at : rows_at + part, cols] = inside


def out_kernel(q_ref, base_ref, total_ref, received_ref, inside_ref, emb_ref, hgain_ref, out_w_ref, out_ref, att_ref):
    model_width = out_ref.shape[1]
    lane = lax.broadcasted_iota(jnp.int32, (1, PAIR), 1)
    first = lane < PAIR // 2
    head_size = PAIR // 2
    for pair in range(model_width // PAIR):
        cols = slice(pair * PAIR, (pair + 1) * PAIR)
        packed = base_ref[0, pair] + (total_ref[pair] + received_ref[pair])
        diag = jnp.concatenate([jnp.where(first, packed, 0.0), jnp.where(first, 0.0, packed)], axis=0)
        high = diag.astype(jnp.bfloat16)
        low = (diag - high.astype(jnp.float32)).astype(jnp.bfloat16)
        q_pair = q_ref[:, cols]
        carried = (jnp.dot(q_pair, high, preferred_element_type=jnp.float32)
                   + jnp.dot(q_pair, low, preferred_element_type=jnp.float32))
        combined = inside_ref[:, cols] + carried
        square = combined * combined
        sum_first = jnp.sum(jnp.where(first, square, 0.0), axis=-1, keepdims=True)
        sum_second = jnp.sum(jnp.where(first, 0.0, square), axis=-1, keepdims=True)
        scale = jnp.where(first, lax.rsqrt(sum_first / head_size + 1e-06),
                          lax.rsqrt(sum_second / head_size + 1e-06))
        att_ref[:, cols] = (combined * scale * hgain_ref[:, cols]).astype(jnp.bfloat16)
    out = emb_ref[...].astype(jnp.float32) + jnp.dot(att_ref[...], out_w_ref[...],
                                                     preferred_element_type=jnp.float32)
    out_ref[...] = out.astype(jnp.bfloat16)


def full(shape):
    return pl.BlockSpec(shape, lambda b: (0,) * len(shape))


def shards(ticks, conv_weight, norm_gain, qkv_weight, head_gain, out_weight, state_in):
    tick_count, feat = ticks.shape
    token_count = tick_count // STRIDE
    model_width = conv_weight.shape[1]
    head_count, head_size = state_in.shape[0], state_in.shape[1]
    pairs = model_width // PAIR
    blocks = token_count // BLK
    block_ticks = BLK * STRIDE

    prev = from_behind(ticks[tick_count - 2 * STRIDE :], "inner", 1)
    rows_spec = pl.BlockSpec((BLK, model_width), lambda b: (b, 0))
    state_spec = full((pairs, head_size, PAIR))
    emb, queries, keys, values, local, first_state = pl.pallas_call(
        embed_kernel,
        grid=(blocks,),
        in_specs=[
            pl.BlockSpec((block_ticks, feat), lambda b: (b, 0)),
            full((2 * STRIDE, feat)),
            pl.BlockSpec(memory_space=pl.ANY),
            full((model_width,)),
            pl.BlockSpec(memory_space=pl.ANY),
        ],
        out_specs=[rows_spec, rows_spec, rows_spec, rows_spec, state_spec, state_spec],
        out_shape=[jax.ShapeDtypeStruct((token_count, model_width), jnp.bfloat16)] * 4 + [
            jax.ShapeDtypeStruct((pairs, head_size, PAIR), jnp.float32),
        ] * 2,
        scratch_shapes=[pltpu.VMEM((block_ticks + STRIDE, feat), jnp.float32),
                        pltpu.VMEM(qkv_weight.shape, qkv_weight.dtype),
                        pltpu.SemaphoreType.DMA(()),
                        pltpu.VMEM(conv_weight.shape, conv_weight.dtype),
                        pltpu.SemaphoreType.DMA(())],
        compiler_params=pltpu.CompilerParams(dimension_semantics=("arbitrary",)),
    )(ticks, prev, conv_weight, norm_gain, qkv_weight)

    halves = 2
    piece_width = model_width // halves

    def inside_block(piece, earlier, q, k, v):
        block, half = divmod(piece, halves)
        spec = pl.BlockSpec((BLK, piece_width), lambda p, block=block, half=half: (block, half + p))
        in_specs, operands, aliases = [spec, spec, spec], [q, k, v], {}
        kernel = inside_kernel
        if earlier is not None:
            in_specs.append(pl.BlockSpec(memory_space=pl.ANY))
            operands.append(earlier)
            aliases = {3: 0}
        else:
            kernel = first_inside_kernel
        return pl.pallas_call(
            kernel,
            grid=(1,),
            in_specs=in_specs,
            out_specs=spec,
            out_shape=jax.ShapeDtypeStruct((token_count, model_width), jnp.float32),
            input_output_aliases=aliases,
            cost_estimate=pl.CostEstimate(flops=8 * BLK * BLK * piece_width, transcendentals=0,
                                          bytes_accessed=10 * BLK * piece_width),
        )(*operands)

    count = lax.axis_size("inner")
    inside = None
    total, steps, block = local, 1, 0
    received = jnp.zeros_like(local)
    while steps < count:
        if block < blocks * halves:
            total, q_in, k_in, v_in = lax.optimization_barrier((total, queries, keys, values))
        received = from_behind(total, "inner", steps)
        if block < blocks * halves:
            inside = inside_block(block, inside, q_in, k_in, v_in)
            received, inside = lax.optimization_barrier((received, inside))
            block += 1
        steps *= 2
        if steps >= count:
            break
        total = total + received
    while block < blocks * halves:
        inside = inside_block(block, inside, queries, keys, values)
        block += 1
    packed_in = state_in.reshape(pairs, 2, head_size, head_size).transpose(0, 2, 1, 3)
    packed_in = packed_in.reshape(pairs, head_size, PAIR)
    base = [packed_in - local]
    for block in range(1, blocks):
        base.append(base[-1] + first_state)
    base = jnp.stack(base)
    base_spec = pl.BlockSpec((1, pairs, head_size, PAIR), lambda b: (b, 0, 0, 0))

    return pl.pallas_call(
        out_kernel,
        grid=(blocks,),
        in_specs=[
            rows_spec,
            base_spec,
            state_spec,
            state_spec,
            rows_spec,
            rows_spec,
            full((1, model_width)),
            full(out_weight.shape),
        ],
        out_specs=rows_spec,
        out_shape=jax.ShapeDtypeStruct((token_count, model_width), jnp.bfloat16),
        scratch_shapes=[pltpu.VMEM((BLK, model_width), jnp.bfloat16)],
        compiler_params=pltpu.CompilerParams(dimension_semantics=("arbitrary",)),
    )(queries, base, total, received, inside, emb, head_gain.reshape(1, model_width), out_weight)


def solution(mesh):
    in_specs = (P(("groups", "inner"), None), P(), P(), P(), P(), P(), P("groups", None, None))
    out_specs = P(("groups", "inner"), None)
    return jax.shard_map(shards, mesh=mesh, in_specs=in_specs, out_specs=out_specs, check_vma=False)
```

```python
import functools

import jax
import jax.numpy as jnp
from jax import lax
from jax.experimental import pallas as pl
from jax.experimental.pallas import tpu as pltpu
from jax.sharding import PartitionSpec as P

STRIDE = 8
BLK = 512
PAIR = 128


def from_behind(value, axis, steps):
    count = lax.axis_size(axis)
    initial, last = (max(0, -steps), min(count, count - steps))
    return lax.ppermute(value, axis, [(source, source + steps) for source in range(initial, last)])


def exclusive_scan(value, axis):
    count = lax.axis_size(axis)
    total = value
    steps = 1
    while steps < count:
        total = total + from_behind(total, axis, steps)
        steps *= 2
    return total - value


def embed_kernel(ticks_ref, prev_ref, conv_ref, gain_ref, qkv_hbm,
                 emb_ref, q_ref, k_ref, v_ref, total_ref, first_ref, wide_ref, qkv_w_ref, copy_sem):
    b = pl.program_id(0)
    block_ticks = ticks_ref.shape[0]
    tokens = block_ticks // STRIDE
    model_width = emb_ref.shape[1]

    weight_copy = pltpu.make_async_copy(qkv_hbm, qkv_w_ref, copy_sem)

    @pl.when(b == 0)
    def _():
        weight_copy.start()
        wide_ref[0:STRIDE, :] = prev_ref[STRIDE : 2 * STRIDE, :].astype(jnp.float32)

    @pl.when(b > 0)
    def _():
        wide_ref[0:STRIDE, :] = wide_ref[block_ticks : block_ticks + STRIDE, :]

    wide_ref[STRIDE:, :] = ticks_ref[...].astype(jnp.float32)
    pieces = [wide_ref[pl.ds(j, tokens, stride=STRIDE), :] for j in range(2 * STRIDE)]
    lhs = jnp.concatenate(pieces, axis=1).astype(jnp.bfloat16)
    emb = jnp.dot(lhs, conv_ref[...], preferred_element_type=jnp.float32).astype(jnp.bfloat16)
    emb_ref[...] = emb
    embed_f = emb.astype(jnp.float32)
    mean_sq = jnp.mean(embed_f * embed_f, axis=-1, keepdims=True)
    normed = (embed_f * lax.rsqrt(mean_sq + 1e-05) * gain_ref[...][None, :]).astype(jnp.bfloat16)

    @pl.when(b == 0)
    def _():
        weight_copy.wait()

    def project(part):
        weight = qkv_w_ref[:, part * model_width : (part + 1) * model_width]
        return jnp.dot(normed, weight, preferred_element_type=jnp.float32).astype(jnp.bfloat16)

    queries, keys, values = project(0), project(1), project(2)
    q_ref[...] = queries
    k_ref[...] = keys
    v_ref[...] = values
    lane = lax.broadcasted_iota(jnp.int32, (1, PAIR), 1)
    first = lane < PAIR // 2
    for pair in range(model_width // PAIR):
        cols = slice(pair * PAIR, (pair + 1) * PAIR)
        kv = lax.dot_general(keys[:, cols], values[:, cols], (((0,), (0,)), ((), ())),
                             preferred_element_type=jnp.float32)
        half = PAIR // 2
        packed = jnp.where(first, kv[:half], kv[half:])
        total_ref[pair] = jnp.where(b > 0, total_ref[pair], 0.0) + packed
        first_ref[pair] = jnp.where(b > 0, first_ref[pair], packed)


def inside_kernel(q_ref, k_ref, v_ref, earlier_ref, inside_ref):
    del earlier_ref
    first_inside_kernel(q_ref, k_ref, v_ref, inside_ref)


def first_inside_kernel(q_ref, k_ref, v_ref, inside_ref):
    tokens = q_ref.shape[0]
    part = tokens // 2
    lane = lax.broadcasted_iota(jnp.int32, (1, PAIR), 1)
    first = lane < PAIR // 2
    zero = jnp.zeros((), jnp.bfloat16)
    for pair in range(q_ref.shape[1] // PAIR):
        cols = slice(pair * PAIR, (pair + 1) * PAIR)
        for rows_at in (0, part):
            seen = rows_at + part
            q_rows = q_ref[rows_at : rows_at + part, cols]
            k_seen, v_seen = k_ref[0:seen, cols], v_ref[0:seen, cols]
            causal = (lax.broadcasted_iota(jnp.int32, (part, seen), 0) + rows_at
                      >= lax.broadcasted_iota(jnp.int32, (part, seen), 1))
            inside = None
            for use in (first, ~first):
                q_one = jnp.where(use, q_rows, zero)
                scores = lax.dot_general(q_one, k_seen, (((1,), (1,)), ((), ())),
                                         preferred_element_type=jnp.float32)
                scores = jnp.where(causal, scores, 0.0).astype(jnp.bfloat16)
                term = jnp.dot(scores, jnp.where(use, v_seen, zero), preferred_element_type=jnp.float32)
                inside = term if inside is None else inside + term
            inside_ref[rows_at : rows_at + part, cols] = inside


def out_kernel(q_ref, base_ref, total_ref, received_ref, inside_ref, emb_ref, hgain_ref, out_w_ref, out_ref, att_ref):
    model_width = out_ref.shape[1]
    lane = lax.broadcasted_iota(jnp.int32, (1, PAIR), 1)
    first = lane < PAIR // 2
    head_size = PAIR // 2
    for pair in range(model_width // PAIR):
        cols = slice(pair * PAIR, (pair + 1) * PAIR)
        packed = base_ref[0, pair] + (total_ref[pair] + received_ref[pair])
        diag = jnp.concatenate([jnp.where(first, packed, 0.0), jnp.where(first, 0.0, packed)], axis=0)
        high = diag.astype(jnp.bfloat16)
        low = (diag - high.astype(jnp.float32)).astype(jnp.bfloat16)
        q_pair = q_ref[:, cols]
        carried = (jnp.dot(q_pair, high, preferred_element_type=jnp.float32)
                   + jnp.dot(q_pair, low, preferred_element_type=jnp.float32))
        combined = inside_ref[:, cols] + carried
        square = combined * combined
        sum_first = jnp.sum(jnp.where(first, square, 0.0), axis=-1, keepdims=True)
        sum_second = jnp.sum(jnp.where(first, 0.0, square), axis=-1, keepdims=True)
        scale = jnp.where(first, lax.rsqrt(sum_first / head_size + 1e-06),
                          lax.rsqrt(sum_second / head_size + 1e-06))
        att_ref[:, cols] = (combined * scale * hgain_ref[:, cols]).astype(jnp.bfloat16)
    out = emb_ref[...].astype(jnp.float32) + jnp.dot(att_ref[...], out_w_ref[...],
                                                     preferred_element_type=jnp.float32)
    out_ref[...] = out.astype(jnp.bfloat16)


def full(shape):
    return pl.BlockSpec(shape, lambda b: (0,) * len(shape))


def shards(ticks, conv_weight, norm_gain, qkv_weight, head_gain, out_weight, state_in):
    tick_count, feat = ticks.shape
    token_count = tick_count // STRIDE
    model_width = conv_weight.shape[1]
    head_count, head_size = state_in.shape[0], state_in.shape[1]
    pairs = model_width // PAIR
    blocks = token_count // BLK
    block_ticks = BLK * STRIDE

    prev = from_behind(ticks[tick_count - 2 * STRIDE :], "inner", 1)
    rows_spec = pl.BlockSpec((BLK, model_width), lambda b: (b, 0))
    state_spec = full((pairs, head_size, PAIR))
    emb, queries, keys, values, local, first_state = pl.pallas_call(
        embed_kernel,
        grid=(blocks,),
        in_specs=[
            pl.BlockSpec((block_ticks, feat), lambda b: (b, 0)),
            full((2 * STRIDE, feat)),
            full(conv_weight.shape),
            full((model_width,)),
            pl.BlockSpec(memory_space=pl.ANY),
        ],
        out_specs=[rows_spec, rows_spec, rows_spec, rows_spec, state_spec, state_spec],
        out_shape=[jax.ShapeDtypeStruct((token_count, model_width), jnp.bfloat16)] * 4 + [
            jax.ShapeDtypeStruct((pairs, head_size, PAIR), jnp.float32),
        ] * 2,
        scratch_shapes=[pltpu.VMEM((block_ticks + STRIDE, feat), jnp.float32),
                        pltpu.VMEM(qkv_weight.shape, qkv_weight.dtype),
                        pltpu.SemaphoreType.DMA(())],
        compiler_params=pltpu.CompilerParams(dimension_semantics=("arbitrary",)),
    )(ticks, prev, conv_weight, norm_gain, qkv_weight)

    halves = 2
    piece_width = model_width // halves

    def inside_block(piece, earlier, q, k, v):
        block, half = divmod(piece, halves)
        spec = pl.BlockSpec((BLK, piece_width), lambda p, block=block, half=half: (block, half + p))
        in_specs, operands, aliases = [spec, spec, spec], [q, k, v], {}
        kernel = inside_kernel
        if earlier is not None:
            in_specs.append(pl.BlockSpec(memory_space=pl.ANY))
            operands.append(earlier)
            aliases = {3: 0}
        else:
            kernel = first_inside_kernel
        return pl.pallas_call(
            kernel,
            grid=(1,),
            in_specs=in_specs,
            out_specs=spec,
            out_shape=jax.ShapeDtypeStruct((token_count, model_width), jnp.float32),
            input_output_aliases=aliases,
            cost_estimate=pl.CostEstimate(flops=8 * BLK * BLK * piece_width, transcendentals=0,
                                          bytes_accessed=10 * BLK * piece_width),
        )(*operands)

    count = lax.axis_size("inner")
    inside = None
    total, steps, block = local, 1, 0
    received = jnp.zeros_like(local)
    while steps < count:
        if block < blocks * halves:
            total, q_in, k_in, v_in = lax.optimization_barrier((total, queries, keys, values))
        received = from_behind(total, "inner", steps)
        if block < blocks * halves:
            inside = inside_block(block, inside, q_in, k_in, v_in)
            received, inside = lax.optimization_barrier((received, inside))
            block += 1
        steps *= 2
        if steps >= count:
            break
        total = total + received
    while block < blocks * halves:
        inside = inside_block(block, inside, queries, keys, values)
        block += 1
    packed_in = state_in.reshape(pairs, 2, head_size, head_size).transpose(0, 2, 1, 3)
    packed_in = packed_in.reshape(pairs, head_size, PAIR)
    base = [packed_in - local]
    for block in range(1, blocks):
        base.append(base[-1] + first_state)
    base = jnp.stack(base)
    out_rows = BLK // 2
    base_spec = pl.BlockSpec((1, pairs, head_size, PAIR), lambda b: (b * out_rows // BLK, 0, 0, 0))
    out_rows_spec = pl.BlockSpec((out_rows, model_width), lambda b: (b, 0))

    return pl.pallas_call(
        out_kernel,
        grid=(token_count // out_rows,),
        in_specs=[
            out_rows_spec,
            base_spec,
            state_spec,
            state_spec,
            out_rows_spec,
            out_rows_spec,
            full((1, model_width)),
            full(out_weight.shape),
        ],
        out_specs=out_rows_spec,
        out_shape=jax.ShapeDtypeStruct((token_count, model_width), jnp.bfloat16),
        scratch_shapes=[pltpu.VMEM((out_rows, model_width), jnp.bfloat16)],
        compiler_params=pltpu.CompilerParams(dimension_semantics=("arbitrary",)),
    )(queries, base, total, received, inside, emb, head_gain.reshape(1, model_width), out_weight)


def solution(mesh):
    in_specs = (P(("groups", "inner"), None), P(), P(), P(), P(), P(), P("groups", None, None))
    out_specs = P(("groups", "inner"), None)
    return jax.shard_map(shards, mesh=mesh, in_specs=in_specs, out_specs=out_specs, check_vma=False)
```

```python
import functools

import jax
import jax.numpy as jnp
from jax import lax
from jax.experimental import pallas as pl
from jax.experimental.pallas import tpu as pltpu
from jax.sharding import PartitionSpec as P

STRIDE = 8
BLK = 512
PAIR = 128


def from_behind(value, axis, steps):
    count = lax.axis_size(axis)
    initial, last = (max(0, -steps), min(count, count - steps))
    return lax.ppermute(value, axis, [(source, source + steps) for source in range(initial, last)])


def exclusive_scan(value, axis):
    count = lax.axis_size(axis)
    total = value
    steps = 1
    while steps < count:
        total = total + from_behind(total, axis, steps)
        steps *= 2
    return total - value


def embed_kernel(ticks_ref, prev_ref, conv_ref, gain_ref, qkv_hbm, start_ref,
                 emb_ref, q_ref, k_ref, v_ref, total_ref, first_ref, base_ref, wide_ref, qkv_w_ref, copy_sem):
    b = pl.program_id(0)
    block_ticks = ticks_ref.shape[0]
    tokens = block_ticks // STRIDE
    model_width = emb_ref.shape[1]

    weight_copy = pltpu.make_async_copy(qkv_hbm, qkv_w_ref, copy_sem)

    @pl.when(b == 0)
    def _():
        weight_copy.start()
        wide_ref[0:STRIDE, :] = prev_ref[STRIDE : 2 * STRIDE, :].astype(jnp.float32)

    @pl.when(b > 0)
    def _():
        wide_ref[0:STRIDE, :] = wide_ref[block_ticks : block_ticks + STRIDE, :]

    wide_ref[STRIDE:, :] = ticks_ref[...].astype(jnp.float32)
    pieces = [wide_ref[pl.ds(j, tokens, stride=STRIDE), :] for j in range(2 * STRIDE)]
    lhs = jnp.concatenate(pieces, axis=1).astype(jnp.bfloat16)
    emb = jnp.dot(lhs, conv_ref[...], preferred_element_type=jnp.float32).astype(jnp.bfloat16)
    emb_ref[...] = emb
    embed_f = emb.astype(jnp.float32)
    mean_sq = jnp.mean(embed_f * embed_f, axis=-1, keepdims=True)
    normed = (embed_f * lax.rsqrt(mean_sq + 1e-05) * gain_ref[...][None, :]).astype(jnp.bfloat16)

    @pl.when(b == 0)
    def _():
        weight_copy.wait()

    def project(part):
        weight = qkv_w_ref[:, part * model_width : (part + 1) * model_width]
        return jnp.dot(normed, weight, preferred_element_type=jnp.float32).astype(jnp.bfloat16)

    queries, keys, values = project(0), project(1), project(2)
    q_ref[...] = queries
    k_ref[...] = keys
    v_ref[...] = values
    lane = lax.broadcasted_iota(jnp.int32, (1, PAIR), 1)
    first = lane < PAIR // 2
    for pair in range(model_width // PAIR):
        cols = slice(pair * PAIR, (pair + 1) * PAIR)
        kv = lax.dot_general(keys[:, cols], values[:, cols], (((0,), (0,)), ((), ())),
                             preferred_element_type=jnp.float32)
        half = PAIR // 2
        packed = jnp.where(first, kv[:half], kv[half:])
        total = jnp.where(b > 0, total_ref[pair], 0.0) + packed
        first_block = jnp.where(b > 0, first_ref[pair], packed)
        total_ref[pair] = total
        first_ref[pair] = first_block
        base = start_ref[pair] - total
        base_ref[0, pair] = base
        base_ref[1, pair] = base + first_block


def inside_kernel(q_ref, k_ref, v_ref, earlier_ref, inside_ref):
    del earlier_ref
    first_inside_kernel(q_ref, k_ref, v_ref, inside_ref)


def first_inside_kernel(q_ref, k_ref, v_ref, inside_ref):
    tokens = q_ref.shape[0]
    part = tokens // 2
    lane = lax.broadcasted_iota(jnp.int32, (1, PAIR), 1)
    first = lane < PAIR // 2
    zero = jnp.zeros((), jnp.bfloat16)
    for pair in range(q_ref.shape[1] // PAIR):
        cols = slice(pair * PAIR, (pair + 1) * PAIR)
        for rows_at in (0, part):
            seen = rows_at + part
            q_rows = q_ref[rows_at : rows_at + part, cols]
            k_seen, v_seen = k_ref[0:seen, cols], v_ref[0:seen, cols]
            causal = (lax.broadcasted_iota(jnp.int32, (part, seen), 0) + rows_at
                      >= lax.broadcasted_iota(jnp.int32, (part, seen), 1))
            inside = None
            for use in (first, ~first):
                q_one = jnp.where(use, q_rows, zero)
                scores = lax.dot_general(q_one, k_seen, (((1,), (1,)), ((), ())),
                                         preferred_element_type=jnp.float32)
                scores = jnp.where(causal, scores, 0.0).astype(jnp.bfloat16)
                term = jnp.dot(scores, jnp.where(use, v_seen, zero), preferred_element_type=jnp.float32)
                inside = term if inside is None else inside + term
            inside_ref[rows_at : rows_at + part, cols] = inside


def out_kernel(q_ref, base_ref, total_ref, received_ref, inside_ref, emb_ref, hgain_ref, out_w_ref, out_ref, att_ref):
    model_width = out_ref.shape[1]
    lane = lax.broadcasted_iota(jnp.int32, (1, PAIR), 1)
    first = lane < PAIR // 2
    head_size = PAIR // 2
    for pair in range(model_width // PAIR):
        cols = slice(pair * PAIR, (pair + 1) * PAIR)
        packed = base_ref[0, pair] + (total_ref[pair] + received_ref[pair])
        diag = jnp.concatenate([jnp.where(first, packed, 0.0), jnp.where(first, 0.0, packed)], axis=0)
        high = diag.astype(jnp.bfloat16)
        low = (diag - high.astype(jnp.float32)).astype(jnp.bfloat16)
        q_pair = q_ref[:, cols]
        carried = (jnp.dot(q_pair, high, preferred_element_type=jnp.float32)
                   + jnp.dot(q_pair, low, preferred_element_type=jnp.float32))
        combined = inside_ref[:, cols] + carried
        square = combined * combined
        sum_first = jnp.sum(jnp.where(first, square, 0.0), axis=-1, keepdims=True)
        sum_second = jnp.sum(jnp.where(first, 0.0, square), axis=-1, keepdims=True)
        scale = jnp.where(first, lax.rsqrt(sum_first / head_size + 1e-06),
                          lax.rsqrt(sum_second / head_size + 1e-06))
        att_ref[:, cols] = (combined * scale * hgain_ref[:, cols]).astype(jnp.bfloat16)
    out = emb_ref[...].astype(jnp.float32) + jnp.dot(att_ref[...], out_w_ref[...],
                                                     preferred_element_type=jnp.float32)
    out_ref[...] = out.astype(jnp.bfloat16)


def full(shape):
    return pl.BlockSpec(shape, lambda b: (0,) * len(shape))


def shards(ticks, conv_weight, norm_gain, qkv_weight, head_gain, out_weight, state_in):
    tick_count, feat = ticks.shape
    token_count = tick_count // STRIDE
    model_width = conv_weight.shape[1]
    head_count, head_size = state_in.shape[0], state_in.shape[1]
    pairs = model_width // PAIR
    blocks = token_count // BLK
    block_ticks = BLK * STRIDE

    prev = from_behind(ticks[tick_count - 2 * STRIDE :], "inner", 1)
    rows_spec = pl.BlockSpec((BLK, model_width), lambda b: (b, 0))
    state_spec = full((pairs, head_size, PAIR))
    packed_in = state_in.reshape(pairs, 2, head_size, head_size).transpose(0, 2, 1, 3)
    packed_in = packed_in.reshape(pairs, head_size, PAIR)
    emb, queries, keys, values, local, first_state, base = pl.pallas_call(
        embed_kernel,
        grid=(blocks,),
        in_specs=[
            pl.BlockSpec((block_ticks, feat), lambda b: (b, 0)),
            full((2 * STRIDE, feat)),
            full(conv_weight.shape),
            full((model_width,)),
            pl.BlockSpec(memory_space=pl.ANY),
            state_spec,
        ],
        out_specs=[rows_spec, rows_spec, rows_spec, rows_spec, state_spec, state_spec,
                   full((blocks, pairs, head_size, PAIR))],
        out_shape=[jax.ShapeDtypeStruct((token_count, model_width), jnp.bfloat16)] * 4 + [
            jax.ShapeDtypeStruct((pairs, head_size, PAIR), jnp.float32),
        ] * 2 + [jax.ShapeDtypeStruct((blocks, pairs, head_size, PAIR), jnp.float32)],
        scratch_shapes=[pltpu.VMEM((block_ticks + STRIDE, feat), jnp.float32),
                        pltpu.VMEM(qkv_weight.shape, qkv_weight.dtype),
                        pltpu.SemaphoreType.DMA(())],
        compiler_params=pltpu.CompilerParams(dimension_semantics=("arbitrary",)),
    )(ticks, prev, conv_weight, norm_gain, qkv_weight, packed_in)

    halves = 2
    piece_width = model_width // halves

    def inside_block(piece, earlier, q, k, v):
        block, half = divmod(piece, halves)
        spec = pl.BlockSpec((BLK, piece_width), lambda p, block=block, half=half: (block, half + p))
        in_specs, operands, aliases = [spec, spec, spec], [q, k, v], {}
        kernel = inside_kernel
        if earlier is not None:
            in_specs.append(pl.BlockSpec(memory_space=pl.ANY))
            operands.append(earlier)
            aliases = {3: 0}
        else:
            kernel = first_inside_kernel
        return pl.pallas_call(
            kernel,
            grid=(1,),
            in_specs=in_specs,
            out_specs=spec,
            out_shape=jax.ShapeDtypeStruct((token_count, model_width), jnp.float32),
            input_output_aliases=aliases,
            cost_estimate=pl.CostEstimate(flops=8 * BLK * BLK * piece_width, transcendentals=0,
                                          bytes_accessed=10 * BLK * piece_width),
        )(*operands)

    count = lax.axis_size("inner")
    inside = None
    total, steps, block = local, 1, 0
    received = jnp.zeros_like(local)
    while steps < count:
        if block < blocks * halves:
            total, q_in, k_in, v_in = lax.optimization_barrier((total, queries, keys, values))
        received = from_behind(total, "inner", steps)
        if block < blocks * halves:
            inside = inside_block(block, inside, q_in, k_in, v_in)
            received, inside = lax.optimization_barrier((received, inside))
            block += 1
        steps *= 2
        if steps >= count:
            break
        total = total + received
    while block < blocks * halves:
        inside = inside_block(block, inside, queries, keys, values)
        block += 1
    base_spec = pl.BlockSpec((1, pairs, head_size, PAIR), lambda b: (b, 0, 0, 0))

    return pl.pallas_call(
        out_kernel,
        grid=(blocks,),
        in_specs=[
            rows_spec,
            base_spec,
            state_spec,
            state_spec,
            rows_spec,
            rows_spec,
            full((1, model_width)),
            full(out_weight.shape),
        ],
        out_specs=rows_spec,
        out_shape=jax.ShapeDtypeStruct((token_count, model_width), jnp.bfloat16),
        scratch_shapes=[pltpu.VMEM((BLK, model_width), jnp.bfloat16)],
        compiler_params=pltpu.CompilerParams(dimension_semantics=("arbitrary",)),
    )(queries, base, total, received, inside, emb, head_gain.reshape(1, model_width), out_weight)


def solution(mesh):
    in_specs = (P(("groups", "inner"), None), P(), P(), P(), P(), P(), P("groups", None, None))
    out_specs = P(("groups", "inner"), None)
    return jax.shard_map(shards, mesh=mesh, in_specs=in_specs, out_specs=out_specs, check_vma=False)
```
